128 devices in a mesh: req: 8 (over z, core), mp: 16 (over x, y).
Axes of the slice: x: 4, y: 4, z: 4, core: 2. Of those that a mesh axis runs over, the one named last changes fastest.
Arguments:
- states: bfloat16 [8, 32, 16, 5120], P('req', None, 'mp'), may hold values from -6 to 6
- lengths: int32 [8, 4], replicated, may hold values from 1 to 509, as said below
- request_adapters: int32 [8, 4], replicated, may hold values from 0 to 7
- attention_norm_gain: float32 [5120], replicated, may hold values from 0.1 to 1.9
- query_weight: bfloat16 [5120, 4096], P(None, 'mp')
- key_weight: bfloat16 [5120, 1024], P(None, 'mp')
- value_weight: bfloat16 [5120, 1024], P(None, 'mp'), may hold values from -0.078125 to 0.078125
- output_weight: bfloat16 [4096, 5120], P('mp'), may hold values from -0.09375 to 0.09375
- adapter_down_attention: bfloat16 [5120, 384], replicated, may hold values from -0.078125 to 0.078125
- adapter_up_query: bfloat16 [128, 4096], P(None, 'mp'), may hold values from -0.5 to 0.5
- adapter_up_key_value: bfloat16 [2, 128, 1024], P(None, None, 'mp'), may hold values from -0.5 to 0.5
- adapter_down_output: bfloat16 [4096, 128], P('mp'), may hold values from -0.09375 to 0.09375
- adapter_up_output: bfloat16 [128, 5120], replicated, may hold values from -0.875 to 0.875
- feed_norm_gain: float32 [5120], replicated, may hold values from 0.1 to 1.9
- gate_up_weight: bfloat16 [2, 5120, 10240], P(None, 'req', 'mp'), may hold values from -0.078125 to 0.078125
- down_weight: bfloat16 [5120, 10240], P('req', 'mp'), may hold values from -0.0625 to 0.0625
- adapter_down_gate_up: bfloat16 [5120, 256], replicated, may hold values from -0.078125 to 0.078125
- adapter_up_gate_up: bfloat16 [2, 128, 10240], P(None, None, 'mp'), may hold values from -0.5 to 0.5
- adapter_down_feed: bfloat16 [10240, 128], P('mp'), may hold values from -0.0625 to 0.0625
- adapter_up_feed: bfloat16 [128, 5120], replicated, may hold values from -0.875 to 0.875
Outputs:
- layer_out: bfloat16 [8, 32, 16, 5120], P('req', None, 'mp')
The draws below stay inside these ranges and needn't reach their ends.
Inputs may be any that keep to these rules, and one draw needn't show every extreme that they name: `lengths`: each request has at least one token; each row sums to at most 512, some row to exactly 512, and all rows together to exactly 2048; some request is 509 tokens long.
All inputs are finite; a program needn't handle non-finite values.
Results may differ from the reference program's by a relative error of at most 0.03.
Values may be sent and summed in bfloat16 or wider, within the bound.
No kernel may reach another device: no remote copies, remote signals or barrier semaphores. Data moves between devices by JAX's collectives and lax.ppermute only.
A program may use at most 128 MiB of HBM per device.

```python
import jax
import jax.numpy as jnp
from jax import lax

MODEL_DIM = 5120
QUERY_HEADS = 32
KEY_VALUE_HEADS = 8
HEAD_SIZE = 128
FEED_UNITS = 10240
NAD = 8
ADAPTER_RANK = 16
ADAPTER_COLUMNS = 128
RPG = 4
WINDOW = 128
SINK = 4
SLOT_DEV = 32
SLOTS = 512
TOTAL = 2048
N_REQ = 8
N_MP = 16


def query_base(key):
    noise = jax.random.normal(jax.random.fold_in(key, 31), (MODEL_DIM, QUERY_HEADS * HEAD_SIZE), jnp.float32)
    return jnp.clip(noise, -4.0, 4.0) * MODEL_DIM ** (-0.5)


def draw_query_weight(key, part):
    return query_base(key).astype(jnp.bfloat16)


def draw_key_weight(key, part):
    noise = jnp.clip(jax.random.normal(jax.random.fold_in(key, 32), (MODEL_DIM, KEY_VALUE_HEADS * HEAD_SIZE), jnp.float32), -4.0, 4.0) * MODEL_DIM ** (-0.5)
    return noise.astype(jnp.bfloat16)


def draw_lengths(key, part):
    key_heavy = jax.random.fold_in(key, 21)
    key_shift = jax.random.fold_in(key, 22)
    key_order = jax.random.fold_in(key, 23)
    key_cuts = jax.random.fold_in(key, 24)
    others = N_REQ - 1
    spare_tokens = TOTAL - SLOTS
    base_load = spare_tokens // others
    remainder = spare_tokens - base_load * others
    reach_max = base_load // 4
    shifts = jax.random.randint(key_shift, (others,), -reach_max, reach_max + 1, dtype=jnp.int32)
    group_loads = base_load + (jnp.arange(others, dtype=jnp.int32) < remainder).astype(jnp.int32) + jnp.roll(shifts, 1) - shifts
    group_loads = jax.random.permutation(key_order, group_loads)
    heavy_group = jax.random.randint(key_heavy, (), 0, N_REQ, dtype=jnp.int32)
    groups = jnp.arange(N_REQ, dtype=jnp.int32)
    source = jnp.clip(jnp.where(groups > heavy_group, groups - 1, groups), 0, others - 1)
    totals = jnp.where(groups == heavy_group, SLOTS, jnp.take(group_loads, source)).astype(jnp.int32)
    spare_room = totals - RPG
    cut_points = jax.random.randint(key_cuts, (N_REQ, RPG - 1), 0, spare_room[:, None] + 1, dtype=jnp.int32)
    cut_points = jnp.sort(cut_points, axis=1)
    cut_points = jnp.where((groups == heavy_group)[:, None], 0, cut_points).astype(jnp.int32)
    bounds = jnp.concatenate([jnp.zeros((N_REQ, 1), jnp.int32), cut_points, spare_room[:, None]], axis=1)
    return (bounds[:, 1:] - bounds[:, :-1] + 1).astype(jnp.int32)


def with_ends(values, stream_key, low, high):
    shape = values.shape
    index_at = [jax.random.randint(jax.random.fold_in(stream_key, axis), (), 0, shape[axis]) for axis in range(len(shape))]
    values = values.at[tuple(index_at)].set(low)
    longest = shape.index(max(shape))
    index_at[longest] = (index_at[longest] + 1) % shape[longest]
    return values.at[tuple(index_at)].set(high)


def shard_levels(own_key, extent, cuts, least, largest):
    loudness = 1.0
    for dim, blocks in cuts:
        steps = jax.random.uniform(jax.random.fold_in(jax.random.fold_in(own_key, 6), dim), (blocks,), jnp.float32, least / len(cuts), largest / len(cuts))
        loudness = loudness * jnp.repeat(jnp.exp(steps), extent[dim] // blocks).reshape((-1,) + (1,) * (len(extent) - 1 - dim))
    return loudness


def centred(own_key, dims, deviation, limit, shards=(), held_as=jnp.bfloat16):
    factor_of = shard_levels(own_key, dims, shards, -0.22, 0.18) if shards else 1.0
    entries = jax.random.normal(own_key, dims, jnp.float32) * deviation * factor_of
    return jnp.minimum(jnp.maximum(entries, -limit), limit).astype(held_as)


def setup_inputs(seed: int = 0) -> dict:
    seeds = jax.random.split(jax.random.key(seed), 21)
    return {
        "states": centred(seeds[0], (N_REQ, SLOT_DEV, N_MP, MODEL_DIM), 1.0, 6.0, ((0, 8), (2, 16))),
        "lengths": draw_lengths(jax.random.fold_in(seeds[20], 71), 0),
        "request_adapters": with_ends(jax.random.randint(seeds[2], (N_REQ, RPG), 0, NAD), jax.random.fold_in(seeds[2], 1), 0, NAD - 1).astype(jnp.int32),
        "attention_norm_gain": jnp.clip(1.0 + 0.18 * jax.random.normal(seeds[3], (MODEL_DIM,), jnp.float32), 0.1, 1.9),
        "query_weight": draw_query_weight(jax.random.fold_in(seeds[20], 71), 0),
        "key_weight": draw_key_weight(jax.random.fold_in(seeds[20], 71), 0),
        "value_weight": centred(seeds[6], (MODEL_DIM, KEY_VALUE_HEADS * HEAD_SIZE), MODEL_DIM ** -0.5, 0.078125, ((1, 16),)),
        "output_weight": centred(seeds[7], (QUERY_HEADS * HEAD_SIZE, MODEL_DIM), (QUERY_HEADS * HEAD_SIZE) ** -0.5, 0.09375, ((0, 16),)),
        "adapter_down_attention": centred(seeds[8], (MODEL_DIM, 3 * ADAPTER_COLUMNS), MODEL_DIM ** -0.5, 0.078125),
        "adapter_up_query": centred(seeds[9], (ADAPTER_COLUMNS, QUERY_HEADS * HEAD_SIZE), 0.08, 0.5, ((1, 16),)),
        "adapter_up_key_value": centred(seeds[10], (2, ADAPTER_COLUMNS, KEY_VALUE_HEADS * HEAD_SIZE), 0.08, 0.5, ((2, 16),)),
        "adapter_down_output": centred(seeds[11], (QUERY_HEADS * HEAD_SIZE, ADAPTER_COLUMNS), (QUERY_HEADS * HEAD_SIZE) ** -0.5, 0.09375, ((0, 16),)),
        "adapter_up_output": centred(seeds[12], (ADAPTER_COLUMNS, MODEL_DIM), 0.15, 0.875),
        "feed_norm_gain": jnp.clip(1.0 + 0.18 * jax.random.normal(seeds[13], (MODEL_DIM,), jnp.float32), 0.1, 1.9),
        "gate_up_weight": centred(seeds[14], (2, MODEL_DIM, FEED_UNITS), MODEL_DIM ** -0.5, 0.078125, ((1, 8), (2, 16))),
        "down_weight": centred(seeds[15], (MODEL_DIM, FEED_UNITS), FEED_UNITS ** -0.5, 0.0625, ((0, 8), (1, 16))),
        "adapter_down_gate_up": centred(seeds[16], (MODEL_DIM, 2 * ADAPTER_COLUMNS), MODEL_DIM ** -0.5, 0.078125),
        "adapter_up_gate_up": centred(seeds[17], (2, ADAPTER_COLUMNS, FEED_UNITS), 0.08, 0.5, ((2, 16),)),
        "adapter_down_feed": centred(seeds[18], (FEED_UNITS, ADAPTER_COLUMNS), FEED_UNITS ** -0.5, 0.0625, ((0, 16),)),
        "adapter_up_feed": centred(seeds[19], (ADAPTER_COLUMNS, MODEL_DIM), 0.15, 0.875),
    }


EPSILON = 1e-05
ROPE_THETA = 1000000.0

def slot_info(length_rows, adapter_rows, slot_ids):
    request_ends = jnp.cumsum(length_rows, axis=1, dtype=jnp.int32)
    starts = request_ends - length_rows
    count_req = length_rows.shape[1]
    request = lax.optimization_barrier(jnp.sum((slot_ids[:, None] >= request_ends).astype(jnp.int32), axis=1, dtype=jnp.int32))
    living = request < count_req
    matches = request[:, None] == jnp.arange(count_req, dtype=jnp.int32)[None, :]
    opening = lax.optimization_barrier(jnp.sum(jnp.where(matches, starts, 0), axis=1, dtype=jnp.int32))
    position = jnp.where(living, slot_ids - opening, 0).astype(jnp.int32)
    segment = jnp.where(living, request, count_req + slot_ids).astype(jnp.int32)
    chosen = lax.optimization_barrier(jnp.sum(jnp.where(matches, adapter_rows, 0), axis=1, dtype=jnp.int32))
    adapter_slot = jnp.where(living, chosen, -1).astype(jnp.int32)
    return (living, position, segment, adapter_slot)

def normalize(input_tokens, gain_vec):
    values = input_tokens.astype(jnp.float32)
    factor = lax.rsqrt(lax.optimization_barrier(jnp.mean(values * values, axis=-1, keepdims=True)) + EPSILON)
    return (values * factor * gain_vec).astype(jnp.bfloat16)

def adapter_select_mask(adapter_slot, adapter_column_count, adapter_rank_size):
    token_owner_request = jnp.arange(adapter_column_count, dtype=jnp.int32) // adapter_rank_size
    return (adapter_slot[:, None] == token_owner_request[None, :]).astype(jnp.float32)

def rotate(vectors, position):
    half_dim = vectors.shape[-1] // 2
    inverse = ROPE_THETA ** (-(jnp.arange(half_dim, dtype=jnp.float32) * (2.0 / vectors.shape[-1])))
    angles = position.astype(jnp.float32)[:, None] * inverse[None, :]
    cosine = jnp.cos(angles)[:, None, :]
    sine_part = jnp.sin(angles)[:, None, :]
    lower_half = vectors[..., :half_dim]
    upper_half = vectors[..., half_dim:]
    return jnp.concatenate([lower_half * cosine - upper_half * sine_part, upper_half * cosine + lower_half * sine_part], axis=-1)

def attend(queries, key_rows, value_rows, position, segment):
    key_heads = key_rows.shape[1]
    group_size = queries.shape[1] // key_heads
    token_count = queries.shape[0]
    grouped_queries = queries.reshape(token_count, key_heads, group_size, queries.shape[2])
    scores = jnp.einsum('qkgd,skd->kgqs', grouped_queries.astype(jnp.float32), key_rows.astype(jnp.float32)) * queries.shape[2] ** (-0.5)
    allowed = (segment[:, None] == segment[None, :]) & (position[None, :] <= position[:, None])
    allowed = allowed & ((position[:, None] - position[None, :] < WINDOW) | (position[None, :] < SINK))
    scores = jnp.where(allowed[None, None], scores, -jnp.inf)
    highest = lax.optimization_barrier(jnp.max(scores, axis=-1, keepdims=True))
    weights_raw = jnp.exp(scores - highest)
    weights = (weights_raw / lax.optimization_barrier(jnp.sum(weights_raw, axis=-1, keepdims=True))).astype(jnp.bfloat16)
    blended = jnp.einsum('kgqs,skd->qkgd', weights.astype(jnp.float32), value_rows.astype(jnp.float32))
    return blended.reshape(token_count, -1).astype(jnp.bfloat16)

def block_total_sum(partials):
    rounded = lax.optimization_barrier(partials.astype(jnp.bfloat16))
    return lax.optimization_barrier(jnp.sum(rounded.astype(jnp.float32), axis=0))

def reference(states, lengths, request_adapters, attention_norm_gain, query_weight, key_weight, value_weight, output_weight, adapter_down_attention, adapter_up_query, adapter_up_key_value, adapter_down_output, adapter_up_output, feed_norm_gain, gate_up_weight, down_weight, adapter_down_gate_up, adapter_up_gate_up, adapter_down_feed, adapter_up_feed):
    grouped = states.reshape(N_REQ, SLOTS, MODEL_DIM)
    slot_ids = jnp.arange(SLOTS, dtype=jnp.int32)
    head_block_output = QUERY_HEADS * HEAD_SIZE // N_MP
    feed_block_output = FEED_UNITS // N_MP

    def one_group(group_index):
        input_tokens = grouped[group_index]
        length_rows = jnp.broadcast_to(lengths[group_index][None, :], (SLOTS, RPG))
        adapter_rows = jnp.broadcast_to(request_adapters[group_index][None, :], (SLOTS, RPG))
        living, position, segment, adapter_slot = slot_info(length_rows, adapter_rows, slot_ids)
        adapter_indicator = adapter_select_mask(adapter_slot, ADAPTER_COLUMNS, ADAPTER_RANK)
        normed_rows = normalize(input_tokens, attention_norm_gain)
        down_adapter_terms = (jnp.dot(normed_rows, adapter_down_attention, preferred_element_type=jnp.float32) * jnp.tile(adapter_indicator, (1, 3))).astype(jnp.bfloat16)
        query_projected = jnp.dot(normed_rows, query_weight, preferred_element_type=jnp.float32) + jnp.dot(down_adapter_terms[:, :ADAPTER_COLUMNS], adapter_up_query, preferred_element_type=jnp.float32)
        key_projected = jnp.dot(normed_rows, key_weight, preferred_element_type=jnp.float32) + jnp.dot(down_adapter_terms[:, ADAPTER_COLUMNS:2 * ADAPTER_COLUMNS], adapter_up_key_value[0], preferred_element_type=jnp.float32)
        value_projected = jnp.dot(normed_rows, value_weight, preferred_element_type=jnp.float32) + jnp.dot(down_adapter_terms[:, 2 * ADAPTER_COLUMNS:], adapter_up_key_value[1], preferred_element_type=jnp.float32)
        queries = rotate(query_projected.reshape(SLOTS, QUERY_HEADS, HEAD_SIZE), position).astype(jnp.bfloat16)
        key_rows = rotate(key_projected.reshape(SLOTS, KEY_VALUE_HEADS, HEAD_SIZE), position).astype(jnp.bfloat16)
        value_rows = value_projected.reshape(SLOTS, KEY_VALUE_HEADS, HEAD_SIZE).astype(jnp.bfloat16)
        attention_output = attend(queries, key_rows, value_rows, position, segment)
        attention_head_blocks = attention_output.reshape(SLOTS, N_MP, head_block_output).astype(jnp.float32)
        projected_rows = block_total_sum(jnp.einsum('tkb,kbe->kte', attention_head_blocks, output_weight.reshape(N_MP, head_block_output, MODEL_DIM).astype(jnp.float32)))
        output_adapter_ranks = (block_total_sum(jnp.einsum('aod,odu->oau', attention_head_blocks, adapter_down_output.reshape(N_MP, head_block_output, ADAPTER_COLUMNS).astype(jnp.float32))) * adapter_indicator).astype(jnp.bfloat16)
        residual_stream = (input_tokens.astype(jnp.float32) + projected_rows + jnp.dot(output_adapter_ranks, adapter_up_output, preferred_element_type=jnp.float32)).astype(jnp.bfloat16)
        feed_input = normalize(residual_stream, feed_norm_gain)
        gate_adapter_ranks = (jnp.dot(feed_input, adapter_down_gate_up, preferred_element_type=jnp.float32) * jnp.tile(adapter_indicator, (1, 2))).astype(jnp.bfloat16)
        gate_activation = jnp.dot(feed_input, gate_up_weight[0], preferred_element_type=jnp.float32) + jnp.dot(gate_adapter_ranks[:, :ADAPTER_COLUMNS], adapter_up_gate_up[0], preferred_element_type=jnp.float32)
        up_projected = jnp.dot(feed_input, gate_up_weight[1], preferred_element_type=jnp.float32) + jnp.dot(gate_adapter_ranks[:, ADAPTER_COLUMNS:], adapter_up_gate_up[1], preferred_element_type=jnp.float32)
        hidden_activation = (jax.nn.silu(gate_activation) * up_projected).astype(jnp.bfloat16)
        hidden_unit_blocks = hidden_activation.reshape(SLOTS, N_MP, feed_block_output).astype(jnp.float32)
        down_total_sum = block_total_sum(jnp.einsum('cmf,dmf->mcd', hidden_unit_blocks, down_weight.reshape(MODEL_DIM, N_MP, feed_block_output).astype(jnp.float32)))
        down_adapter_ranks = (block_total_sum(jnp.einsum('ksw,swp->skp', hidden_unit_blocks, adapter_down_feed.reshape(N_MP, feed_block_output, ADAPTER_COLUMNS).astype(jnp.float32))) * adapter_indicator).astype(jnp.bfloat16)
        layer_result = residual_stream.astype(jnp.float32) + down_total_sum + jnp.dot(down_adapter_ranks, adapter_up_feed, preferred_element_type=jnp.float32)
        return jnp.where(living[:, None], layer_result, jnp.zeros_like(layer_result)).astype(jnp.bfloat16)
    outputs = lax.map(one_group, jnp.arange(N_REQ, dtype=jnp.int32))
    return outputs.reshape(N_REQ, SLOT_DEV, N_MP, MODEL_DIM)
```

```python
import jax
import jax.numpy as jnp
from jax import lax
from jax.sharding import PartitionSpec as P

HEAD_SIZE = 128
ADAPTER_RANK = 16
WINDOW = 128
SINK = 4


EPSILON = 1e-05
ROPE_THETA = 1000000.0


RING = 4


def _ring_pairs(size, stride, step):
    pairs = []
    for i in range(size):
        low = i % stride
        pos = (i // stride) % RING
        high = i // (stride * RING)
        dst = (high * RING + (pos + step) % RING) * stride + low
        pairs.append((i, dst))
    return pairs


def _shift(x, axis, stride, step):
    return lax.ppermute(x, axis, _ring_pairs(lax.axis_size(axis), stride, step))


def ring_gather(block, axis, stride):
    half = block.shape[0] // 2
    from_minus = _shift(block, axis, stride, 1)
    from_plus = _shift(block, axis, stride, -1)
    first = _shift(from_plus[:half], axis, stride, -1)
    second = _shift(from_minus[half:], axis, stride, 1)
    across = jnp.concatenate([first, second], axis=0)
    return jnp.stack([block, from_plus, across, from_minus])


def ring_scatter(parts, axis, stride):
    half = parts.shape[1] // 2
    wire = jnp.bfloat16
    got_a = _shift(parts[2, :half].astype(wire), axis, stride, 1).astype(jnp.float32)
    got_b = _shift(parts[2, half:].astype(wire), axis, stride, -1).astype(jnp.float32)
    plus = parts[1].at[:half].add(got_a)
    minus = parts[3].at[half:].add(got_b)
    back_a = _shift(minus.astype(wire), axis, stride, -1).astype(jnp.float32)
    back_b = _shift(plus.astype(wire), axis, stride, 1).astype(jnp.float32)
    return parts[0] + back_a + back_b


def plane_gather(block, axis):
    rows, cols = block.shape
    half = rows // 2
    a1 = ring_gather(block[:half], axis, 4)
    b1 = ring_gather(block[half:], axis, 1)
    a2 = ring_gather(a1.reshape(RING * half, cols), axis, 1)
    b2 = ring_gather(b1.reshape(RING * half, cols), axis, 4)
    return jnp.concatenate([a2.reshape(-1, cols), b2.reshape(-1, cols)], axis=0)


def plane_rows(mp_index, rows):
    half = rows // 2
    px, py = mp_index // RING, mp_index % RING
    g = jnp.arange(16 * rows, dtype=jnp.int32)
    second = g >= 8 * rows
    h = g % half
    outer = (g % (8 * rows)) // (RING * half)
    inner = (g % (RING * half)) // half
    kx = jnp.where(second, outer, inner)
    ky = jnp.where(second, inner, outer)
    src = ((px + kx) % RING) * RING + (py + ky) % RING
    local = jnp.where(second, h + half, h)
    return src, local


def plane_scatter(parts, axis, rows):
    cols = parts.shape[1]
    half = rows // 2
    a = parts[: 8 * rows].reshape(RING, RING * half, cols)
    b = parts[8 * rows:].reshape(RING, RING * half, cols)
    a1 = ring_scatter(a, axis, 1).reshape(RING, half, cols)
    b1 = ring_scatter(b, axis, 4).reshape(RING, half, cols)
    a2 = ring_scatter(a1, axis, 4)
    b2 = ring_scatter(b1, axis, 1)
    return jnp.concatenate([a2, b2], axis=0)


def align_partner_rows(partner, parity, rows):
    half = rows // 2
    lead = partner.shape[:-2]
    cols = partner.shape[-1]
    first = partner[..., : 8 * rows, :].reshape(*lead, RING, RING * half, cols)
    second = partner[..., 8 * rows :, :].reshape(*lead, RING, RING, half, cols)
    axis_a = len(lead)
    axis_b = len(lead) + 1
    first = jnp.where(parity == 0, jnp.roll(first, 1, axis_a), jnp.roll(first, -1, axis_a))
    second = jnp.where(parity == 0, jnp.roll(second, 1, axis_b), jnp.roll(second, -1, axis_b))
    return jnp.concatenate(
        [first.reshape(*lead, 8 * rows, cols), second.reshape(*lead, 8 * rows, cols)], axis=-2
    )


def from_partner(shard, axis, stride):
    return lax.ppermute(shard, axis, [(i, i ^ 1 << stride) for i in range(lax.axis_size(axis))])


def slot_info(length_rows, adapter_rows, slot_ids):
    request_ends = jnp.cumsum(length_rows, axis=1, dtype=jnp.int32)
    starts = request_ends - length_rows
    count_req = length_rows.shape[1]
    request = jnp.sum(
        (slot_ids[:, None] >= request_ends).astype(jnp.int32), axis=1, dtype=jnp.int32
    )
    living = request < count_req
    matches = request[:, None] == jnp.arange(count_req, dtype=jnp.int32)[None, :]
    opening = jnp.sum(jnp.where(matches, starts, 0), axis=1, dtype=jnp.int32)
    position = jnp.where(living, slot_ids - opening, 0)
    segment = jnp.where(living, request, count_req + slot_ids)
    chosen = jnp.sum(jnp.where(matches, adapter_rows, 0), axis=1, dtype=jnp.int32)
    adapter_slot = jnp.where(living, chosen, -1)
    return (living, position, segment, adapter_slot)


def normalize(input_tokens, gain_vec):
    values = input_tokens.astype(jnp.float32)
    factor = lax.rsqrt(jnp.mean(values * values, axis=-1, keepdims=True) + EPSILON)
    return (values * factor * gain_vec).astype(jnp.bfloat16)


def adapter_select_mask(adapter_slot, adapter_column_count, adapter_rank_size):
    token_owner_request = jnp.arange(adapter_column_count, dtype=jnp.int32) // adapter_rank_size
    return (adapter_slot[:, None] == token_owner_request[None, :]).astype(jnp.float32)


def rotate(vectors, position):
    half_dim = vectors.shape[-1] // 2
    inverse = ROPE_THETA ** (-(jnp.arange(half_dim, dtype=jnp.float32) * (2.0 / vectors.shape[-1])))
    angles = position.astype(jnp.float32)[:, None] * inverse[None, :]
    cosine = jnp.cos(angles)[:, None, :]
    sine_part = jnp.sin(angles)[:, None, :]
    lower_half = vectors[..., :half_dim]
    upper_half = vectors[..., half_dim:]
    return jnp.concatenate(
        [
            lower_half * cosine - upper_half * sine_part,
            upper_half * cosine + lower_half * sine_part,
        ],
        axis=-1,
    )


def attend(queries, key_rows, value_rows, position, segment):
    key_heads = key_rows.shape[1]
    group_size = queries.shape[1] // key_heads
    token_count = queries.shape[0]
    grouped_queries = queries.reshape(token_count, key_heads, group_size, queries.shape[2])
    scores = jnp.einsum(
        "qkgd,skd->kgqs", grouped_queries, key_rows, preferred_element_type=jnp.float32
    ) * queries.shape[2] ** (-0.5)
    allowed = (segment[:, None] == segment[None, :]) & (position[None, :] <= position[:, None])
    allowed = allowed & (
        (position[:, None] - position[None, :] < WINDOW) | (position[None, :] < SINK)
    )
    scores = jnp.where(allowed[None, None], scores, -jnp.inf)
    highest = jnp.max(scores, axis=-1, keepdims=True)
    weights_raw = jnp.exp(scores - highest)
    weights = (weights_raw / jnp.sum(weights_raw, axis=-1, keepdims=True)).astype(jnp.bfloat16)
    blended = jnp.einsum("kgqs,skd->qkgd", weights, value_rows, preferred_element_type=jnp.float32)
    return blended.reshape(token_count, -1).astype(jnp.bfloat16)


def spread_rows(first_part, second_part):
    width = first_part.shape[1]
    joined = plane_gather(jnp.concatenate([first_part, second_part], axis=1), "mp")
    return joined[:, :width], joined[:, width:]


def sum_rows(term_fn, row_count):
    return plane_scatter(term_fn(jnp.int32(0), lax.axis_size("mp") * row_count), "mp", row_count)


def feed_forward(
    residual_stream,
    adapter_indicator,
    feed_norm_gain,
    adapter_down_gate_up,
    adapter_up_gate_up,
    gate_up_full,
    down_full,
    adapter_down_feed,
    adapter_up_feed,
):
    adapter_column_count = adapter_indicator.shape[1]
    model_width = residual_stream.shape[1]
    feed_input = normalize(residual_stream, feed_norm_gain)
    gate_terms = (
        jnp.dot(feed_input, adapter_down_gate_up, preferred_element_type=jnp.float32)
        * jnp.tile(adapter_indicator, (1, 2))
    ).astype(jnp.bfloat16)
    mlp_all, gate_adapter_ranks = spread_rows(feed_input, gate_terms)
    gate_activation = jnp.dot(
        mlp_all, gate_up_full[0], preferred_element_type=jnp.float32
    ) + jnp.dot(
        gate_adapter_ranks[:, :adapter_column_count],
        adapter_up_gate_up[0],
        preferred_element_type=jnp.float32,
    )
    up_projected = jnp.dot(mlp_all, gate_up_full[1], preferred_element_type=jnp.float32) + jnp.dot(
        gate_adapter_ranks[:, adapter_column_count:],
        adapter_up_gate_up[1],
        preferred_element_type=jnp.float32,
    )
    hidden_activation = (jax.nn.silu(gate_activation) * up_projected).astype(jnp.bfloat16)

    def down_term(first_row, row_count):
        projected_rows = lax.dot_general(
            hidden_activation,
            down_full,
            (((1,), (1,)), ((), ())),
            preferred_element_type=jnp.float32,
        )
        return jnp.concatenate(
            [
                projected_rows,
                jnp.dot(hidden_activation, adapter_down_feed, preferred_element_type=jnp.float32),
            ],
            axis=1,
        )

    summed = sum_rows(down_term, residual_stream.shape[0])
    down_adapter_ranks = (summed[:, model_width:] * adapter_indicator).astype(jnp.bfloat16)
    return (
        residual_stream.astype(jnp.float32)
        + summed[:, :model_width]
        + jnp.dot(down_adapter_ranks, adapter_up_feed, preferred_element_type=jnp.float32)
    )


def shards(
    states,
    lengths,
    request_adapters,
    attention_norm_gain,
    query_weight,
    key_weight,
    value_weight,
    output_weight,
    adapter_down_attention,
    adapter_up_query,
    adapter_up_key_value,
    adapter_down_output,
    adapter_up_output,
    feed_norm_gain,
    gate_up_weight,
    down_weight,
    adapter_down_gate_up,
    adapter_up_gate_up,
    adapter_down_feed,
    adapter_up_feed,
):
    mp_count = lax.axis_size("mp")
    group_index = lax.axis_index("req")
    mp_index = lax.axis_index("mp")
    slot_dev = states.shape[1]
    model_width = states.shape[3]
    adapter_column_count = adapter_up_output.shape[0]
    total_rows = slot_dev * mp_count
    gate_up_full, down_full = (
        lax.all_gather(gate_up_weight, "req", axis=1, tiled=True),
        lax.all_gather(down_weight, "req", axis=0, tiled=True),
    )
    local_rows = states.reshape(slot_dev, model_width)
    own_lengths = lax.dynamic_index_in_dim(lengths, group_index, 0, keepdims=False)
    own_adapters = lax.dynamic_index_in_dim(request_adapters, group_index, 0, keepdims=False)
    request_count = own_lengths.shape[0]
    local_slots = jnp.arange(slot_dev, dtype=jnp.int32) * mp_count + mp_index
    living, unused_pos, unused_seg, adapter_within = slot_info(
        jnp.broadcast_to(own_lengths[None, :], (slot_dev, request_count)),
        jnp.broadcast_to(own_adapters[None, :], (slot_dev, request_count)),
        local_slots,
    )
    indicator_within = adapter_select_mask(adapter_within, adapter_column_count, ADAPTER_RANK)
    normed_rows = normalize(local_rows, attention_norm_gain)
    down_adapter_terms = (
        jnp.dot(normed_rows, adapter_down_attention, preferred_element_type=jnp.float32)
        * jnp.tile(indicator_within, (1, 3))
    ).astype(jnp.bfloat16)
    normed_all, adapter_terms_all = spread_rows(normed_rows, down_adapter_terms)
    source_device, source_row = plane_rows(mp_index, slot_dev)
    gathered_slots = source_row * mp_count + source_device
    ignored, position_all, segment_all, unused = slot_info(
        jnp.broadcast_to(own_lengths[None, :], (total_rows, request_count)),
        jnp.broadcast_to(own_adapters[None, :], (total_rows, request_count)),
        gathered_slots,
    )
    query_projected = jnp.dot(
        normed_all, query_weight, preferred_element_type=jnp.float32
    ) + jnp.dot(
        adapter_terms_all[:, :adapter_column_count],
        adapter_up_query,
        preferred_element_type=jnp.float32,
    )
    key_projected = jnp.dot(normed_all, key_weight, preferred_element_type=jnp.float32) + jnp.dot(
        adapter_terms_all[:, adapter_column_count : 2 * adapter_column_count],
        adapter_up_key_value[0],
        preferred_element_type=jnp.float32,
    )
    value_projected = jnp.dot(
        normed_all, value_weight, preferred_element_type=jnp.float32
    ) + jnp.dot(
        adapter_terms_all[:, 2 * adapter_column_count :],
        adapter_up_key_value[1],
        preferred_element_type=jnp.float32,
    )
    kv_pair = jnp.stack([key_projected, value_projected])
    partner = align_partner_rows(
        from_partner(kv_pair.astype(jnp.bfloat16), "mp", 0), mp_index % 2, slot_dev
    ).astype(kv_pair.dtype)
    parity = mp_index % 2
    joined = jnp.where(
        parity == 0,
        jnp.concatenate([kv_pair, partner], axis=2),
        jnp.concatenate([partner, kv_pair], axis=2),
    )
    key_projected = joined[0]
    value_projected = joined[1]
    queries = rotate(query_projected.reshape(total_rows, -1, HEAD_SIZE), position_all).astype(
        jnp.bfloat16
    )
    key_rows = rotate(key_projected.reshape(total_rows, -1, HEAD_SIZE), position_all).astype(
        jnp.bfloat16
    )
    value_rows = value_projected.reshape(total_rows, -1, HEAD_SIZE).astype(jnp.bfloat16)
    attention_output = attend(queries, key_rows, value_rows, position_all, segment_all)

    def out_term(first_row, row_count):
        return jnp.concatenate(
            [
                jnp.dot(attention_output, output_weight, preferred_element_type=jnp.float32),
                jnp.dot(attention_output, adapter_down_output, preferred_element_type=jnp.float32),
            ],
            axis=1,
        )

    summed = sum_rows(out_term, slot_dev)
    output_adapter_ranks = (summed[:, model_width:] * indicator_within).astype(jnp.bfloat16)
    residual_stream = (
        local_rows.astype(jnp.float32)
        + summed[:, :model_width]
        + jnp.dot(output_adapter_ranks, adapter_up_output, preferred_element_type=jnp.float32)
    ).astype(jnp.bfloat16)
    layer_result = feed_forward(
        residual_stream,
        indicator_within,
        feed_norm_gain,
        adapter_down_gate_up,
        adapter_up_gate_up,
        gate_up_full,
        down_full,
        adapter_down_feed,
        adapter_up_feed,
    )
    finished = jnp.where(living[:, None], layer_result, jnp.zeros_like(layer_result)).astype(
        jnp.bfloat16
    )
    return finished.reshape(1, slot_dev, 1, model_width)


def solution(mesh):
    placed = (
        P("req", None, "mp", None),
        P(),
        P(),
        P(),
        P(None, "mp"),
        P(None, "mp"),
        P(None, "mp"),
        P("mp", None),
        P(),
        P(None, "mp"),
        P(None, None, "mp"),
        P("mp", None),
        P(),
        P(),
        P(None, "req", "mp"),
        P("req", "mp"),
        P(),
        P(None, None, "mp"),
        P("mp", None),
        P(),
    )
    return jax.shard_map(
        shards, mesh=mesh, in_specs=placed, out_specs=P("req", None, "mp", None), check_vma=False
    )
```

```python
import jax
import jax.numpy as jnp
from jax import lax
from jax.sharding import PartitionSpec as P

HEAD_SIZE = 128
ADAPTER_RANK = 16
WINDOW = 128
SINK = 4


EPSILON = 1e-05
ROPE_THETA = 1000000.0


RING = 4


def _ring_pairs(size, stride, step):
    pairs = []
    for i in range(size):
        low = i % stride
        pos = (i // stride) % RING
        high = i // (stride * RING)
        dst = (high * RING + (pos + step) % RING) * stride + low
        pairs.append((i, dst))
    return pairs


def _shift(x, axis, stride, step):
    return lax.ppermute(x, axis, _ring_pairs(lax.axis_size(axis), stride, step))


def ring_gather(block, axis, stride):
    half = block.shape[0] // 2
    from_minus = _shift(block, axis, stride, 1)
    from_plus = _shift(block, axis, stride, -1)
    first = _shift(from_plus[:half], axis, stride, -1)
    second = _shift(from_minus[half:], axis, stride, 1)
    across = jnp.concatenate([first, second], axis=0)
    return jnp.stack([block, from_plus, across, from_minus])


def ring_scatter(parts, axis, stride):
    half = parts.shape[1] // 2
    wire = jnp.bfloat16
    got_a = _shift(parts[2, :half].astype(wire), axis, stride, 1).astype(jnp.float32)
    got_b = _shift(parts[2, half:].astype(wire), axis, stride, -1).astype(jnp.float32)
    plus = parts[1].at[:half].add(got_a)
    minus = parts[3].at[half:].add(got_b)
    back_a = _shift(minus.astype(wire), axis, stride, -1).astype(jnp.float32)
    back_b = _shift(plus.astype(wire), axis, stride, 1).astype(jnp.float32)
    return parts[0] + back_a + back_b


def ring_gather_direct(block, axis, stride):
    from_minus = _shift(block, axis, stride, 1)
    from_plus = _shift(block, axis, stride, -1)
    across = _shift(block, axis, stride, 2)
    return jnp.stack([block, from_plus, across, from_minus])


def ring_scatter_direct(parts, axis, stride):
    wire = jnp.bfloat16
    got_minus = _shift(parts[1].astype(wire), axis, stride, 1)
    got_plus = _shift(parts[3].astype(wire), axis, stride, -1)
    got_across = _shift(parts[2].astype(wire), axis, stride, 2)
    return (
        parts[0]
        + got_minus.astype(jnp.float32)
        + got_plus.astype(jnp.float32)
        + got_across.astype(jnp.float32)
    )


def plane_gather(block, axis):
    rows, cols = block.shape
    half = rows // 2
    a1 = ring_gather_direct(block[:half], axis, 4)
    b1 = ring_gather_direct(block[half:], axis, 1)
    a2 = ring_gather(a1.reshape(RING * half, cols), axis, 1)
    b2 = ring_gather(b1.reshape(RING * half, cols), axis, 4)
    return jnp.concatenate([a2.reshape(-1, cols), b2.reshape(-1, cols)], axis=0)


def plane_rows(mp_index, rows):
    half = rows // 2
    px, py = mp_index // RING, mp_index % RING
    g = jnp.arange(16 * rows, dtype=jnp.int32)
    second = g >= 8 * rows
    h = g % half
    outer = (g % (8 * rows)) // (RING * half)
    inner = (g % (RING * half)) // half
    kx = jnp.where(second, outer, inner)
    ky = jnp.where(second, inner, outer)
    src = ((px + kx) % RING) * RING + (py + ky) % RING
    local = jnp.where(second, h + half, h)
    return src, local


def plane_scatter(parts, axis, rows):
    cols = parts.shape[1]
    half = rows // 2
    a = parts[: 8 * rows].reshape(RING, RING * half, cols)
    b = parts[8 * rows:].reshape(RING, RING * half, cols)
    a1 = ring_scatter(a, axis, 1).reshape(RING, half, cols)
    b1 = ring_scatter(b, axis, 4).reshape(RING, half, cols)
    a2 = ring_scatter_direct(a1, axis, 4)
    b2 = ring_scatter_direct(b1, axis, 1)
    return jnp.concatenate([a2, b2], axis=0)


def align_partner_rows(partner, parity, rows):
    half = rows // 2
    lead = partner.shape[:-2]
    cols = partner.shape[-1]
    first = partner[..., : 8 * rows, :].reshape(*lead, RING, RING * half, cols)
    second = partner[..., 8 * rows :, :].reshape(*lead, RING, RING, half, cols)
    axis_a = len(lead)
    axis_b = len(lead) + 1
    first = jnp.where(parity == 0, jnp.roll(first, 1, axis_a), jnp.roll(first, -1, axis_a))
    second = jnp.where(parity == 0, jnp.roll(second, 1, axis_b), jnp.roll(second, -1, axis_b))
    return jnp.concatenate(
        [first.reshape(*lead, 8 * rows, cols), second.reshape(*lead, 8 * rows, cols)], axis=-2
    )


def from_partner(shard, axis, stride):
    return lax.ppermute(shard, axis, [(i, i ^ 1 << stride) for i in range(lax.axis_size(axis))])


def slot_info(length_rows, adapter_rows, slot_ids):
    request_ends = jnp.cumsum(length_rows, axis=1, dtype=jnp.int32)
    starts = request_ends - length_rows
    count_req = length_rows.shape[1]
    request = jnp.sum(
        (slot_ids[:, None] >= request_ends).astype(jnp.int32), axis=1, dtype=jnp.int32
    )
    living = request < count_req
    matches = request[:, None] == jnp.arange(count_req, dtype=jnp.int32)[None, :]
    opening = jnp.sum(jnp.where(matches, starts, 0), axis=1, dtype=jnp.int32)
    position = jnp.where(living, slot_ids - opening, 0)
    segment = jnp.where(living, request, count_req + slot_ids)
    chosen = jnp.sum(jnp.where(matches, adapter_rows, 0), axis=1, dtype=jnp.int32)
    adapter_slot = jnp.where(living, chosen, -1)
    return (living, position, segment, adapter_slot)


def normalize(input_tokens, gain_vec):
    values = input_tokens.astype(jnp.float32)
    factor = lax.rsqrt(jnp.mean(values * values, axis=-1, keepdims=True) + EPSILON)
    return (values * factor * gain_vec).astype(jnp.bfloat16)


def adapter_select_mask(adapter_slot, adapter_column_count, adapter_rank_size):
    token_owner_request = jnp.arange(adapter_column_count, dtype=jnp.int32) // adapter_rank_size
    return (adapter_slot[:, None] == token_owner_request[None, :]).astype(jnp.float32)


def rotate(vectors, position):
    half_dim = vectors.shape[-1] // 2
    inverse = ROPE_THETA ** (-(jnp.arange(half_dim, dtype=jnp.float32) * (2.0 / vectors.shape[-1])))
    angles = position.astype(jnp.float32)[:, None] * inverse[None, :]
    cosine = jnp.cos(angles)[:, None, :]
    sine_part = jnp.sin(angles)[:, None, :]
    lower_half = vectors[..., :half_dim]
    upper_half = vectors[..., half_dim:]
    return jnp.concatenate(
        [
            lower_half * cosine - upper_half * sine_part,
            upper_half * cosine + lower_half * sine_part,
        ],
        axis=-1,
    )


def attend(queries, key_rows, value_rows, position, segment):
    key_heads = key_rows.shape[1]
    group_size = queries.shape[1] // key_heads
    token_count = queries.shape[0]
    grouped_queries = queries.reshape(token_count, key_heads, group_size, queries.shape[2])
    scores = jnp.einsum(
        "qkgd,skd->kgqs", grouped_queries, key_rows, preferred_element_type=jnp.float32
    ) * queries.shape[2] ** (-0.5)
    allowed = (segment[:, None] == segment[None, :]) & (position[None, :] <= position[:, None])
    allowed = allowed & (
        (position[:, None] - position[None, :] < WINDOW) | (position[None, :] < SINK)
    )
    scores = jnp.where(allowed[None, None], scores, -jnp.inf)
    highest = jnp.max(scores, axis=-1, keepdims=True)
    weights_raw = jnp.exp(scores - highest)
    weights = (weights_raw / jnp.sum(weights_raw, axis=-1, keepdims=True)).astype(jnp.bfloat16)
    blended = jnp.einsum("kgqs,skd->qkgd", weights, value_rows, preferred_element_type=jnp.float32)
    return blended.reshape(token_count, -1).astype(jnp.bfloat16)


def spread_rows(first_part, second_part):
    width = first_part.shape[1]
    joined = plane_gather(jnp.concatenate([first_part, second_part], axis=1), "mp")
    return joined[:, :width], joined[:, width:]


def sum_rows(term_fn, row_count):
    return plane_scatter(term_fn(jnp.int32(0), lax.axis_size("mp") * row_count), "mp", row_count)


def feed_forward(
    residual_stream,
    adapter_indicator,
    feed_norm_gain,
    adapter_down_gate_up,
    adapter_up_gate_up,
    gate_up_full,
    down_full,
    adapter_down_feed,
    adapter_up_feed,
):
    adapter_column_count = adapter_indicator.shape[1]
    model_width = residual_stream.shape[1]
    feed_input = normalize(residual_stream, feed_norm_gain)
    gate_terms = (
        jnp.dot(feed_input, adapter_down_gate_up, preferred_element_type=jnp.float32)
        * jnp.tile(adapter_indicator, (1, 2))
    ).astype(jnp.bfloat16)
    mlp_all, gate_adapter_ranks = spread_rows(feed_input, gate_terms)
    gate_activation = jnp.dot(
        mlp_all, gate_up_full[0], preferred_element_type=jnp.float32
    ) + jnp.dot(
        gate_adapter_ranks[:, :adapter_column_count],
        adapter_up_gate_up[0],
        preferred_element_type=jnp.float32,
    )
    up_projected = jnp.dot(mlp_all, gate_up_full[1], preferred_element_type=jnp.float32) + jnp.dot(
        gate_adapter_ranks[:, adapter_column_count:],
        adapter_up_gate_up[1],
        preferred_element_type=jnp.float32,
    )
    hidden_activation = (jax.nn.silu(gate_activation) * up_projected).astype(jnp.bfloat16)

    def down_term(first_row, row_count):
        projected_rows = lax.dot_general(
            hidden_activation,
            down_full,
            (((1,), (1,)), ((), ())),
            preferred_element_type=jnp.float32,
        )
        return jnp.concatenate(
            [
                projected_rows,
                jnp.dot(hidden_activation, adapter_down_feed, preferred_element_type=jnp.float32),
            ],
            axis=1,
        )

    summed = sum_rows(down_term, residual_stream.shape[0])
    down_adapter_ranks = (summed[:, model_width:] * adapter_indicator).astype(jnp.bfloat16)
    return (
        residual_stream.astype(jnp.float32)
        + summed[:, :model_width]
        + jnp.dot(down_adapter_ranks, adapter_up_feed, preferred_element_type=jnp.float32)
    )


def shards(
    states,
    lengths,
    request_adapters,
    attention_norm_gain,
    query_weight,
    key_weight,
    value_weight,
    output_weight,
    adapter_down_attention,
    adapter_up_query,
    adapter_up_key_value,
    adapter_down_output,
    adapter_up_output,
    feed_norm_gain,
    gate_up_weight,
    down_weight,
    adapter_down_gate_up,
    adapter_up_gate_up,
    adapter_down_feed,
    adapter_up_feed,
):
    mp_count = lax.axis_size("mp")
    group_index = lax.axis_index("req")
    mp_index = lax.axis_index("mp")
    slot_dev = states.shape[1]
    model_width = states.shape[3]
    adapter_column_count = adapter_up_output.shape[0]
    total_rows = slot_dev * mp_count
    gate_up_full, down_full = (
        lax.all_gather(gate_up_weight, "req", axis=1, tiled=True),
        lax.all_gather(down_weight, "req", axis=0, tiled=True),
    )
    local_rows = states.reshape(slot_dev, model_width)
    own_lengths = lax.dynamic_index_in_dim(lengths, group_index, 0, keepdims=False)
    own_adapters = lax.dynamic_index_in_dim(request_adapters, group_index, 0, keepdims=False)
    request_count = own_lengths.shape[0]
    local_slots = jnp.arange(slot_dev, dtype=jnp.int32) * mp_count + mp_index
    living, unused_pos, unused_seg, adapter_within = slot_info(
        jnp.broadcast_to(own_lengths[None, :], (slot_dev, request_count)),
        jnp.broadcast_to(own_adapters[None, :], (slot_dev, request_count)),
        local_slots,
    )
    indicator_within = adapter_select_mask(adapter_within, adapter_column_count, ADAPTER_RANK)
    normed_rows = normalize(local_rows, attention_norm_gain)
    down_adapter_terms = (
        jnp.dot(normed_rows, adapter_down_attention, preferred_element_type=jnp.float32)
        * jnp.tile(indicator_within, (1, 3))
    ).astype(jnp.bfloat16)
    normed_all, adapter_terms_all = spread_rows(normed_rows, down_adapter_terms)
    source_device, source_row = plane_rows(mp_index, slot_dev)
    gathered_slots = source_row * mp_count + source_device
    ignored, position_all, segment_all, unused = slot_info(
        jnp.broadcast_to(own_lengths[None, :], (total_rows, request_count)),
        jnp.broadcast_to(own_adapters[None, :], (total_rows, request_count)),
        gathered_slots,
    )
    query_projected = jnp.dot(
        normed_all, query_weight, preferred_element_type=jnp.float32
    ) + jnp.dot(
        adapter_terms_all[:, :adapter_column_count],
        adapter_up_query,
        preferred_element_type=jnp.float32,
    )
    key_projected = jnp.dot(normed_all, key_weight, preferred_element_type=jnp.float32) + jnp.dot(
        adapter_terms_all[:, adapter_column_count : 2 * adapter_column_count],
        adapter_up_key_value[0],
        preferred_element_type=jnp.float32,
    )
    value_projected = jnp.dot(
        normed_all, value_weight, preferred_element_type=jnp.float32
    ) + jnp.dot(
        adapter_terms_all[:, 2 * adapter_column_count :],
        adapter_up_key_value[1],
        preferred_element_type=jnp.float32,
    )
    kv_pair = jnp.stack([key_projected, value_projected])
    partner = align_partner_rows(
        from_partner(kv_pair.astype(jnp.bfloat16), "mp", 0), mp_index % 2, slot_dev
    ).astype(kv_pair.dtype)
    parity = mp_index % 2
    joined = jnp.where(
        parity == 0,
        jnp.concatenate([kv_pair, partner], axis=2),
        jnp.concatenate([partner, kv_pair], axis=2),
    )
    key_projected = joined[0]
    value_projected = joined[1]
    queries = rotate(query_projected.reshape(total_rows, -1, HEAD_SIZE), position_all).astype(
        jnp.bfloat16
    )
    key_rows = rotate(key_projected.reshape(total_rows, -1, HEAD_SIZE), position_all).astype(
        jnp.bfloat16
    )
    value_rows = value_projected.reshape(total_rows, -1, HEAD_SIZE).astype(jnp.bfloat16)
    attention_output = attend(queries, key_rows, value_rows, position_all, segment_all)

    def out_term(first_row, row_count):
        return jnp.concatenate(
            [
                jnp.dot(attention_output, output_weight, preferred_element_type=jnp.float32),
                jnp.dot(attention_output, adapter_down_output, preferred_element_type=jnp.float32),
            ],
            axis=1,
        )

    summed = sum_rows(out_term, slot_dev)
    output_adapter_ranks = (summed[:, model_width:] * indicator_within).astype(jnp.bfloat16)
    residual_stream = (
        local_rows.astype(jnp.float32)
        + summed[:, :model_width]
        + jnp.dot(output_adapter_ranks, adapter_up_output, preferred_element_type=jnp.float32)
    ).astype(jnp.bfloat16)
    layer_result = feed_forward(
        residual_stream,
        indicator_within,
        feed_norm_gain,
        adapter_down_gate_up,
        adapter_up_gate_up,
        gate_up_full,
        down_full,
        adapter_down_feed,
        adapter_up_feed,
    )
    finished = jnp.where(living[:, None], layer_result, jnp.zeros_like(layer_result)).astype(
        jnp.bfloat16
    )
    return finished.reshape(1, slot_dev, 1, model_width)


def solution(mesh):
    placed = (
        P("req", None, "mp", None),
        P(),
        P(),
        P(),
        P(None, "mp"),
        P(None, "mp"),
        P(None, "mp"),
        P("mp", None),
        P(),
        P(None, "mp"),
        P(None, None, "mp"),
        P("mp", None),
        P(),
        P(),
        P(None, "req", "mp"),
        P("req", "mp"),
        P(),
        P(None, None, "mp"),
        P("mp", None),
        P(),
    )
    return jax.shard_map(
        shards, mesh=mesh, in_specs=placed, out_specs=P("req", None, "mp", None), check_vma=False
    )
```

```python
import jax
import jax.numpy as jnp
from jax import lax
from jax.sharding import PartitionSpec as P

HEAD_SIZE = 128
ADAPTER_RANK = 16
WINDOW = 128
SINK = 4


EPSILON = 1e-05
ROPE_THETA = 1000000.0


RING = 4


def _ring_pairs(size, stride, step):
    pairs = []
    for i in range(size):
        low = i % stride
        pos = (i // stride) % RING
        high = i // (stride * RING)
        dst = (high * RING + (pos + step) % RING) * stride + low
        pairs.append((i, dst))
    return pairs


def _shift(x, axis, stride, step):
    return lax.ppermute(x, axis, _ring_pairs(lax.axis_size(axis), stride, step))


def ring_gather(block, axis, stride):
    half = block.shape[0] // 2
    from_minus = _shift(block, axis, stride, 1)
    from_plus = _shift(block, axis, stride, -1)
    first = _shift(from_plus[:half], axis, stride, -1)
    second = _shift(from_minus[half:], axis, stride, 1)
    across = jnp.concatenate([first, second], axis=0)
    return jnp.stack([block, from_plus, across, from_minus])


def ring_scatter(parts, axis, stride):
    half = parts.shape[1] // 2
    wire = jnp.bfloat16
    got_a = _shift(parts[2, :half].astype(wire), axis, stride, 1).astype(jnp.float32)
    got_b = _shift(parts[2, half:].astype(wire), axis, stride, -1).astype(jnp.float32)
    plus = parts[1].at[:half].add(got_a)
    minus = parts[3].at[half:].add(got_b)
    back_a = _shift(minus.astype(wire), axis, stride, -1).astype(jnp.float32)
    back_b = _shift(plus.astype(wire), axis, stride, 1).astype(jnp.float32)
    return parts[0] + back_a + back_b


def ring_gather_direct(block, axis, stride):
    from_minus = _shift(block, axis, stride, 1)
    from_plus = _shift(block, axis, stride, -1)
    across = _shift(block, axis, stride, 2)
    return jnp.stack([block, from_plus, across, from_minus])


def ring_scatter_direct(parts, axis, stride):
    wire = jnp.bfloat16
    got_minus = _shift(parts[1].astype(wire), axis, stride, 1)
    got_plus = _shift(parts[3].astype(wire), axis, stride, -1)
    got_across = _shift(parts[2].astype(wire), axis, stride, 2)
    return (
        parts[0]
        + got_minus.astype(jnp.float32)
        + got_plus.astype(jnp.float32)
        + got_across.astype(jnp.float32)
    )


def plane_gather(block, axis):
    rows, cols = block.shape
    half = rows // 2
    a1 = ring_gather_direct(block[:half], axis, 4)
    b1 = ring_gather_direct(block[half:], axis, 1)
    a2 = ring_gather(a1.reshape(RING * half, cols), axis, 1)
    b2 = ring_gather(b1.reshape(RING * half, cols), axis, 4)
    return jnp.concatenate([a2.reshape(-1, cols), b2.reshape(-1, cols)], axis=0)


def stream_gather(part, axis, strides):
    half, cols = part.shape
    first = ring_gather_direct(part, axis, strides[0])
    return ring_gather(first.reshape(RING * half, cols), axis, strides[1]).reshape(-1, cols)


def stream_scatter(parts, axis, strides):
    cols = parts.shape[1]
    half = parts.shape[0] // (RING * RING)
    first = ring_scatter(parts.reshape(RING, RING * half, cols), axis, strides[1])
    return ring_scatter_direct(first.reshape(RING, half, cols), axis, strides[0])


STREAM_STRIDES = ((4, 1), (1, 4))


def plane_rows(mp_index, rows):
    half = rows // 2
    px, py = mp_index // RING, mp_index % RING
    g = jnp.arange(16 * rows, dtype=jnp.int32)
    second = g >= 8 * rows
    h = g % half
    outer = (g % (8 * rows)) // (RING * half)
    inner = (g % (RING * half)) // half
    kx = jnp.where(second, outer, inner)
    ky = jnp.where(second, inner, outer)
    src = ((px + kx) % RING) * RING + (py + ky) % RING
    local = jnp.where(second, h + half, h)
    return src, local


def plane_scatter(parts, axis, rows):
    cols = parts.shape[1]
    half = rows // 2
    a = parts[: 8 * rows].reshape(RING, RING * half, cols)
    b = parts[8 * rows:].reshape(RING, RING * half, cols)
    a1 = ring_scatter(a, axis, 1).reshape(RING, half, cols)
    b1 = ring_scatter(b, axis, 4).reshape(RING, half, cols)
    a2 = ring_scatter_direct(a1, axis, 4)
    b2 = ring_scatter_direct(b1, axis, 1)
    return jnp.concatenate([a2, b2], axis=0)


def align_partner_rows(partner, parity, rows):
    half = rows // 2
    lead = partner.shape[:-2]
    cols = partner.shape[-1]
    first = partner[..., : 8 * rows, :].reshape(*lead, RING, RING * half, cols)
    second = partner[..., 8 * rows :, :].reshape(*lead, RING, RING, half, cols)
    axis_a = len(lead)
    axis_b = len(lead) + 1
    first = jnp.where(parity == 0, jnp.roll(first, 1, axis_a), jnp.roll(first, -1, axis_a))
    second = jnp.where(parity == 0, jnp.roll(second, 1, axis_b), jnp.roll(second, -1, axis_b))
    return jnp.concatenate(
        [first.reshape(*lead, 8 * rows, cols), second.reshape(*lead, 8 * rows, cols)], axis=-2
    )


def from_partner(shard, axis, stride):
    return lax.ppermute(shard, axis, [(i, i ^ 1 << stride) for i in range(lax.axis_size(axis))])


def slot_info(length_rows, adapter_rows, slot_ids):
    request_ends = jnp.cumsum(length_rows, axis=1, dtype=jnp.int32)
    starts = request_ends - length_rows
    count_req = length_rows.shape[1]
    request = jnp.sum(
        (slot_ids[:, None] >= request_ends).astype(jnp.int32), axis=1, dtype=jnp.int32
    )
    living = request < count_req
    matches = request[:, None] == jnp.arange(count_req, dtype=jnp.int32)[None, :]
    opening = jnp.sum(jnp.where(matches, starts, 0), axis=1, dtype=jnp.int32)
    position = jnp.where(living, slot_ids - opening, 0)
    segment = jnp.where(living, request, count_req + slot_ids)
    chosen = jnp.sum(jnp.where(matches, adapter_rows, 0), axis=1, dtype=jnp.int32)
    adapter_slot = jnp.where(living, chosen, -1)
    return (living, position, segment, adapter_slot)


def normalize(input_tokens, gain_vec):
    values = input_tokens.astype(jnp.float32)
    factor = lax.rsqrt(jnp.mean(values * values, axis=-1, keepdims=True) + EPSILON)
    return (values * factor * gain_vec).astype(jnp.bfloat16)


def adapter_select_mask(adapter_slot, adapter_column_count, adapter_rank_size):
    token_owner_request = jnp.arange(adapter_column_count, dtype=jnp.int32) // adapter_rank_size
    return (adapter_slot[:, None] == token_owner_request[None, :]).astype(jnp.float32)


def rotate(vectors, position):
    half_dim = vectors.shape[-1] // 2
    inverse = ROPE_THETA ** (-(jnp.arange(half_dim, dtype=jnp.float32) * (2.0 / vectors.shape[-1])))
    angles = position.astype(jnp.float32)[:, None] * inverse[None, :]
    cosine = jnp.cos(angles)[:, None, :]
    sine_part = jnp.sin(angles)[:, None, :]
    lower_half = vectors[..., :half_dim]
    upper_half = vectors[..., half_dim:]
    return jnp.concatenate(
        [
            lower_half * cosine - upper_half * sine_part,
            upper_half * cosine + lower_half * sine_part,
        ],
        axis=-1,
    )


def attend(queries, key_rows, value_rows, position, segment):
    key_heads = key_rows.shape[1]
    group_size = queries.shape[1] // key_heads
    token_count = queries.shape[0]
    grouped_queries = queries.reshape(token_count, key_heads, group_size, queries.shape[2])
    scores = jnp.einsum(
        "qkgd,skd->kgqs", grouped_queries, key_rows, preferred_element_type=jnp.float32
    ) * queries.shape[2] ** (-0.5)
    allowed = (segment[:, None] == segment[None, :]) & (position[None, :] <= position[:, None])
    allowed = allowed & (
        (position[:, None] - position[None, :] < WINDOW) | (position[None, :] < SINK)
    )
    scores = jnp.where(allowed[None, None], scores, -jnp.inf)
    highest = jnp.max(scores, axis=-1, keepdims=True)
    weights_raw = jnp.exp(scores - highest)
    weights = (weights_raw / jnp.sum(weights_raw, axis=-1, keepdims=True)).astype(jnp.bfloat16)
    blended = jnp.einsum("kgqs,skd->qkgd", weights, value_rows, preferred_element_type=jnp.float32)
    return blended.reshape(token_count, -1).astype(jnp.bfloat16)


def spread_rows(first_part, second_part):
    width = first_part.shape[1]
    joined = plane_gather(jnp.concatenate([first_part, second_part], axis=1), "mp")
    return joined[:, :width], joined[:, width:]


def sum_rows(term_fn, row_count):
    return plane_scatter(term_fn(jnp.int32(0), lax.axis_size("mp") * row_count), "mp", row_count)


def feed_forward(
    residual_stream,
    adapter_indicator,
    feed_norm_gain,
    adapter_down_gate_up,
    adapter_up_gate_up,
    gate_up_full,
    down_full,
    adapter_down_feed,
    adapter_up_feed,
    strides,
):
    adapter_column_count = adapter_indicator.shape[1]
    model_width = residual_stream.shape[1]
    feed_input = normalize(residual_stream, feed_norm_gain)
    gate_terms = (
        jnp.dot(feed_input, adapter_down_gate_up, preferred_element_type=jnp.float32)
        * jnp.tile(adapter_indicator, (1, 2))
    ).astype(jnp.bfloat16)
    joined = stream_gather(jnp.concatenate([feed_input, gate_terms], axis=1), "mp", strides)
    mlp_all = joined[:, :model_width]
    gate_adapter_ranks = joined[:, model_width:]
    gate_activation = jnp.dot(
        mlp_all, gate_up_full[0], preferred_element_type=jnp.float32
    ) + jnp.dot(
        gate_adapter_ranks[:, :adapter_column_count],
        adapter_up_gate_up[0],
        preferred_element_type=jnp.float32,
    )
    up_projected = jnp.dot(mlp_all, gate_up_full[1], preferred_element_type=jnp.float32) + jnp.dot(
        gate_adapter_ranks[:, adapter_column_count:],
        adapter_up_gate_up[1],
        preferred_element_type=jnp.float32,
    )
    hidden_activation = (jax.nn.silu(gate_activation) * up_projected).astype(jnp.bfloat16)

    def down_term(first_row, row_count):
        projected_rows = lax.dot_general(
            hidden_activation,
            down_full,
            (((1,), (1,)), ((), ())),
            preferred_element_type=jnp.float32,
        )
        return jnp.concatenate(
            [
                projected_rows,
                jnp.dot(hidden_activation, adapter_down_feed, preferred_element_type=jnp.float32),
            ],
            axis=1,
        )

    summed = stream_scatter(down_term(0, 0), "mp", strides)
    down_adapter_ranks = (summed[:, model_width:] * adapter_indicator).astype(jnp.bfloat16)
    return (
        residual_stream.astype(jnp.float32)
        + summed[:, :model_width]
        + jnp.dot(down_adapter_ranks, adapter_up_feed, preferred_element_type=jnp.float32)
    )


def shards(
    states,
    lengths,
    request_adapters,
    attention_norm_gain,
    query_weight,
    key_weight,
    value_weight,
    output_weight,
    adapter_down_attention,
    adapter_up_query,
    adapter_up_key_value,
    adapter_down_output,
    adapter_up_output,
    feed_norm_gain,
    gate_up_weight,
    down_weight,
    adapter_down_gate_up,
    adapter_up_gate_up,
    adapter_down_feed,
    adapter_up_feed,
):
    mp_count = lax.axis_size("mp")
    group_index = lax.axis_index("req")
    mp_index = lax.axis_index("mp")
    slot_dev = states.shape[1]
    model_width = states.shape[3]
    adapter_column_count = adapter_up_output.shape[0]
    total_rows = slot_dev * mp_count
    gate_up_full, down_full = (
        lax.all_gather(gate_up_weight, "req", axis=1, tiled=True),
        lax.all_gather(down_weight, "req", axis=0, tiled=True),
    )
    local_rows = states.reshape(slot_dev, model_width)
    own_lengths = lax.dynamic_index_in_dim(lengths, group_index, 0, keepdims=False)
    own_adapters = lax.dynamic_index_in_dim(request_adapters, group_index, 0, keepdims=False)
    request_count = own_lengths.shape[0]
    local_slots = jnp.arange(slot_dev, dtype=jnp.int32) * mp_count + mp_index
    living, unused_pos, unused_seg, adapter_within = slot_info(
        jnp.broadcast_to(own_lengths[None, :], (slot_dev, request_count)),
        jnp.broadcast_to(own_adapters[None, :], (slot_dev, request_count)),
        local_slots,
    )
    indicator_within = adapter_select_mask(adapter_within, adapter_column_count, ADAPTER_RANK)
    normed_rows = normalize(local_rows, attention_norm_gain)
    down_adapter_terms = (
        jnp.dot(normed_rows, adapter_down_attention, preferred_element_type=jnp.float32)
        * jnp.tile(indicator_within, (1, 3))
    ).astype(jnp.bfloat16)
    normed_all, adapter_terms_all = spread_rows(normed_rows, down_adapter_terms)
    source_device, source_row = plane_rows(mp_index, slot_dev)
    gathered_slots = source_row * mp_count + source_device
    ignored, position_all, segment_all, unused = slot_info(
        jnp.broadcast_to(own_lengths[None, :], (total_rows, request_count)),
        jnp.broadcast_to(own_adapters[None, :], (total_rows, request_count)),
        gathered_slots,
    )
    query_projected = jnp.dot(
        normed_all, query_weight, preferred_element_type=jnp.float32
    ) + jnp.dot(
        adapter_terms_all[:, :adapter_column_count],
        adapter_up_query,
        preferred_element_type=jnp.float32,
    )
    key_projected = jnp.dot(normed_all, key_weight, preferred_element_type=jnp.float32) + jnp.dot(
        adapter_terms_all[:, adapter_column_count : 2 * adapter_column_count],
        adapter_up_key_value[0],
        preferred_element_type=jnp.float32,
    )
    value_projected = jnp.dot(
        normed_all, value_weight, preferred_element_type=jnp.float32
    ) + jnp.dot(
        adapter_terms_all[:, 2 * adapter_column_count :],
        adapter_up_key_value[1],
        preferred_element_type=jnp.float32,
    )
    kv_pair = jnp.stack([key_projected, value_projected])
    partner = align_partner_rows(
        from_partner(kv_pair.astype(jnp.bfloat16), "mp", 0), mp_index % 2, slot_dev
    ).astype(kv_pair.dtype)
    parity = mp_index % 2
    joined = jnp.where(
        parity == 0,
        jnp.concatenate([kv_pair, partner], axis=2),
        jnp.concatenate([partner, kv_pair], axis=2),
    )
    key_projected = joined[0]
    value_projected = joined[1]
    queries = rotate(query_projected.reshape(total_rows, -1, HEAD_SIZE), position_all).astype(
        jnp.bfloat16
    )
    key_rows = rotate(key_projected.reshape(total_rows, -1, HEAD_SIZE), position_all).astype(
        jnp.bfloat16
    )
    value_rows = value_projected.reshape(total_rows, -1, HEAD_SIZE).astype(jnp.bfloat16)
    attention_output = attend(queries, key_rows, value_rows, position_all, segment_all)

    stream_rows = attention_output.shape[0] // len(STREAM_STRIDES)
    local_half = slot_dev // len(STREAM_STRIDES)
    results = []
    for index, strides in enumerate(STREAM_STRIDES):
        attended = attention_output[index * stream_rows : (index + 1) * stream_rows]
        own = slice(index * local_half, (index + 1) * local_half)
        indicator = indicator_within[own]
        partial = jnp.concatenate(
            [
                jnp.dot(attended, output_weight, preferred_element_type=jnp.float32),
                jnp.dot(attended, adapter_down_output, preferred_element_type=jnp.float32),
            ],
            axis=1,
        )
        summed = stream_scatter(partial, "mp", strides)
        output_adapter_ranks = (summed[:, model_width:] * indicator).astype(jnp.bfloat16)
        residual_stream = (
            local_rows[own].astype(jnp.float32)
            + summed[:, :model_width]
            + jnp.dot(output_adapter_ranks, adapter_up_output, preferred_element_type=jnp.float32)
        ).astype(jnp.bfloat16)
        results.append(
            feed_forward(
                residual_stream,
                indicator,
                feed_norm_gain,
                adapter_down_gate_up,
                adapter_up_gate_up,
                gate_up_full,
                down_full,
                adapter_down_feed,
                adapter_up_feed,
                strides,
            )
        )
    layer_result = jnp.concatenate(results, axis=0)
    finished = jnp.where(living[:, None], layer_result, jnp.zeros_like(layer_result)).astype(
        jnp.bfloat16
    )
    return finished.reshape(1, slot_dev, 1, model_width)


def solution(mesh):
    placed = (
        P("req", None, "mp", None),
        P(),
        P(),
        P(),
        P(None, "mp"),
        P(None, "mp"),
        P(None, "mp"),
        P("mp", None),
        P(),
        P(None, "mp"),
        P(None, None, "mp"),
        P("mp", None),
        P(),
        P(),
        P(None, "req", "mp"),
        P("req", "mp"),
        P(),
        P(None, None, "mp"),
        P("mp", None),
        P(),
    )
    return jax.shard_map(
        shards, mesh=mesh, in_specs=placed, out_specs=P("req", None, "mp", None), check_vma=False
    )
```

```python
import jax
import jax.numpy as jnp
from jax import lax
from jax.sharding import PartitionSpec as P

HEAD_SIZE = 128
ADAPTER_RANK = 16
WINDOW = 128
SINK = 4


EPSILON = 1e-05
ROPE_THETA = 1000000.0


RING = 4


def _ring_pairs(size, stride, step):
    pairs = []
    for i in range(size):
        low = i % stride
        pos = (i // stride) % RING
        high = i // (stride * RING)
        dst = (high * RING + (pos + step) % RING) * stride + low
        pairs.append((i, dst))
    return pairs


def _shift(x, axis, stride, step):
    return lax.ppermute(x, axis, _ring_pairs(lax.axis_size(axis), stride, step))


def ring_gather(block, axis, stride):
    half = block.shape[0] // 2
    from_minus = _shift(block, axis, stride, 1)
    from_plus = _shift(block, axis, stride, -1)
    first = _shift(from_plus[:half], axis, stride, -1)
    second = _shift(from_minus[half:], axis, stride, 1)
    across = jnp.concatenate([first, second], axis=0)
    return jnp.stack([block, from_plus, across, from_minus])


def ring_scatter(parts, axis, stride):
    half = parts.shape[1] // 2
    wire = jnp.bfloat16
    got_a = _shift(parts[2, :half].astype(wire), axis, stride, 1).astype(jnp.float32)
    got_b = _shift(parts[2, half:].astype(wire), axis, stride, -1).astype(jnp.float32)
    plus = parts[1].at[:half].add(got_a)
    minus = parts[3].at[half:].add(got_b)
    back_a = _shift(minus.astype(wire), axis, stride, -1).astype(jnp.float32)
    back_b = _shift(plus.astype(wire), axis, stride, 1).astype(jnp.float32)
    return parts[0] + back_a + back_b


def ring_gather_direct(block, axis, stride):
    from_minus = _shift(block, axis, stride, 1)
    from_plus = _shift(block, axis, stride, -1)
    across = _shift(block, axis, stride, 2)
    return jnp.stack([block, from_plus, across, from_minus])


def ring_scatter_direct(parts, axis, stride):
    wire = jnp.bfloat16
    got_minus = _shift(parts[1].astype(wire), axis, stride, 1)
    got_plus = _shift(parts[3].astype(wire), axis, stride, -1)
    got_across = _shift(parts[2].astype(wire), axis, stride, 2)
    return (
        parts[0]
        + got_minus.astype(jnp.float32)
        + got_plus.astype(jnp.float32)
        + got_across.astype(jnp.float32)
    )


def plane_gather(block, axis):
    rows, cols = block.shape
    half = rows // 2
    a1 = ring_gather_direct(block[:half], axis, 4)
    b1 = ring_gather_direct(block[half:], axis, 1)
    a2 = ring_gather(a1.reshape(RING * half, cols), axis, 1)
    b2 = ring_gather(b1.reshape(RING * half, cols), axis, 4)
    return jnp.concatenate([a2.reshape(-1, cols), b2.reshape(-1, cols)], axis=0)


def plane_rows(mp_index, rows):
    half = rows // 2
    px, py = mp_index // RING, mp_index % RING
    g = jnp.arange(16 * rows, dtype=jnp.int32)
    second = g >= 8 * rows
    h = g % half
    outer = (g % (8 * rows)) // (RING * half)
    inner = (g % (RING * half)) // half
    kx = jnp.where(second, outer, inner)
    ky = jnp.where(second, inner, outer)
    src = ((px + kx) % RING) * RING + (py + ky) % RING
    local = jnp.where(second, h + half, h)
    return src, local


def plane_scatter(parts, axis, rows):
    cols = parts.shape[1]
    half = rows // 2
    a = parts[: 8 * rows].reshape(RING, RING * half, cols)
    b = parts[8 * rows:].reshape(RING, RING * half, cols)
    a1 = ring_scatter(a, axis, 1).reshape(RING, half, cols)
    b1 = ring_scatter(b, axis, 4).reshape(RING, half, cols)
    a2 = ring_scatter_direct(a1, axis, 4)
    b2 = ring_scatter_direct(b1, axis, 1)
    return jnp.concatenate([a2, b2], axis=0)


def align_partner_rows(partner, parity, rows):
    half = rows // 2
    lead = partner.shape[:-2]
    cols = partner.shape[-1]
    first = partner[..., : 8 * rows, :].reshape(*lead, RING, RING * half, cols)
    second = partner[..., 8 * rows :, :].reshape(*lead, RING, RING, half, cols)
    axis_a = len(lead)
    axis_b = len(lead) + 1
    first = jnp.where(parity == 0, jnp.roll(first, 1, axis_a), jnp.roll(first, -1, axis_a))
    second = jnp.where(parity == 0, jnp.roll(second, 1, axis_b), jnp.roll(second, -1, axis_b))
    return jnp.concatenate(
        [first.reshape(*lead, 8 * rows, cols), second.reshape(*lead, 8 * rows, cols)], axis=-2
    )


def from_partner(shard, axis, stride):
    return lax.ppermute(shard, axis, [(i, i ^ 1 << stride) for i in range(lax.axis_size(axis))])


def slot_info(length_rows, adapter_rows, slot_ids):
    request_ends = jnp.cumsum(length_rows, axis=1, dtype=jnp.int32)
    starts = request_ends - length_rows
    count_req = length_rows.shape[1]
    request = jnp.sum(
        (slot_ids[:, None] >= request_ends).astype(jnp.int32), axis=1, dtype=jnp.int32
    )
    living = request < count_req
    matches = request[:, None] == jnp.arange(count_req, dtype=jnp.int32)[None, :]
    opening = jnp.sum(jnp.where(matches, starts, 0), axis=1, dtype=jnp.int32)
    position = jnp.where(living, slot_ids - opening, 0)
    segment = jnp.where(living, request, count_req + slot_ids)
    chosen = jnp.sum(jnp.where(matches, adapter_rows, 0), axis=1, dtype=jnp.int32)
    adapter_slot = jnp.where(living, chosen, -1)
    return (living, position, segment, adapter_slot)


def normalize(input_tokens, gain_vec):
    values = input_tokens.astype(jnp.float32)
    factor = lax.rsqrt(jnp.mean(values * values, axis=-1, keepdims=True) + EPSILON)
    return (values * factor * gain_vec).astype(jnp.bfloat16)


def adapter_select_mask(adapter_slot, adapter_column_count, adapter_rank_size):
    token_owner_request = jnp.arange(adapter_column_count, dtype=jnp.int32) // adapter_rank_size
    return (adapter_slot[:, None] == token_owner_request[None, :]).astype(jnp.float32)


def rotate(vectors, position):
    half_dim = vectors.shape[-1] // 2
    inverse = ROPE_THETA ** (-(jnp.arange(half_dim, dtype=jnp.float32) * (2.0 / vectors.shape[-1])))
    angles = position.astype(jnp.float32)[:, None] * inverse[None, :]
    cosine = jnp.cos(angles)[:, None, :]
    sine_part = jnp.sin(angles)[:, None, :]
    lower_half = vectors[..., :half_dim]
    upper_half = vectors[..., half_dim:]
    return jnp.concatenate(
        [
            lower_half * cosine - upper_half * sine_part,
            upper_half * cosine + lower_half * sine_part,
        ],
        axis=-1,
    )


def attend(queries, key_rows, value_rows, position, segment):
    key_heads = key_rows.shape[1]
    group_size = queries.shape[1] // key_heads
    token_count = queries.shape[0]
    grouped_queries = queries.reshape(token_count, key_heads, group_size, queries.shape[2])
    scores = jnp.einsum(
        "qkgd,skd->kgqs", grouped_queries, key_rows, preferred_element_type=jnp.float32
    ) * queries.shape[2] ** (-0.5)
    allowed = (segment[:, None] == segment[None, :]) & (position[None, :] <= position[:, None])
    allowed = allowed & (
        (position[:, None] - position[None, :] < WINDOW) | (position[None, :] < SINK)
    )
    scores = jnp.where(allowed[None, None], scores, -jnp.inf)
    highest = jnp.max(scores, axis=-1, keepdims=True)
    weights_raw = jnp.exp(scores - highest)
    weights = (weights_raw / jnp.sum(weights_raw, axis=-1, keepdims=True)).astype(jnp.bfloat16)
    blended = jnp.einsum("kgqs,skd->qkgd", weights, value_rows, preferred_element_type=jnp.float32)
    return blended.reshape(token_count, -1).astype(jnp.bfloat16)


def spread_rows(first_part, second_part):
    width = first_part.shape[1]
    joined = plane_gather(jnp.concatenate([first_part, second_part], axis=1), "mp")
    return joined[:, :width], joined[:, width:]


def sum_rows(term_fn, row_count):
    return plane_scatter(term_fn(jnp.int32(0), lax.axis_size("mp") * row_count), "mp", row_count)


def feed_forward(
    residual_stream,
    adapter_indicator,
    feed_norm_gain,
    adapter_down_gate_up,
    adapter_up_gate_up,
    gate_up_full,
    down_full,
    adapter_down_feed,
    adapter_up_feed,
):
    adapter_column_count = adapter_indicator.shape[1]
    model_width = residual_stream.shape[1]
    feed_input = normalize(residual_stream, feed_norm_gain)
    gate_terms = (
        jnp.dot(feed_input, adapter_down_gate_up, preferred_element_type=jnp.float32)
        * jnp.tile(adapter_indicator, (1, 2))
    ).astype(jnp.bfloat16)
    mlp_all, gate_adapter_ranks = spread_rows(feed_input, gate_terms)
    gate_activation = jnp.dot(
        mlp_all, gate_up_full[0], preferred_element_type=jnp.float32
    ) + jnp.dot(
        gate_adapter_ranks[:, :adapter_column_count],
        adapter_up_gate_up[0],
        preferred_element_type=jnp.float32,
    )
    up_projected = jnp.dot(mlp_all, gate_up_full[1], preferred_element_type=jnp.float32) + jnp.dot(
        gate_adapter_ranks[:, adapter_column_count:],
        adapter_up_gate_up[1],
        preferred_element_type=jnp.float32,
    )
    hidden_activation = (jax.nn.silu(gate_activation) * up_projected).astype(jnp.bfloat16)

    def down_term(first_row, row_count):
        projected_rows = lax.dot_general(
            hidden_activation,
            down_full,
            (((1,), (1,)), ((), ())),
            preferred_element_type=jnp.float32,
        )
        return jnp.concatenate(
            [
                projected_rows,
                jnp.dot(hidden_activation, adapter_down_feed, preferred_element_type=jnp.float32),
            ],
            axis=1,
        )

    summed = sum_rows(down_term, residual_stream.shape[0])
    down_adapter_ranks = (summed[:, model_width:] * adapter_indicator).astype(jnp.bfloat16)
    return (
        residual_stream.astype(jnp.float32)
        + summed[:, :model_width]
        + jnp.dot(down_adapter_ranks, adapter_up_feed, preferred_element_type=jnp.float32)
    )


def shards(
    states,
    lengths,
    request_adapters,
    attention_norm_gain,
    query_weight,
    key_weight,
    value_weight,
    output_weight,
    adapter_down_attention,
    adapter_up_query,
    adapter_up_key_value,
    adapter_down_output,
    adapter_up_output,
    feed_norm_gain,
    gate_up_weight,
    down_weight,
    adapter_down_gate_up,
    adapter_up_gate_up,
    adapter_down_feed,
    adapter_up_feed,
):
    mp_count = lax.axis_size("mp")
    group_index = lax.axis_index("req")
    mp_index = lax.axis_index("mp")
    slot_dev = states.shape[1]
    model_width = states.shape[3]
    adapter_column_count = adapter_up_output.shape[0]
    total_rows = slot_dev * mp_count
    gate_up_full, down_full = (
        lax.all_gather(gate_up_weight, "req", axis=1, tiled=True),
        lax.all_gather(down_weight, "req", axis=0, tiled=True),
    )
    local_rows = states.reshape(slot_dev, model_width)
    own_lengths = lax.dynamic_index_in_dim(lengths, group_index, 0, keepdims=False)
    own_adapters = lax.dynamic_index_in_dim(request_adapters, group_index, 0, keepdims=False)
    request_count = own_lengths.shape[0]
    local_slots = jnp.arange(slot_dev, dtype=jnp.int32) * mp_count + mp_index
    living, unused_pos, unused_seg, adapter_within = slot_info(
        jnp.broadcast_to(own_lengths[None, :], (slot_dev, request_count)),
        jnp.broadcast_to(own_adapters[None, :], (slot_dev, request_count)),
        local_slots,
    )
    indicator_within = adapter_select_mask(adapter_within, adapter_column_count, ADAPTER_RANK)
    states_all = plane_gather(local_rows, "mp")
    source_device, source_row = plane_rows(mp_index, slot_dev)
    gathered_slots = source_row * mp_count + source_device
    ignored, position_all, segment_all, adapter_all = slot_info(
        jnp.broadcast_to(own_lengths[None, :], (total_rows, request_count)),
        jnp.broadcast_to(own_adapters[None, :], (total_rows, request_count)),
        gathered_slots,
    )
    indicator_all = adapter_select_mask(adapter_all, adapter_column_count, ADAPTER_RANK)
    normed_all = normalize(states_all, attention_norm_gain)
    adapter_terms_all = (
        jnp.dot(normed_all, adapter_down_attention, preferred_element_type=jnp.float32)
        * jnp.tile(indicator_all, (1, 3))
    ).astype(jnp.bfloat16)
    query_projected = jnp.dot(
        normed_all, query_weight, preferred_element_type=jnp.float32
    ) + jnp.dot(
        adapter_terms_all[:, :adapter_column_count],
        adapter_up_query,
        preferred_element_type=jnp.float32,
    )
    key_projected = jnp.dot(normed_all, key_weight, preferred_element_type=jnp.float32) + jnp.dot(
        adapter_terms_all[:, adapter_column_count : 2 * adapter_column_count],
        adapter_up_key_value[0],
        preferred_element_type=jnp.float32,
    )
    value_projected = jnp.dot(
        normed_all, value_weight, preferred_element_type=jnp.float32
    ) + jnp.dot(
        adapter_terms_all[:, 2 * adapter_column_count :],
        adapter_up_key_value[1],
        preferred_element_type=jnp.float32,
    )
    kv_pair = jnp.stack([key_projected, value_projected])
    partner = align_partner_rows(
        from_partner(kv_pair.astype(jnp.bfloat16), "mp", 0), mp_index % 2, slot_dev
    ).astype(kv_pair.dtype)
    parity = mp_index % 2
    joined = jnp.where(
        parity == 0,
        jnp.concatenate([kv_pair, partner], axis=2),
        jnp.concatenate([partner, kv_pair], axis=2),
    )
    key_projected = joined[0]
    value_projected = joined[1]
    queries = rotate(query_projected.reshape(total_rows, -1, HEAD_SIZE), position_all).astype(
        jnp.bfloat16
    )
    key_rows = rotate(key_projected.reshape(total_rows, -1, HEAD_SIZE), position_all).astype(
        jnp.bfloat16
    )
    value_rows = value_projected.reshape(total_rows, -1, HEAD_SIZE).astype(jnp.bfloat16)
    attention_output = attend(queries, key_rows, value_rows, position_all, segment_all)

    def out_term(first_row, row_count):
        return jnp.concatenate(
            [
                jnp.dot(attention_output, output_weight, preferred_element_type=jnp.float32),
                jnp.dot(attention_output, adapter_down_output, preferred_element_type=jnp.float32),
            ],
            axis=1,
        )

    summed = sum_rows(out_term, slot_dev)
    output_adapter_ranks = (summed[:, model_width:] * indicator_within).astype(jnp.bfloat16)
    residual_stream = (
        local_rows.astype(jnp.float32)
        + summed[:, :model_width]
        + jnp.dot(output_adapter_ranks, adapter_up_output, preferred_element_type=jnp.float32)
    ).astype(jnp.bfloat16)
    layer_result = feed_forward(
        residual_stream,
        indicator_within,
        feed_norm_gain,
        adapter_down_gate_up,
        adapter_up_gate_up,
        gate_up_full,
        down_full,
        adapter_down_feed,
        adapter_up_feed,
    )
    finished = jnp.where(living[:, None], layer_result, jnp.zeros_like(layer_result)).astype(
        jnp.bfloat16
    )
    return finished.reshape(1, slot_dev, 1, model_width)


def solution(mesh):
    placed = (
        P("req", None, "mp", None),
        P(),
        P(),
        P(),
        P(None, "mp"),
        P(None, "mp"),
        P(None, "mp"),
        P("mp", None),
        P(),
        P(None, "mp"),
        P(None, None, "mp"),
        P("mp", None),
        P(),
        P(),
        P(None, "req", "mp"),
        P("req", "mp"),
        P(),
        P(None, None, "mp"),
        P("mp", None),
        P(),
    )
    return jax.shard_map(
        shards, mesh=mesh, in_specs=placed, out_specs=P("req", None, "mp", None), check_vma=False
    )
```

```python
import jax
import jax.numpy as jnp
from jax import lax
from jax.sharding import PartitionSpec as P

HEAD_SIZE = 128
ADAPTER_RANK = 16
WINDOW = 128
SINK = 4


EPSILON = 1e-05
ROPE_THETA = 1000000.0


RING = 4


def _ring_pairs(size, stride, step):
    pairs = []
    for i in range(size):
        low = i % stride
        pos = (i // stride) % RING
        high = i // (stride * RING)
        dst = (high * RING + (pos + step) % RING) * stride + low
        pairs.append((i, dst))
    return pairs


def _shift(x, axis, stride, step):
    return lax.ppermute(x, axis, _ring_pairs(lax.axis_size(axis), stride, step))


def ring_gather(block, axis, stride):
    half = block.shape[0] // 2
    from_minus = _shift(block, axis, stride, 1)
    from_plus = _shift(block, axis, stride, -1)
    first = _shift(from_plus[:half], axis, stride, -1)
    second = _shift(from_minus[half:], axis, stride, 1)
    across = jnp.concatenate([first, second], axis=0)
    return jnp.stack([block, from_plus, across, from_minus])


def ring_scatter(parts, axis, stride):
    half = parts.shape[1] // 2
    wire = jnp.bfloat16
    got_a = _shift(parts[2, :half].astype(wire), axis, stride, 1).astype(jnp.float32)
    got_b = _shift(parts[2, half:].astype(wire), axis, stride, -1).astype(jnp.float32)
    plus = parts[1].at[:half].add(got_a)
    minus = parts[3].at[half:].add(got_b)
    back_a = _shift(minus.astype(wire), axis, stride, -1).astype(jnp.float32)
    back_b = _shift(plus.astype(wire), axis, stride, 1).astype(jnp.float32)
    return parts[0] + back_a + back_b


def ring_gather_direct(block, axis, stride):
    from_minus = _shift(block, axis, stride, 1)
    from_plus = _shift(block, axis, stride, -1)
    across = _shift(block, axis, stride, 2)
    return jnp.stack([block, from_plus, across, from_minus])


def ring_scatter_direct(parts, axis, stride):
    wire = jnp.bfloat16
    got_minus = _shift(parts[1].astype(wire), axis, stride, 1)
    got_plus = _shift(parts[3].astype(wire), axis, stride, -1)
    got_across = _shift(parts[2].astype(wire), axis, stride, 2)
    return (
        parts[0]
        + got_minus.astype(jnp.float32)
        + got_plus.astype(jnp.float32)
        + got_across.astype(jnp.float32)
    )


def plane_gather(block, axis):
    rows, cols = block.shape
    half = rows // 2
    a1 = ring_gather_direct(block[:half], axis, 4)
    b1 = ring_gather_direct(block[half:], axis, 1)
    a2 = ring_gather(a1.reshape(RING * half, cols), axis, 1)
    b2 = ring_gather(b1.reshape(RING * half, cols), axis, 4)
    return jnp.concatenate([a2.reshape(-1, cols), b2.reshape(-1, cols)], axis=0)


def plane_rows(mp_index, rows):
    half = rows // 2
    px, py = mp_index // RING, mp_index % RING
    g = jnp.arange(16 * rows, dtype=jnp.int32)
    second = g >= 8 * rows
    h = g % half
    outer = (g % (8 * rows)) // (RING * half)
    inner = (g % (RING * half)) // half
    kx = jnp.where(second, outer, inner)
    ky = jnp.where(second, inner, outer)
    src = ((px + kx) % RING) * RING + (py + ky) % RING
    local = jnp.where(second, h + half, h)
    return src, local


def plane_scatter(parts, axis, rows):
    cols = parts.shape[1]
    half = rows // 2
    a = parts[: 8 * rows].reshape(RING, RING * half, cols)
    b = parts[8 * rows:].reshape(RING, RING * half, cols)
    a1 = ring_scatter(a, axis, 1).reshape(RING, half, cols)
    b1 = ring_scatter(b, axis, 4).reshape(RING, half, cols)
    a2 = ring_scatter_direct(a1, axis, 4)
    b2 = ring_scatter_direct(b1, axis, 1)
    return jnp.concatenate([a2, b2], axis=0)


def align_partner_rows(partner, parity, rows):
    half = rows // 2
    lead = partner.shape[:-2]
    cols = partner.shape[-1]
    first = partner[..., : 8 * rows, :].reshape(*lead, RING, RING * half, cols)
    second = partner[..., 8 * rows :, :].reshape(*lead, RING, RING, half, cols)
    axis_a = len(lead)
    axis_b = len(lead) + 1
    first = jnp.where(parity == 0, jnp.roll(first, 1, axis_a), jnp.roll(first, -1, axis_a))
    second = jnp.where(parity == 0, jnp.roll(second, 1, axis_b), jnp.roll(second, -1, axis_b))
    return jnp.concatenate(
        [first.reshape(*lead, 8 * rows, cols), second.reshape(*lead, 8 * rows, cols)], axis=-2
    )


def from_partner(shard, axis, stride):
    return lax.ppermute(shard, axis, [(i, i ^ 1 << stride) for i in range(lax.axis_size(axis))])


def slot_info(length_rows, adapter_rows, slot_ids):
    request_ends = jnp.cumsum(length_rows, axis=1, dtype=jnp.int32)
    starts = request_ends - length_rows
    count_req = length_rows.shape[1]
    request = jnp.sum(
        (slot_ids[:, None] >= request_ends).astype(jnp.int32), axis=1, dtype=jnp.int32
    )
    living = request < count_req
    matches = request[:, None] == jnp.arange(count_req, dtype=jnp.int32)[None, :]
    opening = jnp.sum(jnp.where(matches, starts, 0), axis=1, dtype=jnp.int32)
    position = jnp.where(living, slot_ids - opening, 0)
    segment = jnp.where(living, request, count_req + slot_ids)
    chosen = jnp.sum(jnp.where(matches, adapter_rows, 0), axis=1, dtype=jnp.int32)
    adapter_slot = jnp.where(living, chosen, -1)
    return (living, position, segment, adapter_slot)


def normalize(input_tokens, gain_vec):
    values = input_tokens.astype(jnp.float32)
    factor = lax.rsqrt(jnp.mean(values * values, axis=-1, keepdims=True) + EPSILON)
    return (values * factor * gain_vec).astype(jnp.bfloat16)


def adapter_select_mask(adapter_slot, adapter_column_count, adapter_rank_size):
    token_owner_request = jnp.arange(adapter_column_count, dtype=jnp.int32) // adapter_rank_size
    return (adapter_slot[:, None] == token_owner_request[None, :]).astype(jnp.float32)


def rotate(vectors, position):
    half_dim = vectors.shape[-1] // 2
    inverse = ROPE_THETA ** (-(jnp.arange(half_dim, dtype=jnp.float32) * (2.0 / vectors.shape[-1])))
    angles = position.astype(jnp.float32)[:, None] * inverse[None, :]
    cosine = jnp.cos(angles)[:, None, :]
    sine_part = jnp.sin(angles)[:, None, :]
    lower_half = vectors[..., :half_dim]
    upper_half = vectors[..., half_dim:]
    return jnp.concatenate(
        [
            lower_half * cosine - upper_half * sine_part,
            upper_half * cosine + lower_half * sine_part,
        ],
        axis=-1,
    )


def attend(queries, key_rows, value_rows, position, segment):
    key_heads = key_rows.shape[1]
    group_size = queries.shape[1] // key_heads
    token_count = queries.shape[0]
    grouped_queries = queries.reshape(token_count, key_heads, group_size, queries.shape[2])
    scores = jnp.einsum(
        "qkgd,skd->kgqs", grouped_queries, key_rows, preferred_element_type=jnp.float32
    ) * queries.shape[2] ** (-0.5)
    allowed = (segment[:, None] == segment[None, :]) & (position[None, :] <= position[:, None])
    allowed = allowed & (
        (position[:, None] - position[None, :] < WINDOW) | (position[None, :] < SINK)
    )
    scores = jnp.where(allowed[None, None], scores, -jnp.inf)
    highest = jnp.max(scores, axis=-1, keepdims=True)
    weights_raw = jnp.exp(scores - highest)
    weights = (weights_raw / jnp.sum(weights_raw, axis=-1, keepdims=True)).astype(jnp.bfloat16)
    blended = jnp.einsum("kgqs,skd->qkgd", weights, value_rows, preferred_element_type=jnp.float32)
    return blended.reshape(token_count, -1).astype(jnp.bfloat16)


def sum_rows(term_fn, row_count):
    return plane_scatter(term_fn(jnp.int32(0), lax.axis_size("mp") * row_count), "mp", row_count)


def feed_forward(
    residual_stream,
    adapter_indicator,
    feed_norm_gain,
    adapter_down_gate_up,
    adapter_up_gate_up,
    gate_up_full,
    down_full,
    adapter_down_feed,
    adapter_up_feed,
    indicator_all,
):
    adapter_column_count = adapter_indicator.shape[1]
    model_width = residual_stream.shape[1]
    mlp_all = normalize(plane_gather(residual_stream, "mp"), feed_norm_gain)
    gate_adapter_ranks = (
        jnp.dot(mlp_all, adapter_down_gate_up, preferred_element_type=jnp.float32)
        * jnp.tile(indicator_all, (1, 2))
    ).astype(jnp.bfloat16)
    gate_activation = jnp.dot(
        mlp_all, gate_up_full[0], preferred_element_type=jnp.float32
    ) + jnp.dot(
        gate_adapter_ranks[:, :adapter_column_count],
        adapter_up_gate_up[0],
        preferred_element_type=jnp.float32,
    )
    up_projected = jnp.dot(mlp_all, gate_up_full[1], preferred_element_type=jnp.float32) + jnp.dot(
        gate_adapter_ranks[:, adapter_column_count:],
        adapter_up_gate_up[1],
        preferred_element_type=jnp.float32,
    )
    hidden_activation = (jax.nn.silu(gate_activation) * up_projected).astype(jnp.bfloat16)

    def down_term(first_row, row_count):
        projected_rows = lax.dot_general(
            hidden_activation,
            down_full,
            (((1,), (1,)), ((), ())),
            preferred_element_type=jnp.float32,
        )
        return jnp.concatenate(
            [
                projected_rows,
                jnp.dot(hidden_activation, adapter_down_feed, preferred_element_type=jnp.float32),
            ],
            axis=1,
        )

    summed = sum_rows(down_term, residual_stream.shape[0])
    down_adapter_ranks = (summed[:, model_width:] * adapter_indicator).astype(jnp.bfloat16)
    return (
        residual_stream.astype(jnp.float32)
        + summed[:, :model_width]
        + jnp.dot(down_adapter_ranks, adapter_up_feed, preferred_element_type=jnp.float32)
    )


def shards(
    states,
    lengths,
    request_adapters,
    attention_norm_gain,
    query_weight,
    key_weight,
    value_weight,
    output_weight,
    adapter_down_attention,
    adapter_up_query,
    adapter_up_key_value,
    adapter_down_output,
    adapter_up_output,
    feed_norm_gain,
    gate_up_weight,
    down_weight,
    adapter_down_gate_up,
    adapter_up_gate_up,
    adapter_down_feed,
    adapter_up_feed,
):
    mp_count = lax.axis_size("mp")
    group_index = lax.axis_index("req")
    mp_index = lax.axis_index("mp")
    slot_dev = states.shape[1]
    model_width = states.shape[3]
    adapter_column_count = adapter_up_output.shape[0]
    total_rows = slot_dev * mp_count
    gate_up_full, down_full = (
        lax.all_gather(gate_up_weight, "req", axis=1, tiled=True),
        lax.all_gather(down_weight, "req", axis=0, tiled=True),
    )
    local_rows = states.reshape(slot_dev, model_width)
    own_lengths = lax.dynamic_index_in_dim(lengths, group_index, 0, keepdims=False)
    own_adapters = lax.dynamic_index_in_dim(request_adapters, group_index, 0, keepdims=False)
    request_count = own_lengths.shape[0]
    local_slots = jnp.arange(slot_dev, dtype=jnp.int32) * mp_count + mp_index
    living, unused_pos, unused_seg, adapter_within = slot_info(
        jnp.broadcast_to(own_lengths[None, :], (slot_dev, request_count)),
        jnp.broadcast_to(own_adapters[None, :], (slot_dev, request_count)),
        local_slots,
    )
    indicator_within = adapter_select_mask(adapter_within, adapter_column_count, ADAPTER_RANK)
    states_all = plane_gather(local_rows, "mp")
    source_device, source_row = plane_rows(mp_index, slot_dev)
    gathered_slots = source_row * mp_count + source_device
    ignored, position_all, segment_all, adapter_all = slot_info(
        jnp.broadcast_to(own_lengths[None, :], (total_rows, request_count)),
        jnp.broadcast_to(own_adapters[None, :], (total_rows, request_count)),
        gathered_slots,
    )
    indicator_all = adapter_select_mask(adapter_all, adapter_column_count, ADAPTER_RANK)
    normed_all = normalize(states_all, attention_norm_gain)
    adapter_terms_all = (
        jnp.dot(normed_all, adapter_down_attention, preferred_element_type=jnp.float32)
        * jnp.tile(indicator_all, (1, 3))
    ).astype(jnp.bfloat16)
    query_projected = jnp.dot(
        normed_all, query_weight, preferred_element_type=jnp.float32
    ) + jnp.dot(
        adapter_terms_all[:, :adapter_column_count],
        adapter_up_query,
        preferred_element_type=jnp.float32,
    )
    key_projected = jnp.dot(normed_all, key_weight, preferred_element_type=jnp.float32) + jnp.dot(
        adapter_terms_all[:, adapter_column_count : 2 * adapter_column_count],
        adapter_up_key_value[0],
        preferred_element_type=jnp.float32,
    )
    value_projected = jnp.dot(
        normed_all, value_weight, preferred_element_type=jnp.float32
    ) + jnp.dot(
        adapter_terms_all[:, 2 * adapter_column_count :],
        adapter_up_key_value[1],
        preferred_element_type=jnp.float32,
    )
    kv_pair = jnp.stack([key_projected, value_projected])
    partner = align_partner_rows(
        from_partner(kv_pair.astype(jnp.bfloat16), "mp", 0), mp_index % 2, slot_dev
    ).astype(kv_pair.dtype)
    parity = mp_index % 2
    joined = jnp.where(
        parity == 0,
        jnp.concatenate([kv_pair, partner], axis=2),
        jnp.concatenate([partner, kv_pair], axis=2),
    )
    key_projected = joined[0]
    value_projected = joined[1]
    queries = rotate(query_projected.reshape(total_rows, -1, HEAD_SIZE), position_all).astype(
        jnp.bfloat16
    )
    key_rows = rotate(key_projected.reshape(total_rows, -1, HEAD_SIZE), position_all).astype(
        jnp.bfloat16
    )
    value_rows = value_projected.reshape(total_rows, -1, HEAD_SIZE).astype(jnp.bfloat16)
    attention_output = attend(queries, key_rows, value_rows, position_all, segment_all)

    def out_term(first_row, row_count):
        return jnp.concatenate(
            [
                jnp.dot(attention_output, output_weight, preferred_element_type=jnp.float32),
                jnp.dot(attention_output, adapter_down_output, preferred_element_type=jnp.float32),
            ],
            axis=1,
        )

    summed = sum_rows(out_term, slot_dev)
    output_adapter_ranks = (summed[:, model_width:] * indicator_within).astype(jnp.bfloat16)
    residual_stream = (
        local_rows.astype(jnp.float32)
        + summed[:, :model_width]
        + jnp.dot(output_adapter_ranks, adapter_up_output, preferred_element_type=jnp.float32)
    ).astype(jnp.bfloat16)
    layer_result = feed_forward(
        residual_stream,
        indicator_within,
        feed_norm_gain,
        adapter_down_gate_up,
        adapter_up_gate_up,
        gate_up_full,
        down_full,
        adapter_down_feed,
        adapter_up_feed,
        indicator_all,
    )
    finished = jnp.where(living[:, None], layer_result, jnp.zeros_like(layer_result)).astype(
        jnp.bfloat16
    )
    return finished.reshape(1, slot_dev, 1, model_width)


def solution(mesh):
    placed = (
        P("req", None, "mp", None),
        P(),
        P(),
        P(),
        P(None, "mp"),
        P(None, "mp"),
        P(None, "mp"),
        P("mp", None),
        P(),
        P(None, "mp"),
        P(None, None, "mp"),
        P("mp", None),
        P(),
        P(),
        P(None, "req", "mp"),
        P("req", "mp"),
        P(),
        P(None, None, "mp"),
        P("mp", None),
        P(),
    )
    return jax.shard_map(
        shards, mesh=mesh, in_specs=placed, out_specs=P("req", None, "mp", None), check_vma=False
    )
```

```python
import jax
import jax.numpy as jnp
from jax import lax
from jax.sharding import PartitionSpec as P

HEAD_SIZE = 128
ADAPTER_RANK = 16
WINDOW = 128
SINK = 4


EPSILON = 1e-05
ROPE_THETA = 1000000.0


RING = 4


def _ring_pairs(size, stride, step):
    pairs = []
    for i in range(size):
        low = i % stride
        pos = (i // stride) % RING
        high = i // (stride * RING)
        dst = (high * RING + (pos + step) % RING) * stride + low
        pairs.append((i, dst))
    return pairs


def _shift(x, axis, stride, step):
    return lax.ppermute(x, axis, _ring_pairs(lax.axis_size(axis), stride, step))


def ring_gather(block, axis, stride):
    half = block.shape[0] // 2
    from_minus = _shift(block, axis, stride, 1)
    from_plus = _shift(block, axis, stride, -1)
    first = _shift(from_plus[:half], axis, stride, -1)
    second = _shift(from_minus[half:], axis, stride, 1)
    across = jnp.concatenate([first, second], axis=0)
    return jnp.stack([block, from_plus, across, from_minus])


def ring_scatter(parts, axis, stride):
    half = parts.shape[1] // 2
    wire = jnp.bfloat16
    got_a = _shift(parts[2, :half].astype(wire), axis, stride, 1).astype(jnp.float32)
    got_b = _shift(parts[2, half:].astype(wire), axis, stride, -1).astype(jnp.float32)
    plus = parts[1].at[:half].add(got_a)
    minus = parts[3].at[half:].add(got_b)
    back_a = _shift(minus.astype(wire), axis, stride, -1).astype(jnp.float32)
    back_b = _shift(plus.astype(wire), axis, stride, 1).astype(jnp.float32)
    return parts[0] + back_a + back_b


def ring_gather_direct(block, axis, stride):
    from_minus = _shift(block, axis, stride, 1)
    from_plus = _shift(block, axis, stride, -1)
    across = _shift(block, axis, stride, 2)
    return jnp.stack([block, from_plus, across, from_minus])


def ring_scatter_direct(parts, axis, stride):
    wire = jnp.bfloat16
    got_minus = _shift(parts[1].astype(wire), axis, stride, 1)
    got_plus = _shift(parts[3].astype(wire), axis, stride, -1)
    got_across = _shift(parts[2].astype(wire), axis, stride, 2)
    return (
        parts[0]
        + got_minus.astype(jnp.float32)
        + got_plus.astype(jnp.float32)
        + got_across.astype(jnp.float32)
    )


def plane_gather(block, axis):
    rows, cols = block.shape
    half = rows // 2
    a1 = ring_gather_direct(block[:half], axis, 4)
    b1 = ring_gather_direct(block[half:], axis, 1)
    a2 = ring_gather(a1.reshape(RING * half, cols), axis, 1)
    b2 = ring_gather(b1.reshape(RING * half, cols), axis, 4)
    return jnp.concatenate([a2.reshape(-1, cols), b2.reshape(-1, cols)], axis=0)


def plane_rows(mp_index, rows):
    half = rows // 2
    px, py = mp_index // RING, mp_index % RING
    g = jnp.arange(16 * rows, dtype=jnp.int32)
    second = g >= 8 * rows
    h = g % half
    outer = (g % (8 * rows)) // (RING * half)
    inner = (g % (RING * half)) // half
    kx = jnp.where(second, outer, inner)
    ky = jnp.where(second, inner, outer)
    src = ((px + kx) % RING) * RING + (py + ky) % RING
    local = jnp.where(second, h + half, h)
    return src, local


def plane_scatter(parts, axis, rows):
    cols = parts.shape[1]
    half = rows // 2
    a = parts[: 8 * rows].reshape(RING, RING * half, cols)
    b = parts[8 * rows:].reshape(RING, RING * half, cols)
    a1 = ring_scatter(a, axis, 1).reshape(RING, half, cols)
    b1 = ring_scatter(b, axis, 4).reshape(RING, half, cols)
    a2 = ring_scatter_direct(a1, axis, 4)
    b2 = ring_scatter_direct(b1, axis, 1)
    return jnp.concatenate([a2, b2], axis=0)


def align_partner_rows(partner, parity, rows):
    half = rows // 2
    lead = partner.shape[:-2]
    cols = partner.shape[-1]
    first = partner[..., : 8 * rows, :].reshape(*lead, RING, RING * half, cols)
    second = partner[..., 8 * rows :, :].reshape(*lead, RING, RING, half, cols)
    axis_a = len(lead)
    axis_b = len(lead) + 1
    first = jnp.where(parity == 0, jnp.roll(first, 1, axis_a), jnp.roll(first, -1, axis_a))
    second = jnp.where(parity == 0, jnp.roll(second, 1, axis_b), jnp.roll(second, -1, axis_b))
    return jnp.concatenate(
        [first.reshape(*lead, 8 * rows, cols), second.reshape(*lead, 8 * rows, cols)], axis=-2
    )


def from_partner(shard, axis, stride):
    return lax.ppermute(shard, axis, [(i, i ^ 1 << stride) for i in range(lax.axis_size(axis))])


def slot_info(length_rows, adapter_rows, slot_ids):
    request_ends = jnp.cumsum(length_rows, axis=1, dtype=jnp.int32)
    starts = request_ends - length_rows
    count_req = length_rows.shape[1]
    request = jnp.sum(
        (slot_ids[:, None] >= request_ends).astype(jnp.int32), axis=1, dtype=jnp.int32
    )
    living = request < count_req
    matches = request[:, None] == jnp.arange(count_req, dtype=jnp.int32)[None, :]
    opening = jnp.sum(jnp.where(matches, starts, 0), axis=1, dtype=jnp.int32)
    position = jnp.where(living, slot_ids - opening, 0)
    segment = jnp.where(living, request, count_req + slot_ids)
    chosen = jnp.sum(jnp.where(matches, adapter_rows, 0), axis=1, dtype=jnp.int32)
    adapter_slot = jnp.where(living, chosen, -1)
    return (living, position, segment, adapter_slot)


def normalize(input_tokens, gain_vec):
    values = input_tokens.astype(jnp.float32)
    factor = lax.rsqrt(jnp.mean(values * values, axis=-1, keepdims=True) + EPSILON)
    return (values * factor * gain_vec).astype(jnp.bfloat16)


def adapter_select_mask(adapter_slot, adapter_column_count, adapter_rank_size):
    token_owner_request = jnp.arange(adapter_column_count, dtype=jnp.int32) // adapter_rank_size
    return (adapter_slot[:, None] == token_owner_request[None, :]).astype(jnp.float32)


def rotate(vectors, position):
    half_dim = vectors.shape[-1] // 2
    inverse = ROPE_THETA ** (-(jnp.arange(half_dim, dtype=jnp.float32) * (2.0 / vectors.shape[-1])))
    angles = position.astype(jnp.float32)[:, None] * inverse[None, :]
    cosine = jnp.cos(angles)[:, None, :]
    sine_part = jnp.sin(angles)[:, None, :]
    lower_half = vectors[..., :half_dim]
    upper_half = vectors[..., half_dim:]
    return jnp.concatenate(
        [
            lower_half * cosine - upper_half * sine_part,
            upper_half * cosine + lower_half * sine_part,
        ],
        axis=-1,
    )


def attend(queries, key_rows, value_rows, position, segment):
    key_heads = key_rows.shape[1]
    group_size = queries.shape[1] // key_heads
    token_count = queries.shape[0]
    grouped_queries = queries.reshape(token_count, key_heads, group_size, queries.shape[2])
    scores = jnp.einsum(
        "qkgd,skd->kgqs", grouped_queries, key_rows, preferred_element_type=jnp.float32
    ) * queries.shape[2] ** (-0.5)
    allowed = (segment[:, None] == segment[None, :]) & (position[None, :] <= position[:, None])
    allowed = allowed & (
        (position[:, None] - position[None, :] < WINDOW) | (position[None, :] < SINK)
    )
    scores = jnp.where(allowed[None, None], scores, -jnp.inf)
    highest = jnp.max(scores, axis=-1, keepdims=True)
    weights_raw = jnp.exp(scores - highest)
    weights = (weights_raw / jnp.sum(weights_raw, axis=-1, keepdims=True)).astype(jnp.bfloat16)
    blended = jnp.einsum("kgqs,skd->qkgd", weights, value_rows, preferred_element_type=jnp.float32)
    return blended.reshape(token_count, -1).astype(jnp.bfloat16)


def spread_rows(first_part, second_part):
    width = first_part.shape[1]
    joined = plane_gather(jnp.concatenate([first_part, second_part], axis=1), "mp")
    return joined[:, :width], joined[:, width:]


def sum_rows(term_fn, row_count):
    return plane_scatter(term_fn(jnp.int32(0), lax.axis_size("mp") * row_count), "mp", row_count)


def feed_forward(
    residual_stream,
    adapter_indicator,
    feed_norm_gain,
    adapter_down_gate_up,
    adapter_up_gate_up,
    gate_up_full,
    down_full,
    adapter_down_feed,
    adapter_up_feed,
):
    adapter_column_count = adapter_indicator.shape[1]
    model_width = residual_stream.shape[1]
    feed_input = normalize(residual_stream, feed_norm_gain)
    gate_terms = (
        jnp.dot(feed_input, adapter_down_gate_up, preferred_element_type=jnp.float32)
        * jnp.tile(adapter_indicator, (1, 2))
    ).astype(jnp.bfloat16)
    mlp_all, gate_adapter_ranks = spread_rows(feed_input, gate_terms)
    gate_activation = jnp.dot(
        mlp_all, gate_up_full[0], preferred_element_type=jnp.float32
    ) + jnp.dot(
        gate_adapter_ranks[:, :adapter_column_count],
        adapter_up_gate_up[0],
        preferred_element_type=jnp.float32,
    )
    up_projected = jnp.dot(mlp_all, gate_up_full[1], preferred_element_type=jnp.float32) + jnp.dot(
        gate_adapter_ranks[:, adapter_column_count:],
        adapter_up_gate_up[1],
        preferred_element_type=jnp.float32,
    )
    hidden_activation = (jax.nn.silu(gate_activation) * up_projected).astype(jnp.bfloat16)

    def down_term(first_row, row_count):
        projected_rows = lax.dot_general(
            hidden_activation,
            down_full,
            (((1,), (1,)), ((), ())),
            preferred_element_type=jnp.float32,
        )
        return jnp.concatenate(
            [
                projected_rows,
                jnp.dot(hidden_activation, adapter_down_feed, preferred_element_type=jnp.float32),
            ],
            axis=1,
        )

    summed = sum_rows(down_term, residual_stream.shape[0])
    down_adapter_ranks = (summed[:, model_width:] * adapter_indicator).astype(jnp.bfloat16)
    return (
        residual_stream.astype(jnp.float32)
        + summed[:, :model_width]
        + jnp.dot(down_adapter_ranks, adapter_up_feed, preferred_element_type=jnp.float32)
    )


def shards(
    states,
    lengths,
    request_adapters,
    attention_norm_gain,
    query_weight,
    key_weight,
    value_weight,
    output_weight,
    adapter_down_attention,
    adapter_up_query,
    adapter_up_key_value,
    adapter_down_output,
    adapter_up_output,
    feed_norm_gain,
    gate_up_weight,
    down_weight,
    adapter_down_gate_up,
    adapter_up_gate_up,
    adapter_down_feed,
    adapter_up_feed,
):
    mp_count = lax.axis_size("mp")
    group_index = lax.axis_index("req")
    mp_index = lax.axis_index("mp")
    slot_dev = states.shape[1]
    model_width = states.shape[3]
    adapter_column_count = adapter_up_output.shape[0]
    total_rows = slot_dev * mp_count
    gate_up_full, down_full = (
        lax.all_gather(gate_up_weight, "req", axis=1, tiled=True),
        lax.all_gather(down_weight, "req", axis=0, tiled=True),
    )
    local_rows = states.reshape(slot_dev, model_width)
    own_lengths = lax.dynamic_index_in_dim(lengths, group_index, 0, keepdims=False)
    own_adapters = lax.dynamic_index_in_dim(request_adapters, group_index, 0, keepdims=False)
    request_count = own_lengths.shape[0]
    local_slots = jnp.arange(slot_dev, dtype=jnp.int32) * mp_count + mp_index
    living, unused_pos, unused_seg, adapter_within = slot_info(
        jnp.broadcast_to(own_lengths[None, :], (slot_dev, request_count)),
        jnp.broadcast_to(own_adapters[None, :], (slot_dev, request_count)),
        local_slots,
    )
    indicator_within = adapter_select_mask(adapter_within, adapter_column_count, ADAPTER_RANK)
    states_all = plane_gather(local_rows, "mp")
    source_device, source_row = plane_rows(mp_index, slot_dev)
    gathered_slots = source_row * mp_count + source_device
    ignored, position_all, segment_all, adapter_all = slot_info(
        jnp.broadcast_to(own_lengths[None, :], (total_rows, request_count)),
        jnp.broadcast_to(own_adapters[None, :], (total_rows, request_count)),
        gathered_slots,
    )
    indicator_all = adapter_select_mask(adapter_all, adapter_column_count, ADAPTER_RANK)
    normed_all = normalize(states_all, attention_norm_gain)
    widths = [
        query_weight.shape[1],
        key_weight.shape[1],
        value_weight.shape[1],
        adapter_down_attention.shape[1],
    ]
    merged = jnp.dot(
        normed_all,
        jnp.concatenate([query_weight, key_weight, value_weight, adapter_down_attention], axis=1),
        preferred_element_type=jnp.float32,
    )
    edges = [sum(widths[:i]) for i in range(len(widths) + 1)]
    query_base, key_base, value_base, adapter_base = (
        merged[:, edges[i] : edges[i + 1]] for i in range(len(widths))
    )
    adapter_terms_all = (adapter_base * jnp.tile(indicator_all, (1, 3))).astype(jnp.bfloat16)
    query_projected = query_base + jnp.dot(
        adapter_terms_all[:, :adapter_column_count],
        adapter_up_query,
        preferred_element_type=jnp.float32,
    )
    key_projected = key_base + jnp.dot(
        adapter_terms_all[:, adapter_column_count : 2 * adapter_column_count],
        adapter_up_key_value[0],
        preferred_element_type=jnp.float32,
    )
    value_projected = value_base + jnp.dot(
        adapter_terms_all[:, 2 * adapter_column_count :],
        adapter_up_key_value[1],
        preferred_element_type=jnp.float32,
    )
    kv_pair = jnp.stack([key_projected, value_projected])
    partner = align_partner_rows(
        from_partner(kv_pair.astype(jnp.bfloat16), "mp", 0), mp_index % 2, slot_dev
    ).astype(kv_pair.dtype)
    parity = mp_index % 2
    joined = jnp.where(
        parity == 0,
        jnp.concatenate([kv_pair, partner], axis=2),
        jnp.concatenate([partner, kv_pair], axis=2),
    )
    key_projected = joined[0]
    value_projected = joined[1]
    queries = rotate(query_projected.reshape(total_rows, -1, HEAD_SIZE), position_all).astype(
        jnp.bfloat16
    )
    key_rows = rotate(key_projected.reshape(total_rows, -1, HEAD_SIZE), position_all).astype(
        jnp.bfloat16
    )
    value_rows = value_projected.reshape(total_rows, -1, HEAD_SIZE).astype(jnp.bfloat16)
    attention_output = attend(queries, key_rows, value_rows, position_all, segment_all)

    def out_term(first_row, row_count):
        return jnp.concatenate(
            [
                jnp.dot(attention_output, output_weight, preferred_element_type=jnp.float32),
                jnp.dot(attention_output, adapter_down_output, preferred_element_type=jnp.float32),
            ],
            axis=1,
        )

    summed = sum_rows(out_term, slot_dev)
    output_adapter_ranks = (summed[:, model_width:] * indicator_within).astype(jnp.bfloat16)
    residual_stream = (
        local_rows.astype(jnp.float32)
        + summed[:, :model_width]
        + jnp.dot(output_adapter_ranks, adapter_up_output, preferred_element_type=jnp.float32)
    ).astype(jnp.bfloat16)
    layer_result = feed_forward(
        residual_stream,
        indicator_within,
        feed_norm_gain,
        adapter_down_gate_up,
        adapter_up_gate_up,
        gate_up_full,
        down_full,
        adapter_down_feed,
        adapter_up_feed,
    )
    finished = jnp.where(living[:, None], layer_result, jnp.zeros_like(layer_result)).astype(
        jnp.bfloat16
    )
    return finished.reshape(1, slot_dev, 1, model_width)


def solution(mesh):
    placed = (
        P("req", None, "mp", None),
        P(),
        P(),
        P(),
        P(None, "mp"),
        P(None, "mp"),
        P(None, "mp"),
        P("mp", None),
        P(),
        P(None, "mp"),
        P(None, None, "mp"),
        P("mp", None),
        P(),
        P(),
        P(None, "req", "mp"),
        P("req", "mp"),
        P(),
        P(None, None, "mp"),
        P("mp", None),
        P(),
    )
    return jax.shard_map(
        shards, mesh=mesh, in_specs=placed, out_specs=P("req", None, "mp", None), check_vma=False
    )
```

```python
import jax
import jax.numpy as jnp
from jax import lax
from jax.sharding import PartitionSpec as P

HEAD_SIZE = 128
ADAPTER_RANK = 16
WINDOW = 128
SINK = 4


EPSILON = 1e-05
ROPE_THETA = 1000000.0


RING = 4


def _ring_pairs(size, stride, step):
    pairs = []
    for i in range(size):
        low = i % stride
        pos = (i // stride) % RING
        high = i // (stride * RING)
        dst = (high * RING + (pos + step) % RING) * stride + low
        pairs.append((i, dst))
    return pairs


def _shift(x, axis, stride, step):
    return lax.ppermute(x, axis, _ring_pairs(lax.axis_size(axis), stride, step))


def ring_gather(block, axis, stride):
    half = block.shape[0] // 2
    from_minus = _shift(block, axis, stride, 1)
    from_plus = _shift(block, axis, stride, -1)
    first = _shift(from_plus[:half], axis, stride, -1)
    second = _shift(from_minus[half:], axis, stride, 1)
    across = jnp.concatenate([first, second], axis=0)
    return jnp.stack([block, from_plus, across, from_minus])


def ring_scatter(parts, axis, stride):
    half = parts.shape[1] // 2
    wire = jnp.bfloat16
    got_a = _shift(parts[2, :half].astype(wire), axis, stride, 1).astype(jnp.float32)
    got_b = _shift(parts[2, half:].astype(wire), axis, stride, -1).astype(jnp.float32)
    plus = parts[1].at[:half].add(got_a)
    minus = parts[3].at[half:].add(got_b)
    back_a = _shift(minus.astype(wire), axis, stride, -1).astype(jnp.float32)
    back_b = _shift(plus.astype(wire), axis, stride, 1).astype(jnp.float32)
    return parts[0] + back_a + back_b


def ring_gather_direct(block, axis, stride):
    from_minus = _shift(block, axis, stride, 1)
    from_plus = _shift(block, axis, stride, -1)
    across = _shift(block, axis, stride, 2)
    return jnp.stack([block, from_plus, across, from_minus])


def ring_scatter_direct(parts, axis, stride):
    wire = jnp.bfloat16
    got_minus = _shift(parts[1].astype(wire), axis, stride, 1)
    got_plus = _shift(parts[3].astype(wire), axis, stride, -1)
    got_across = _shift(parts[2].astype(wire), axis, stride, 2)
    return (
        parts[0]
        + got_minus.astype(jnp.float32)
        + got_plus.astype(jnp.float32)
        + got_across.astype(jnp.float32)
    )


def plane_gather(block, axis):
    rows, cols = block.shape
    half = rows // 2
    a1 = ring_gather_direct(block[:half], axis, 4)
    b1 = ring_gather_direct(block[half:], axis, 1)
    a2 = ring_gather(a1.reshape(RING * half, cols), axis, 1)
    b2 = ring_gather(b1.reshape(RING * half, cols), axis, 4)
    return jnp.concatenate([a2.reshape(-1, cols), b2.reshape(-1, cols)], axis=0)


def plane_rows(mp_index, rows):
    half = rows // 2
    px, py = mp_index // RING, mp_index % RING
    g = jnp.arange(16 * rows, dtype=jnp.int32)
    second = g >= 8 * rows
    h = g % half
    outer = (g % (8 * rows)) // (RING * half)
    inner = (g % (RING * half)) // half
    kx = jnp.where(second, outer, inner)
    ky = jnp.where(second, inner, outer)
    src = ((px + kx) % RING) * RING + (py + ky) % RING
    local = jnp.where(second, h + half, h)
    return src, local


def plane_scatter(parts, axis, rows):
    cols = parts.shape[1]
    half = rows // 2
    a = parts[: 8 * rows].reshape(RING, RING * half, cols)
    b = parts[8 * rows:].reshape(RING, RING * half, cols)
    a1 = ring_scatter(a, axis, 1).reshape(RING, half, cols)
    b1 = ring_scatter(b, axis, 4).reshape(RING, half, cols)
    a2 = ring_scatter_direct(a1, axis, 4)
    b2 = ring_scatter_direct(b1, axis, 1)
    return jnp.concatenate([a2, b2], axis=0)


def align_partner_rows(partner, parity, rows):
    half = rows // 2
    lead = partner.shape[:-2]
    cols = partner.shape[-1]
    first = partner[..., : 8 * rows, :].reshape(*lead, RING, RING * half, cols)
    second = partner[..., 8 * rows :, :].reshape(*lead, RING, RING, half, cols)
    axis_a = len(lead)
    axis_b = len(lead) + 1
    first = jnp.where(parity == 0, jnp.roll(first, 1, axis_a), jnp.roll(first, -1, axis_a))
    second = jnp.where(parity == 0, jnp.roll(second, 1, axis_b), jnp.roll(second, -1, axis_b))
    return jnp.concatenate(
        [first.reshape(*lead, 8 * rows, cols), second.reshape(*lead, 8 * rows, cols)], axis=-2
    )


def from_partner(shard, axis, stride):
    return lax.ppermute(shard, axis, [(i, i ^ 1 << stride) for i in range(lax.axis_size(axis))])


def slot_info(length_rows, adapter_rows, slot_ids):
    request_ends = jnp.cumsum(length_rows, axis=1, dtype=jnp.int32)
    starts = request_ends - length_rows
    count_req = length_rows.shape[1]
    request = jnp.sum(
        (slot_ids[:, None] >= request_ends).astype(jnp.int32), axis=1, dtype=jnp.int32
    )
    living = request < count_req
    matches = request[:, None] == jnp.arange(count_req, dtype=jnp.int32)[None, :]
    opening = jnp.sum(jnp.where(matches, starts, 0), axis=1, dtype=jnp.int32)
    position = jnp.where(living, slot_ids - opening, 0)
    segment = jnp.where(living, request, count_req + slot_ids)
    chosen = jnp.sum(jnp.where(matches, adapter_rows, 0), axis=1, dtype=jnp.int32)
    adapter_slot = jnp.where(living, chosen, -1)
    return (living, position, segment, adapter_slot)


def normalize(input_tokens, gain_vec):
    values = input_tokens.astype(jnp.float32)
    factor = lax.rsqrt(jnp.mean(values * values, axis=-1, keepdims=True) + EPSILON)
    return (values * factor * gain_vec).astype(jnp.bfloat16)


def adapter_select_mask(adapter_slot, adapter_column_count, adapter_rank_size):
    token_owner_request = jnp.arange(adapter_column_count, dtype=jnp.int32) // adapter_rank_size
    return (adapter_slot[:, None] == token_owner_request[None, :]).astype(jnp.float32)


def rotate(vectors, position):
    half_dim = vectors.shape[-1] // 2
    inverse = ROPE_THETA ** (-(jnp.arange(half_dim, dtype=jnp.float32) * (2.0 / vectors.shape[-1])))
    angles = position.astype(jnp.float32)[:, None] * inverse[None, :]
    cosine = jnp.cos(angles)[:, None, :]
    sine_part = jnp.sin(angles)[:, None, :]
    lower_half = vectors[..., :half_dim]
    upper_half = vectors[..., half_dim:]
    return jnp.concatenate(
        [
            lower_half * cosine - upper_half * sine_part,
            upper_half * cosine + lower_half * sine_part,
        ],
        axis=-1,
    )


def attend(queries, key_rows, value_rows, position, segment):
    key_heads = key_rows.shape[1]
    group_size = queries.shape[1] // key_heads
    token_count = queries.shape[0]
    grouped_queries = queries.reshape(token_count, key_heads, group_size, queries.shape[2])
    scores = jnp.einsum(
        "qkgd,skd->kgqs", grouped_queries, key_rows, preferred_element_type=jnp.float32
    ) * queries.shape[2] ** (-0.5)
    allowed = (segment[:, None] == segment[None, :]) & (position[None, :] <= position[:, None])
    allowed = allowed & (
        (position[:, None] - position[None, :] < WINDOW) | (position[None, :] < SINK)
    )
    scores = jnp.where(allowed[None, None], scores, -jnp.inf)
    highest = jnp.max(scores, axis=-1, keepdims=True)
    weights_raw = jnp.exp(scores - highest)
    weights = (weights_raw / jnp.sum(weights_raw, axis=-1, keepdims=True)).astype(jnp.bfloat16)
    blended = jnp.einsum("kgqs,skd->qkgd", weights, value_rows, preferred_element_type=jnp.float32)
    return blended.reshape(token_count, -1).astype(jnp.bfloat16)


def spread_rows(first_part, second_part):
    width = first_part.shape[1]
    joined = plane_gather(jnp.concatenate([first_part, second_part], axis=1), "mp")
    return joined[:, :width], joined[:, width:]


def sum_rows(term_fn, row_count):
    return plane_scatter(term_fn(jnp.int32(0), lax.axis_size("mp") * row_count), "mp", row_count)


def feed_forward(
    residual_stream,
    adapter_indicator,
    feed_norm_gain,
    adapter_down_gate_up,
    adapter_up_gate_up,
    gate_up_full,
    down_full,
    adapter_down_feed,
    adapter_up_feed,
):
    adapter_column_count = adapter_indicator.shape[1]
    model_width = residual_stream.shape[1]
    feed_input = normalize(residual_stream, feed_norm_gain)
    gate_terms = (
        jnp.dot(feed_input, adapter_down_gate_up, preferred_element_type=jnp.float32)
        * jnp.tile(adapter_indicator, (1, 2))
    ).astype(jnp.bfloat16)
    mlp_all, gate_adapter_ranks = spread_rows(feed_input, gate_terms)
    hidden_width = gate_up_full.shape[1] // 2
    both = jnp.dot(mlp_all, gate_up_full, preferred_element_type=jnp.float32)
    gate_activation = both[:, :hidden_width] + jnp.dot(
        gate_adapter_ranks[:, :adapter_column_count],
        adapter_up_gate_up[0],
        preferred_element_type=jnp.float32,
    )
    up_projected = both[:, hidden_width:] + jnp.dot(
        gate_adapter_ranks[:, adapter_column_count:],
        adapter_up_gate_up[1],
        preferred_element_type=jnp.float32,
    )
    hidden_activation = (jax.nn.silu(gate_activation) * up_projected).astype(jnp.bfloat16)

    def down_term(first_row, row_count):
        return jnp.dot(
            hidden_activation,
            jnp.concatenate([down_full, adapter_down_feed], axis=1),
            preferred_element_type=jnp.float32,
        )

    summed = sum_rows(down_term, residual_stream.shape[0])
    down_adapter_ranks = (summed[:, model_width:] * adapter_indicator).astype(jnp.bfloat16)
    return (
        residual_stream.astype(jnp.float32)
        + summed[:, :model_width]
        + jnp.dot(down_adapter_ranks, adapter_up_feed, preferred_element_type=jnp.float32)
    )


def shards(
    states,
    lengths,
    request_adapters,
    attention_norm_gain,
    query_weight,
    key_weight,
    value_weight,
    output_weight,
    adapter_down_attention,
    adapter_up_query,
    adapter_up_key_value,
    adapter_down_output,
    adapter_up_output,
    feed_norm_gain,
    gate_up_weight,
    down_weight,
    adapter_down_gate_up,
    adapter_up_gate_up,
    adapter_down_feed,
    adapter_up_feed,
):
    mp_count = lax.axis_size("mp")
    group_index = lax.axis_index("req")
    mp_index = lax.axis_index("mp")
    slot_dev = states.shape[1]
    model_width = states.shape[3]
    adapter_column_count = adapter_up_output.shape[0]
    total_rows = slot_dev * mp_count
    gate_up_local = jnp.transpose(gate_up_weight, (1, 0, 2)).reshape(gate_up_weight.shape[1], -1)
    gate_up_full, down_full = (
        lax.all_gather(gate_up_local, "req", axis=0, tiled=True),
        lax.all_gather(jnp.transpose(down_weight), "req", axis=1, tiled=True),
    )
    local_rows = states.reshape(slot_dev, model_width)
    own_lengths = lax.dynamic_index_in_dim(lengths, group_index, 0, keepdims=False)
    own_adapters = lax.dynamic_index_in_dim(request_adapters, group_index, 0, keepdims=False)
    request_count = own_lengths.shape[0]
    local_slots = jnp.arange(slot_dev, dtype=jnp.int32) * mp_count + mp_index
    living, unused_pos, unused_seg, adapter_within = slot_info(
        jnp.broadcast_to(own_lengths[None, :], (slot_dev, request_count)),
        jnp.broadcast_to(own_adapters[None, :], (slot_dev, request_count)),
        local_slots,
    )
    indicator_within = adapter_select_mask(adapter_within, adapter_column_count, ADAPTER_RANK)
    states_all = plane_gather(local_rows, "mp")
    source_device, source_row = plane_rows(mp_index, slot_dev)
    gathered_slots = source_row * mp_count + source_device
    ignored, position_all, segment_all, adapter_all = slot_info(
        jnp.broadcast_to(own_lengths[None, :], (total_rows, request_count)),
        jnp.broadcast_to(own_adapters[None, :], (total_rows, request_count)),
        gathered_slots,
    )
    indicator_all = adapter_select_mask(adapter_all, adapter_column_count, ADAPTER_RANK)
    normed_all = normalize(states_all, attention_norm_gain)
    widths = [
        query_weight.shape[1],
        key_weight.shape[1],
        value_weight.shape[1],
        adapter_down_attention.shape[1],
    ]
    merged = jnp.dot(
        normed_all,
        jnp.concatenate([query_weight, key_weight, value_weight, adapter_down_attention], axis=1),
        preferred_element_type=jnp.float32,
    )
    edges = [sum(widths[:i]) for i in range(len(widths) + 1)]
    query_base, key_base, value_base, adapter_base = (
        merged[:, edges[i] : edges[i + 1]] for i in range(len(widths))
    )
    adapter_terms_all = (adapter_base * jnp.tile(indicator_all, (1, 3))).astype(jnp.bfloat16)
    query_projected = query_base + jnp.dot(
        adapter_terms_all[:, :adapter_column_count],
        adapter_up_query,
        preferred_element_type=jnp.float32,
    )
    key_projected = key_base + jnp.dot(
        adapter_terms_all[:, adapter_column_count : 2 * adapter_column_count],
        adapter_up_key_value[0],
        preferred_element_type=jnp.float32,
    )
    value_projected = value_base + jnp.dot(
        adapter_terms_all[:, 2 * adapter_column_count :],
        adapter_up_key_value[1],
        preferred_element_type=jnp.float32,
    )
    kv_pair = jnp.stack([key_projected, value_projected])
    partner = align_partner_rows(
        from_partner(kv_pair.astype(jnp.bfloat16), "mp", 0), mp_index % 2, slot_dev
    ).astype(kv_pair.dtype)
    parity = mp_index % 2
    joined = jnp.where(
        parity == 0,
        jnp.concatenate([kv_pair, partner], axis=2),
        jnp.concatenate([partner, kv_pair], axis=2),
    )
    key_projected = joined[0]
    value_projected = joined[1]
    queries = rotate(query_projected.reshape(total_rows, -1, HEAD_SIZE), position_all).astype(
        jnp.bfloat16
    )
    key_rows = rotate(key_projected.reshape(total_rows, -1, HEAD_SIZE), position_all).astype(
        jnp.bfloat16
    )
    value_rows = value_projected.reshape(total_rows, -1, HEAD_SIZE).astype(jnp.bfloat16)
    attention_output = attend(queries, key_rows, value_rows, position_all, segment_all)

    def out_term(first_row, row_count):
        return jnp.dot(
            attention_output,
            jnp.concatenate([output_weight, adapter_down_output], axis=1),
            preferred_element_type=jnp.float32,
        )

    summed = sum_rows(out_term, slot_dev)
    output_adapter_ranks = (summed[:, model_width:] * indicator_within).astype(jnp.bfloat16)
    residual_stream = (
        local_rows.astype(jnp.float32)
        + summed[:, :model_width]
        + jnp.dot(output_adapter_ranks, adapter_up_output, preferred_element_type=jnp.float32)
    ).astype(jnp.bfloat16)
    layer_result = feed_forward(
        residual_stream,
        indicator_within,
        feed_norm_gain,
        adapter_down_gate_up,
        adapter_up_gate_up,
        gate_up_full,
        down_full,
        adapter_down_feed,
        adapter_up_feed,
    )
    finished = jnp.where(living[:, None], layer_result, jnp.zeros_like(layer_result)).astype(
        jnp.bfloat16
    )
    return finished.reshape(1, slot_dev, 1, model_width)


def solution(mesh):
    placed = (
        P("req", None, "mp", None),
        P(),
        P(),
        P(),
        P(None, "mp"),
        P(None, "mp"),
        P(None, "mp"),
        P("mp", None),
        P(),
        P(None, "mp"),
        P(None, None, "mp"),
        P("mp", None),
        P(),
        P(),
        P(None, "req", "mp"),
        P("req", "mp"),
        P(),
        P(None, None, "mp"),
        P("mp", None),
        P(),
    )
    return jax.shard_map(
        shards, mesh=mesh, in_specs=placed, out_specs=P("req", None, "mp", None), check_vma=False
    )
```

```python
import jax
import jax.numpy as jnp
from jax import lax
from jax.sharding import PartitionSpec as P

HEAD_SIZE = 128
ADAPTER_RANK = 16
WINDOW = 128
SINK = 4


EPSILON = 1e-05
ROPE_THETA = 1000000.0


RING = 4


def _ring_pairs(size, stride, step):
    pairs = []
    for i in range(size):
        low = i % stride
        pos = (i // stride) % RING
        high = i // (stride * RING)
        dst = (high * RING + (pos + step) % RING) * stride + low
        pairs.append((i, dst))
    return pairs


def _shift(x, axis, stride, step):
    return lax.ppermute(x, axis, _ring_pairs(lax.axis_size(axis), stride, step))


def ring_gather(block, axis, stride):
    half = block.shape[0] // 2
    from_minus = _shift(block, axis, stride, 1)
    from_plus = _shift(block, axis, stride, -1)
    first = _shift(from_plus[:half], axis, stride, -1)
    second = _shift(from_minus[half:], axis, stride, 1)
    across = jnp.concatenate([first, second], axis=0)
    return jnp.stack([block, from_plus, across, from_minus])


def ring_scatter(parts, axis, stride):
    half = parts.shape[1] // 2
    wire = jnp.bfloat16
    got_a = _shift(parts[2, :half].astype(wire), axis, stride, 1).astype(jnp.float32)
    got_b = _shift(parts[2, half:].astype(wire), axis, stride, -1).astype(jnp.float32)
    plus = parts[1].at[:half].add(got_a)
    minus = parts[3].at[half:].add(got_b)
    back_a = _shift(minus.astype(wire), axis, stride, -1).astype(jnp.float32)
    back_b = _shift(plus.astype(wire), axis, stride, 1).astype(jnp.float32)
    return parts[0] + back_a + back_b


def ring_gather_direct(block, axis, stride):
    from_minus = _shift(block, axis, stride, 1)
    from_plus = _shift(block, axis, stride, -1)
    across = _shift(block, axis, stride, 2)
    return jnp.stack([block, from_plus, across, from_minus])


def ring_scatter_direct(parts, axis, stride):
    wire = jnp.bfloat16
    got_minus = _shift(parts[1].astype(wire), axis, stride, 1)
    got_plus = _shift(parts[3].astype(wire), axis, stride, -1)
    got_across = _shift(parts[2].astype(wire), axis, stride, 2)
    return (
        parts[0]
        + got_minus.astype(jnp.float32)
        + got_plus.astype(jnp.float32)
        + got_across.astype(jnp.float32)
    )


def plane_gather(block, axis):
    rows, cols = block.shape
    half = rows // 2
    a1 = ring_gather_direct(block[:half], axis, 4)
    b1 = ring_gather_direct(block[half:], axis, 1)
    a2 = ring_gather(a1.reshape(RING * half, cols), axis, 1)
    b2 = ring_gather(b1.reshape(RING * half, cols), axis, 4)
    return jnp.concatenate([a2.reshape(-1, cols), b2.reshape(-1, cols)], axis=0)


def plane_rows(mp_index, rows):
    half = rows // 2
    px, py = mp_index // RING, mp_index % RING
    g = jnp.arange(16 * rows, dtype=jnp.int32)
    second = g >= 8 * rows
    h = g % half
    outer = (g % (8 * rows)) // (RING * half)
    inner = (g % (RING * half)) // half
    kx = jnp.where(second, outer, inner)
    ky = jnp.where(second, inner, outer)
    src = ((px + kx) % RING) * RING + (py + ky) % RING
    local = jnp.where(second, h + half, h)
    return src, local


def plane_scatter(parts, axis, rows):
    cols = parts.shape[1]
    half = rows // 2
    a = parts[: 8 * rows].reshape(RING, RING * half, cols)
    b = parts[8 * rows:].reshape(RING, RING * half, cols)
    a1 = ring_scatter(a, axis, 1).reshape(RING, half, cols)
    b1 = ring_scatter(b, axis, 4).reshape(RING, half, cols)
    a2 = ring_scatter_direct(a1, axis, 4)
    b2 = ring_scatter_direct(b1, axis, 1)
    return jnp.concatenate([a2, b2], axis=0)


def align_partner_rows(partner, parity, rows):
    half = rows // 2
    lead = partner.shape[:-2]
    cols = partner.shape[-1]
    first = partner[..., : 8 * rows, :].reshape(*lead, RING, RING * half, cols)
    second = partner[..., 8 * rows :, :].reshape(*lead, RING, RING, half, cols)
    axis_a = len(lead)
    axis_b = len(lead) + 1
    first = jnp.where(parity == 0, jnp.roll(first, 1, axis_a), jnp.roll(first, -1, axis_a))
    second = jnp.where(parity == 0, jnp.roll(second, 1, axis_b), jnp.roll(second, -1, axis_b))
    return jnp.concatenate(
        [first.reshape(*lead, 8 * rows, cols), second.reshape(*lead, 8 * rows, cols)], axis=-2
    )


def from_partner(shard, axis, stride):
    return lax.ppermute(shard, axis, [(i, i ^ 1 << stride) for i in range(lax.axis_size(axis))])


def slot_info(length_rows, adapter_rows, slot_ids):
    request_ends = jnp.cumsum(length_rows, axis=1, dtype=jnp.int32)
    starts = request_ends - length_rows
    count_req = length_rows.shape[1]
    request = jnp.sum(
        (slot_ids[:, None] >= request_ends).astype(jnp.int32), axis=1, dtype=jnp.int32
    )
    living = request < count_req
    matches = request[:, None] == jnp.arange(count_req, dtype=jnp.int32)[None, :]
    opening = jnp.sum(jnp.where(matches, starts, 0), axis=1, dtype=jnp.int32)
    position = jnp.where(living, slot_ids - opening, 0)
    segment = jnp.where(living, request, count_req + slot_ids)
    chosen = jnp.sum(jnp.where(matches, adapter_rows, 0), axis=1, dtype=jnp.int32)
    adapter_slot = jnp.where(living, chosen, -1)
    return (living, position, segment, adapter_slot)


def normalize(input_tokens, gain_vec):
    values = input_tokens.astype(jnp.float32)
    factor = lax.rsqrt(jnp.mean(values * values, axis=-1, keepdims=True) + EPSILON)
    return (values * factor * gain_vec).astype(jnp.bfloat16)


def adapter_select_mask(adapter_slot, adapter_column_count, adapter_rank_size):
    token_owner_request = jnp.arange(adapter_column_count, dtype=jnp.int32) // adapter_rank_size
    return (adapter_slot[:, None] == token_owner_request[None, :]).astype(jnp.float32)


def rotate(vectors, position):
    half_dim = vectors.shape[-1] // 2
    inverse = ROPE_THETA ** (-(jnp.arange(half_dim, dtype=jnp.float32) * (2.0 / vectors.shape[-1])))
    angles = position.astype(jnp.float32)[:, None] * inverse[None, :]
    cosine = jnp.cos(angles)[:, None, :]
    sine_part = jnp.sin(angles)[:, None, :]
    lower_half = vectors[..., :half_dim]
    upper_half = vectors[..., half_dim:]
    return jnp.concatenate(
        [
            lower_half * cosine - upper_half * sine_part,
            upper_half * cosine + lower_half * sine_part,
        ],
        axis=-1,
    )


def attend(queries, key_rows, value_rows, position, segment):
    key_heads = key_rows.shape[1]
    group_size = queries.shape[1] // key_heads
    token_count = queries.shape[0]
    grouped_queries = queries.reshape(token_count, key_heads, group_size, queries.shape[2])
    scores = jnp.einsum(
        "qkgd,skd->kgqs", grouped_queries, key_rows, preferred_element_type=jnp.float32
    ) * queries.shape[2] ** (-0.5)
    allowed = (segment[:, None] == segment[None, :]) & (position[None, :] <= position[:, None])
    allowed = allowed & (
        (position[:, None] - position[None, :] < WINDOW) | (position[None, :] < SINK)
    )
    scores = jnp.where(allowed[None, None], scores, -jnp.inf)
    highest = jnp.max(scores, axis=-1, keepdims=True)
    weights_raw = jnp.exp(scores - highest)
    weights = (weights_raw / jnp.sum(weights_raw, axis=-1, keepdims=True)).astype(jnp.bfloat16)
    blended = jnp.einsum("kgqs,skd->qkgd", weights, value_rows, preferred_element_type=jnp.float32)
    return blended.reshape(token_count, -1).astype(jnp.bfloat16)


def spread_rows(first_part, second_part):
    width = first_part.shape[1]
    joined = plane_gather(jnp.concatenate([first_part, second_part], axis=1), "mp")
    return joined[:, :width], joined[:, width:]


def sum_rows(term_fn, row_count):
    return plane_scatter(term_fn(jnp.int32(0), lax.axis_size("mp") * row_count), "mp", row_count)


def feed_forward(
    residual_stream,
    adapter_indicator,
    feed_norm_gain,
    adapter_down_gate_up,
    adapter_up_gate_up,
    gate_up_full,
    down_full,
    adapter_down_feed,
    adapter_up_feed,
):
    adapter_column_count = adapter_indicator.shape[1]
    model_width = residual_stream.shape[1]
    feed_input = normalize(residual_stream, feed_norm_gain)
    gate_terms = (
        jnp.dot(feed_input, adapter_down_gate_up, preferred_element_type=jnp.float32)
        * jnp.tile(adapter_indicator, (1, 2))
    ).astype(jnp.bfloat16)
    mlp_all, gate_adapter_ranks = spread_rows(feed_input, gate_terms)
    gate_activation = jnp.dot(
        mlp_all, gate_up_full[0], preferred_element_type=jnp.float32
    ) + jnp.dot(
        gate_adapter_ranks[:, :adapter_column_count],
        adapter_up_gate_up[0],
        preferred_element_type=jnp.float32,
    )
    up_projected = jnp.dot(mlp_all, gate_up_full[1], preferred_element_type=jnp.float32) + jnp.dot(
        gate_adapter_ranks[:, adapter_column_count:],
        adapter_up_gate_up[1],
        preferred_element_type=jnp.float32,
    )
    hidden_activation = (jax.nn.silu(gate_activation) * up_projected).astype(jnp.bfloat16)

    def down_term(first_row, row_count):
        projected_rows = lax.dot_general(
            hidden_activation,
            down_full,
            (((1,), (1,)), ((), ())),
            preferred_element_type=jnp.float32,
        )
        return jnp.concatenate(
            [
                projected_rows,
                jnp.dot(hidden_activation, adapter_down_feed, preferred_element_type=jnp.float32),
            ],
            axis=1,
        )

    summed = sum_rows(down_term, residual_stream.shape[0])
    down_adapter_ranks = (summed[:, model_width:] * adapter_indicator).astype(jnp.bfloat16)
    return (
        residual_stream.astype(jnp.float32)
        + summed[:, :model_width]
        + jnp.dot(down_adapter_ranks, adapter_up_feed, preferred_element_type=jnp.float32)
    )


def shards(
    states,
    lengths,
    request_adapters,
    attention_norm_gain,
    query_weight,
    key_weight,
    value_weight,
    output_weight,
    adapter_down_attention,
    adapter_up_query,
    adapter_up_key_value,
    adapter_down_output,
    adapter_up_output,
    feed_norm_gain,
    gate_up_weight,
    down_weight,
    adapter_down_gate_up,
    adapter_up_gate_up,
    adapter_down_feed,
    adapter_up_feed,
):
    mp_count = lax.axis_size("mp")
    group_index = lax.axis_index("req")
    mp_index = lax.axis_index("mp")
    slot_dev = states.shape[1]
    model_width = states.shape[3]
    adapter_column_count = adapter_up_output.shape[0]
    total_rows = slot_dev * mp_count
    gate_up_full, down_full = (
        lax.all_gather(gate_up_weight, "req", axis=1, tiled=True),
        lax.all_gather(down_weight, "req", axis=0, tiled=True),
    )
    local_rows = states.reshape(slot_dev, model_width)
    own_lengths = lax.dynamic_index_in_dim(lengths, group_index, 0, keepdims=False)
    own_adapters = lax.dynamic_index_in_dim(request_adapters, group_index, 0, keepdims=False)
    request_count = own_lengths.shape[0]
    local_slots = jnp.arange(slot_dev, dtype=jnp.int32) * mp_count + mp_index
    living, unused_pos, unused_seg, adapter_within = slot_info(
        jnp.broadcast_to(own_lengths[None, :], (slot_dev, request_count)),
        jnp.broadcast_to(own_adapters[None, :], (slot_dev, request_count)),
        local_slots,
    )
    indicator_within = adapter_select_mask(adapter_within, adapter_column_count, ADAPTER_RANK)
    states_all = plane_gather(local_rows, "mp")
    source_device, source_row = plane_rows(mp_index, slot_dev)
    gathered_slots = source_row * mp_count + source_device
    ignored, position_all, segment_all, adapter_all = slot_info(
        jnp.broadcast_to(own_lengths[None, :], (total_rows, request_count)),
        jnp.broadcast_to(own_adapters[None, :], (total_rows, request_count)),
        gathered_slots,
    )
    indicator_all = adapter_select_mask(adapter_all, adapter_column_count, ADAPTER_RANK)
    normed_all = normalize(states_all, attention_norm_gain)
    query_width = query_weight.shape[1]
    merged = jnp.dot(
        normed_all,
        jnp.concatenate([query_weight, adapter_down_attention], axis=1),
        preferred_element_type=jnp.float32,
    )
    query_base = merged[:, :query_width]
    key_base = jnp.dot(normed_all, key_weight, preferred_element_type=jnp.float32)
    value_base = jnp.dot(normed_all, value_weight, preferred_element_type=jnp.float32)
    adapter_base = merged[:, query_width:]
    adapter_terms_all = (adapter_base * jnp.tile(indicator_all, (1, 3))).astype(jnp.bfloat16)
    query_projected = query_base + jnp.dot(
        adapter_terms_all[:, :adapter_column_count],
        adapter_up_query,
        preferred_element_type=jnp.float32,
    )
    key_projected = key_base + jnp.dot(
        adapter_terms_all[:, adapter_column_count : 2 * adapter_column_count],
        adapter_up_key_value[0],
        preferred_element_type=jnp.float32,
    )
    value_projected = value_base + jnp.dot(
        adapter_terms_all[:, 2 * adapter_column_count :],
        adapter_up_key_value[1],
        preferred_element_type=jnp.float32,
    )
    kv_pair = jnp.stack([key_projected, value_projected])
    partner = align_partner_rows(
        from_partner(kv_pair.astype(jnp.bfloat16), "mp", 0), mp_index % 2, slot_dev
    ).astype(kv_pair.dtype)
    parity = mp_index % 2
    joined = jnp.where(
        parity == 0,
        jnp.concatenate([kv_pair, partner], axis=2),
        jnp.concatenate([partner, kv_pair], axis=2),
    )
    key_projected = joined[0]
    value_projected = joined[1]
    queries = rotate(query_projected.reshape(total_rows, -1, HEAD_SIZE), position_all).astype(
        jnp.bfloat16
    )
    key_rows = rotate(key_projected.reshape(total_rows, -1, HEAD_SIZE), position_all).astype(
        jnp.bfloat16
    )
    value_rows = value_projected.reshape(total_rows, -1, HEAD_SIZE).astype(jnp.bfloat16)
    attention_output = attend(queries, key_rows, value_rows, position_all, segment_all)

    def out_term(first_row, row_count):
        return jnp.concatenate(
            [
                jnp.dot(attention_output, output_weight, preferred_element_type=jnp.float32),
                jnp.dot(attention_output, adapter_down_output, preferred_element_type=jnp.float32),
            ],
            axis=1,
        )

    summed = sum_rows(out_term, slot_dev)
    output_adapter_ranks = (summed[:, model_width:] * indicator_within).astype(jnp.bfloat16)
    residual_stream = (
        local_rows.astype(jnp.float32)
        + summed[:, :model_width]
        + jnp.dot(output_adapter_ranks, adapter_up_output, preferred_element_type=jnp.float32)
    ).astype(jnp.bfloat16)
    layer_result = feed_forward(
        residual_stream,
        indicator_within,
        feed_norm_gain,
        adapter_down_gate_up,
        adapter_up_gate_up,
        gate_up_full,
        down_full,
        adapter_down_feed,
        adapter_up_feed,
    )
    finished = jnp.where(living[:, None], layer_result, jnp.zeros_like(layer_result)).astype(
        jnp.bfloat16
    )
    return finished.reshape(1, slot_dev, 1, model_width)


def solution(mesh):
    placed = (
        P("req", None, "mp", None),
        P(),
        P(),
        P(),
        P(None, "mp"),
        P(None, "mp"),
        P(None, "mp"),
        P("mp", None),
        P(),
        P(None, "mp"),
        P(None, None, "mp"),
        P("mp", None),
        P(),
        P(),
        P(None, "req", "mp"),
        P("req", "mp"),
        P(),
        P(None, None, "mp"),
        P("mp", None),
        P(),
    )
    return jax.shard_map(
        shards, mesh=mesh, in_specs=placed, out_specs=P("req", None, "mp", None), check_vma=False
    )
```

```python
import jax
import jax.numpy as jnp
from jax import lax
from jax.sharding import PartitionSpec as P

HEAD_SIZE = 128
ADAPTER_RANK = 16
WINDOW = 128
SINK = 4


EPSILON = 1e-05
ROPE_THETA = 1000000.0


RING = 4


def _ring_pairs(size, stride, step):
    pairs = []
    for i in range(size):
        low = i % stride
        pos = (i // stride) % RING
        high = i // (stride * RING)
        dst = (high * RING + (pos + step) % RING) * stride + low
        pairs.append((i, dst))
    return pairs


def _shift(x, axis, stride, step):
    return lax.ppermute(x, axis, _ring_pairs(lax.axis_size(axis), stride, step))


def ring_gather(block, axis, stride):
    half = block.shape[0] // 2
    from_minus = _shift(block, axis, stride, 1)
    from_plus = _shift(block, axis, stride, -1)
    first = _shift(from_plus[:half], axis, stride, -1)
    second = _shift(from_minus[half:], axis, stride, 1)
    across = jnp.concatenate([first, second], axis=0)
    return jnp.stack([block, from_plus, across, from_minus])


def ring_scatter(parts, axis, stride):
    half = parts.shape[1] // 2
    wire = jnp.bfloat16
    got_a = _shift(parts[2, :half].astype(wire), axis, stride, 1).astype(jnp.float32)
    got_b = _shift(parts[2, half:].astype(wire), axis, stride, -1).astype(jnp.float32)
    plus = parts[1].at[:half].add(got_a)
    minus = parts[3].at[half:].add(got_b)
    back_a = _shift(minus.astype(wire), axis, stride, -1).astype(jnp.float32)
    back_b = _shift(plus.astype(wire), axis, stride, 1).astype(jnp.float32)
    return parts[0] + back_a + back_b


def ring_gather_direct(block, axis, stride):
    from_minus = _shift(block, axis, stride, 1)
    from_plus = _shift(block, axis, stride, -1)
    across = _shift(block, axis, stride, 2)
    return jnp.stack([block, from_plus, across, from_minus])


def ring_scatter_direct(parts, axis, stride):
    wire = jnp.bfloat16
    got_minus = _shift(parts[1].astype(wire), axis, stride, 1)
    got_plus = _shift(parts[3].astype(wire), axis, stride, -1)
    got_across = _shift(parts[2].astype(wire), axis, stride, 2)
    return (
        parts[0]
        + got_minus.astype(jnp.float32)
        + got_plus.astype(jnp.float32)
        + got_across.astype(jnp.float32)
    )


def plane_gather(block, axis):
    rows, cols = block.shape
    half = rows // 2
    a1 = ring_gather_direct(block[:half], axis, 4)
    b1 = ring_gather_direct(block[half:], axis, 1)
    a2 = ring_gather(a1.reshape(RING * half, cols), axis, 1)
    b2 = ring_gather(b1.reshape(RING * half, cols), axis, 4)
    return jnp.concatenate([a2.reshape(-1, cols), b2.reshape(-1, cols)], axis=0)


def plane_rows(mp_index, rows):
    half = rows // 2
    px, py = mp_index // RING, mp_index % RING
    g = jnp.arange(16 * rows, dtype=jnp.int32)
    second = g >= 8 * rows
    h = g % half
    outer = (g % (8 * rows)) // (RING * half)
    inner = (g % (RING * half)) // half
    kx = jnp.where(second, outer, inner)
    ky = jnp.where(second, inner, outer)
    src = ((px + kx) % RING) * RING + (py + ky) % RING
    local = jnp.where(second, h + half, h)
    return src, local


def plane_scatter(parts, axis, rows):
    cols = parts.shape[1]
    half = rows // 2
    a = parts[: 8 * rows].reshape(RING, RING * half, cols)
    b = parts[8 * rows:].reshape(RING, RING * half, cols)
    a1 = ring_scatter(a, axis, 1).reshape(RING, half, cols)
    b1 = ring_scatter(b, axis, 4).reshape(RING, half, cols)
    a2 = ring_scatter_direct(a1, axis, 4)
    b2 = ring_scatter_direct(b1, axis, 1)
    return jnp.concatenate([a2, b2], axis=0)


def align_partner_rows(partner, parity, rows):
    half = rows // 2
    lead = partner.shape[:-2]
    cols = partner.shape[-1]
    first = partner[..., : 8 * rows, :].reshape(*lead, RING, RING * half, cols)
    second = partner[..., 8 * rows :, :].reshape(*lead, RING, RING, half, cols)
    axis_a = len(lead)
    axis_b = len(lead) + 1
    first = jnp.where(parity == 0, jnp.roll(first, 1, axis_a), jnp.roll(first, -1, axis_a))
    second = jnp.where(parity == 0, jnp.roll(second, 1, axis_b), jnp.roll(second, -1, axis_b))
    return jnp.concatenate(
        [first.reshape(*lead, 8 * rows, cols), second.reshape(*lead, 8 * rows, cols)], axis=-2
    )


def from_partner(shard, axis, stride):
    return lax.ppermute(shard, axis, [(i, i ^ 1 << stride) for i in range(lax.axis_size(axis))])


def slot_info(length_rows, adapter_rows, slot_ids):
    request_ends = jnp.cumsum(length_rows, axis=1, dtype=jnp.int32)
    starts = request_ends - length_rows
    count_req = length_rows.shape[1]
    request = jnp.sum(
        (slot_ids[:, None] >= request_ends).astype(jnp.int32), axis=1, dtype=jnp.int32
    )
    living = request < count_req
    matches = request[:, None] == jnp.arange(count_req, dtype=jnp.int32)[None, :]
    opening = jnp.sum(jnp.where(matches, starts, 0), axis=1, dtype=jnp.int32)
    position = jnp.where(living, slot_ids - opening, 0)
    segment = jnp.where(living, request, count_req + slot_ids)
    chosen = jnp.sum(jnp.where(matches, adapter_rows, 0), axis=1, dtype=jnp.int32)
    adapter_slot = jnp.where(living, chosen, -1)
    return (living, position, segment, adapter_slot)


def normalize(input_tokens, gain_vec):
    values = input_tokens.astype(jnp.float32)
    factor = lax.rsqrt(jnp.mean(values * values, axis=-1, keepdims=True) + EPSILON)
    return (values * factor * gain_vec).astype(jnp.bfloat16)


def adapter_select_mask(adapter_slot, adapter_column_count, adapter_rank_size):
    token_owner_request = jnp.arange(adapter_column_count, dtype=jnp.int32) // adapter_rank_size
    return (adapter_slot[:, None] == token_owner_request[None, :]).astype(jnp.float32)


def rotate(vectors, position):
    half_dim = vectors.shape[-1] // 2
    inverse = ROPE_THETA ** (-(jnp.arange(half_dim, dtype=jnp.float32) * (2.0 / vectors.shape[-1])))
    angles = position.astype(jnp.float32)[:, None] * inverse[None, :]
    cosine = jnp.cos(angles)[:, None, :]
    sine_part = jnp.sin(angles)[:, None, :]
    lower_half = vectors[..., :half_dim]
    upper_half = vectors[..., half_dim:]
    return jnp.concatenate(
        [
            lower_half * cosine - upper_half * sine_part,
            upper_half * cosine + lower_half * sine_part,
        ],
        axis=-1,
    )


def attend(queries, key_rows, value_rows, position, segment):
    key_heads = key_rows.shape[1]
    group_size = queries.shape[1] // key_heads
    token_count = queries.shape[0]
    grouped_queries = queries.reshape(token_count, key_heads, group_size, queries.shape[2])
    scores = jnp.einsum(
        "qkgd,skd->kgqs", grouped_queries, key_rows, preferred_element_type=jnp.float32
    ) * queries.shape[2] ** (-0.5)
    allowed = (segment[:, None] == segment[None, :]) & (position[None, :] <= position[:, None])
    allowed = allowed & (
        (position[:, None] - position[None, :] < WINDOW) | (position[None, :] < SINK)
    )
    scores = jnp.where(allowed[None, None], scores, -jnp.inf)
    highest = jnp.max(scores, axis=-1, keepdims=True)
    weights_raw = jnp.exp(scores - highest)
    weights = (weights_raw / jnp.sum(weights_raw, axis=-1, keepdims=True)).astype(jnp.bfloat16)
    blended = jnp.einsum("kgqs,skd->qkgd", weights, value_rows, preferred_element_type=jnp.float32)
    return blended.reshape(token_count, -1).astype(jnp.bfloat16)


def spread_rows(first_part, second_part):
    width = first_part.shape[1]
    joined = plane_gather(jnp.concatenate([first_part, second_part], axis=1), "mp")
    return joined[:, :width], joined[:, width:]


def sum_rows(term_fn, row_count):
    return plane_scatter(term_fn(jnp.int32(0), lax.axis_size("mp") * row_count), "mp", row_count)


def feed_forward(
    residual_stream,
    adapter_indicator,
    feed_norm_gain,
    adapter_down_gate_up,
    adapter_up_gate_up,
    gate_up_full,
    down_full,
    adapter_down_feed,
    adapter_up_feed,
):
    adapter_column_count = adapter_indicator.shape[1]
    model_width = residual_stream.shape[1]
    feed_input = normalize(residual_stream, feed_norm_gain)
    gate_terms = (
        jnp.dot(feed_input, adapter_down_gate_up, preferred_element_type=jnp.float32)
        * jnp.tile(adapter_indicator, (1, 2))
    ).astype(jnp.bfloat16)
    mlp_all, gate_adapter_ranks = spread_rows(feed_input, gate_terms)
    gate_activation = jnp.dot(
        mlp_all, gate_up_full[0], preferred_element_type=jnp.float32
    ) + jnp.dot(
        gate_adapter_ranks[:, :adapter_column_count],
        adapter_up_gate_up[0],
        preferred_element_type=jnp.float32,
    )
    up_projected = jnp.dot(mlp_all, gate_up_full[1], preferred_element_type=jnp.float32) + jnp.dot(
        gate_adapter_ranks[:, adapter_column_count:],
        adapter_up_gate_up[1],
        preferred_element_type=jnp.float32,
    )
    hidden_activation = (jax.nn.silu(gate_activation) * up_projected).astype(jnp.bfloat16)

    def down_term(first_row, row_count):
        projected_rows = lax.dot_general(
            hidden_activation,
            down_full,
            (((1,), (1,)), ((), ())),
            preferred_element_type=jnp.float32,
        )
        return jnp.concatenate(
            [
                projected_rows,
                jnp.dot(hidden_activation, adapter_down_feed, preferred_element_type=jnp.float32),
            ],
            axis=1,
        )

    summed = sum_rows(down_term, residual_stream.shape[0])
    down_adapter_ranks = (summed[:, model_width:] * adapter_indicator).astype(jnp.bfloat16)
    return (
        residual_stream.astype(jnp.float32)
        + summed[:, :model_width]
        + jnp.dot(down_adapter_ranks, adapter_up_feed, preferred_element_type=jnp.float32)
    )


def shards(
    states,
    lengths,
    request_adapters,
    attention_norm_gain,
    query_weight,
    key_weight,
    value_weight,
    output_weight,
    adapter_down_attention,
    adapter_up_query,
    adapter_up_key_value,
    adapter_down_output,
    adapter_up_output,
    feed_norm_gain,
    gate_up_weight,
    down_weight,
    adapter_down_gate_up,
    adapter_up_gate_up,
    adapter_down_feed,
    adapter_up_feed,
):
    mp_count = lax.axis_size("mp")
    group_index = lax.axis_index("req")
    mp_index = lax.axis_index("mp")
    slot_dev = states.shape[1]
    model_width = states.shape[3]
    adapter_column_count = adapter_up_output.shape[0]
    total_rows = slot_dev * mp_count
    gate_up_full, down_full = (
        lax.all_gather(gate_up_weight, "req", axis=1, tiled=True),
        lax.all_gather(down_weight, "req", axis=0, tiled=True),
    )
    local_rows = states.reshape(slot_dev, model_width)
    own_lengths = lax.dynamic_index_in_dim(lengths, group_index, 0, keepdims=False)
    own_adapters = lax.dynamic_index_in_dim(request_adapters, group_index, 0, keepdims=False)
    request_count = own_lengths.shape[0]
    local_slots = jnp.arange(slot_dev, dtype=jnp.int32) * mp_count + mp_index
    living, unused_pos, unused_seg, adapter_within = slot_info(
        jnp.broadcast_to(own_lengths[None, :], (slot_dev, request_count)),
        jnp.broadcast_to(own_adapters[None, :], (slot_dev, request_count)),
        local_slots,
    )
    indicator_within = adapter_select_mask(adapter_within, adapter_column_count, ADAPTER_RANK)
    states_all = plane_gather(local_rows, "mp")
    source_device, source_row = plane_rows(mp_index, slot_dev)
    gathered_slots = source_row * mp_count + source_device
    ignored, position_all, segment_all, adapter_all = slot_info(
        jnp.broadcast_to(own_lengths[None, :], (total_rows, request_count)),
        jnp.broadcast_to(own_adapters[None, :], (total_rows, request_count)),
        gathered_slots,
    )
    indicator_all = adapter_select_mask(adapter_all, adapter_column_count, ADAPTER_RANK)
    normed_all = normalize(states_all, attention_norm_gain)
    widths = [
        query_weight.shape[1],
        key_weight.shape[1],
        value_weight.shape[1],
        adapter_down_attention.shape[1],
    ]
    merged = jnp.dot(
        normed_all,
        jnp.concatenate([query_weight, key_weight, value_weight, adapter_down_attention], axis=1),
        preferred_element_type=jnp.float32,
    )
    edges = [sum(widths[:i]) for i in range(len(widths) + 1)]
    query_base, key_base, value_base, adapter_base = (
        merged[:, edges[i] : edges[i + 1]] for i in range(len(widths))
    )
    column_owner = jnp.arange(adapter_base.shape[1], dtype=jnp.int32) % adapter_column_count // ADAPTER_RANK
    adapter_terms_all = jnp.where(
        adapter_all[:, None] == column_owner[None, :], adapter_base, 0.0
    ).astype(jnp.bfloat16)
    query_projected = query_base + jnp.dot(
        adapter_terms_all[:, :adapter_column_count],
        adapter_up_query,
        preferred_element_type=jnp.float32,
    )
    key_projected = key_base + jnp.dot(
        adapter_terms_all[:, adapter_column_count : 2 * adapter_column_count],
        adapter_up_key_value[0],
        preferred_element_type=jnp.float32,
    )
    value_projected = value_base + jnp.dot(
        adapter_terms_all[:, 2 * adapter_column_count :],
        adapter_up_key_value[1],
        preferred_element_type=jnp.float32,
    )
    kv_pair = jnp.stack([key_projected, value_projected])
    partner = align_partner_rows(
        from_partner(kv_pair.astype(jnp.bfloat16), "mp", 0), mp_index % 2, slot_dev
    ).astype(kv_pair.dtype)
    parity = mp_index % 2
    joined = jnp.where(
        parity == 0,
        jnp.concatenate([kv_pair, partner], axis=2),
        jnp.concatenate([partner, kv_pair], axis=2),
    )
    key_projected = joined[0]
    value_projected = joined[1]
    queries = rotate(query_projected.reshape(total_rows, -1, HEAD_SIZE), position_all).astype(
        jnp.bfloat16
    )
    key_rows = rotate(key_projected.reshape(total_rows, -1, HEAD_SIZE), position_all).astype(
        jnp.bfloat16
    )
    value_rows = value_projected.reshape(total_rows, -1, HEAD_SIZE).astype(jnp.bfloat16)
    attention_output = attend(queries, key_rows, value_rows, position_all, segment_all)

    def out_term(first_row, row_count):
        return jnp.dot(
            attention_output,
            jnp.concatenate([output_weight, adapter_down_output], axis=1),
            preferred_element_type=jnp.float32,
        )

    summed = sum_rows(out_term, slot_dev)
    output_adapter_ranks = (summed[:, model_width:] * indicator_within).astype(jnp.bfloat16)
    residual_stream = (
        local_rows.astype(jnp.float32)
        + summed[:, :model_width]
        + jnp.dot(output_adapter_ranks, adapter_up_output, preferred_element_type=jnp.float32)
    ).astype(jnp.bfloat16)
    layer_result = feed_forward(
        residual_stream,
        indicator_within,
        feed_norm_gain,
        adapter_down_gate_up,
        adapter_up_gate_up,
        gate_up_full,
        down_full,
        adapter_down_feed,
        adapter_up_feed,
    )
    finished = jnp.where(living[:, None], layer_result, jnp.zeros_like(layer_result)).astype(
        jnp.bfloat16
    )
    return finished.reshape(1, slot_dev, 1, model_width)


def solution(mesh):
    placed = (
        P("req", None, "mp", None),
        P(),
        P(),
        P(),
        P(None, "mp"),
        P(None, "mp"),
        P(None, "mp"),
        P("mp", None),
        P(),
        P(None, "mp"),
        P(None, None, "mp"),
        P("mp", None),
        P(),
        P(),
        P(None, "req", "mp"),
        P("req", "mp"),
        P(),
        P(None, None, "mp"),
        P("mp", None),
        P(),
    )
    return jax.shard_map(
        shards, mesh=mesh, in_specs=placed, out_specs=P("req", None, "mp", None), check_vma=False
    )
```

```python
import jax
import jax.numpy as jnp
from jax import lax
from jax.sharding import PartitionSpec as P

HEAD_SIZE = 128
ADAPTER_RANK = 16
WINDOW = 128
SINK = 4


EPSILON = 1e-05
ROPE_THETA = 1000000.0


RING = 4


def _ring_pairs(size, stride, step):
    pairs = []
    for i in range(size):
        low = i % stride
        pos = (i // stride) % RING
        high = i // (stride * RING)
        dst = (high * RING + (pos + step) % RING) * stride + low
        pairs.append((i, dst))
    return pairs


def _shift(x, axis, stride, step):
    return lax.ppermute(x, axis, _ring_pairs(lax.axis_size(axis), stride, step))


def ring_gather(block, axis, stride):
    half = block.shape[0] // 2
    from_minus = _shift(block, axis, stride, 1)
    from_plus = _shift(block, axis, stride, -1)
    first = _shift(from_plus[:half], axis, stride, -1)
    second = _shift(from_minus[half:], axis, stride, 1)
    across = jnp.concatenate([first, second], axis=0)
    return jnp.stack([block, from_plus, across, from_minus])


def ring_scatter(parts, axis, stride):
    half = parts.shape[1] // 2
    wire = jnp.bfloat16
    got_a = _shift(parts[2, :half].astype(wire), axis, stride, 1).astype(jnp.float32)
    got_b = _shift(parts[2, half:].astype(wire), axis, stride, -1).astype(jnp.float32)
    plus = parts[1].at[:half].add(got_a)
    minus = parts[3].at[half:].add(got_b)
    back_a = _shift(minus.astype(wire), axis, stride, -1).astype(jnp.float32)
    back_b = _shift(plus.astype(wire), axis, stride, 1).astype(jnp.float32)
    return parts[0] + back_a + back_b


def ring_gather_direct(block, axis, stride):
    from_minus = _shift(block, axis, stride, 1)
    from_plus = _shift(block, axis, stride, -1)
    across = _shift(block, axis, stride, 2)
    return jnp.stack([block, from_plus, across, from_minus])


def ring_scatter_direct(parts, axis, stride):
    wire = jnp.bfloat16
    got_minus = _shift(parts[1].astype(wire), axis, stride, 1)
    got_plus = _shift(parts[3].astype(wire), axis, stride, -1)
    got_across = _shift(parts[2].astype(wire), axis, stride, 2)
    return (
        parts[0]
        + got_minus.astype(jnp.float32)
        + got_plus.astype(jnp.float32)
        + got_across.astype(jnp.float32)
    )


def plane_gather(block, axis):
    rows, cols = block.shape
    half = rows // 2
    a1 = ring_gather_direct(block[:half], axis, 4)
    b1 = ring_gather_direct(block[half:], axis, 1)
    a2 = ring_gather(a1.reshape(RING * half, cols), axis, 1)
    b2 = ring_gather(b1.reshape(RING * half, cols), axis, 4)
    return jnp.concatenate([a2.reshape(-1, cols), b2.reshape(-1, cols)], axis=0)


def plane_rows(mp_index, rows):
    half = rows // 2
    px, py = mp_index // RING, mp_index % RING
    g = jnp.arange(16 * rows, dtype=jnp.int32)
    second = g >= 8 * rows
    h = g % half
    outer = (g % (8 * rows)) // (RING * half)
    inner = (g % (RING * half)) // half
    kx = jnp.where(second, outer, inner)
    ky = jnp.where(second, inner, outer)
    src = ((px + kx) % RING) * RING + (py + ky) % RING
    local = jnp.where(second, h + half, h)
    return src, local


def plane_scatter(parts, axis, rows):
    cols = parts.shape[1]
    half = rows // 2
    a = parts[: 8 * rows].reshape(RING, RING * half, cols)
    b = parts[8 * rows:].reshape(RING, RING * half, cols)
    a1 = ring_scatter(a, axis, 1).reshape(RING, half, cols)
    b1 = ring_scatter(b, axis, 4).reshape(RING, half, cols)
    a2 = ring_scatter_direct(a1, axis, 4)
    b2 = ring_scatter_direct(b1, axis, 1)
    return jnp.concatenate([a2, b2], axis=0)


def align_partner_rows(partner, parity, rows):
    half = rows // 2
    lead = partner.shape[:-2]
    cols = partner.shape[-1]
    first = partner[..., : 8 * rows, :].reshape(*lead, RING, RING * half, cols)
    second = partner[..., 8 * rows :, :].reshape(*lead, RING, RING, half, cols)
    axis_a = len(lead)
    axis_b = len(lead) + 1
    first = jnp.where(parity == 0, jnp.roll(first, 1, axis_a), jnp.roll(first, -1, axis_a))
    second = jnp.where(parity == 0, jnp.roll(second, 1, axis_b), jnp.roll(second, -1, axis_b))
    return jnp.concatenate(
        [first.reshape(*lead, 8 * rows, cols), second.reshape(*lead, 8 * rows, cols)], axis=-2
    )


def from_partner(shard, axis, stride):
    return lax.ppermute(shard, axis, [(i, i ^ 1 << stride) for i in range(lax.axis_size(axis))])


def slot_info(length_rows, adapter_rows, slot_ids):
    request_ends = jnp.cumsum(length_rows, axis=1, dtype=jnp.int32)
    starts = request_ends - length_rows
    count_req = length_rows.shape[1]
    request = jnp.sum(
        (slot_ids[:, None] >= request_ends).astype(jnp.int32), axis=1, dtype=jnp.int32
    )
    living = request < count_req
    matches = request[:, None] == jnp.arange(count_req, dtype=jnp.int32)[None, :]
    opening = jnp.sum(jnp.where(matches, starts, 0), axis=1, dtype=jnp.int32)
    position = jnp.where(living, slot_ids - opening, 0)
    segment = jnp.where(living, request, count_req + slot_ids)
    chosen = jnp.sum(jnp.where(matches, adapter_rows, 0), axis=1, dtype=jnp.int32)
    adapter_slot = jnp.where(living, chosen, -1)
    return (living, position, segment, adapter_slot)


def normalize(input_tokens, gain_vec):
    values = input_tokens.astype(jnp.float32)
    factor = lax.rsqrt(jnp.mean(values * values, axis=-1, keepdims=True) + EPSILON)
    return (values * factor * gain_vec).astype(jnp.bfloat16)


def adapter_select_mask(adapter_slot, adapter_column_count, adapter_rank_size):
    token_owner_request = jnp.arange(adapter_column_count, dtype=jnp.int32) // adapter_rank_size
    return (adapter_slot[:, None] == token_owner_request[None, :]).astype(jnp.float32)


def rotate(vectors, position):
    half_dim = vectors.shape[-1] // 2
    inverse = ROPE_THETA ** (-(jnp.arange(half_dim, dtype=jnp.float32) * (2.0 / vectors.shape[-1])))
    angles = position.astype(jnp.float32)[:, None] * inverse[None, :]
    cosine = jnp.cos(angles)[:, None, :]
    sine_part = jnp.sin(angles)[:, None, :]
    lower_half = vectors[..., :half_dim]
    upper_half = vectors[..., half_dim:]
    return jnp.concatenate(
        [
            lower_half * cosine - upper_half * sine_part,
            upper_half * cosine + lower_half * sine_part,
        ],
        axis=-1,
    )


def attend(queries, key_rows, value_rows, position, segment):
    key_heads = key_rows.shape[1]
    group_size = queries.shape[1] // key_heads
    token_count = queries.shape[0]
    grouped_queries = queries.reshape(token_count, key_heads, group_size, queries.shape[2])
    scores = jnp.einsum(
        "qkgd,skd->kgqs", grouped_queries, key_rows, preferred_element_type=jnp.float32
    ) * queries.shape[2] ** (-0.5)
    allowed = (segment[:, None] == segment[None, :]) & (position[None, :] <= position[:, None])
    allowed = allowed & (
        (position[:, None] - position[None, :] < WINDOW) | (position[None, :] < SINK)
    )
    scores = jnp.where(allowed[None, None], scores, -jnp.inf)
    highest = jnp.max(scores, axis=-1, keepdims=True)
    weights_raw = jnp.exp(scores - highest)
    weights = (weights_raw / jnp.sum(weights_raw, axis=-1, keepdims=True)).astype(jnp.bfloat16)
    blended = jnp.einsum("kgqs,skd->qkgd", weights, value_rows, preferred_element_type=jnp.float32)
    return blended.reshape(token_count, -1).astype(jnp.bfloat16)


def spread_rows(first_part, second_part):
    width = first_part.shape[1]
    joined = plane_gather(jnp.concatenate([first_part, second_part], axis=1), "mp")
    return joined[:, :width], joined[:, width:]


def sum_rows(term_fn, row_count):
    return plane_scatter(term_fn(jnp.int32(0), lax.axis_size("mp") * row_count), "mp", row_count)


def feed_forward(
    residual_stream,
    adapter_indicator,
    feed_norm_gain,
    adapter_down_gate_up,
    adapter_up_gate_up,
    gate_up_full,
    down_full,
    adapter_down_feed,
    adapter_up_feed,
):
    adapter_column_count = adapter_indicator.shape[1]
    model_width = residual_stream.shape[1]
    feed_input = normalize(residual_stream, feed_norm_gain)
    gate_terms = (
        jnp.dot(feed_input, adapter_down_gate_up, preferred_element_type=jnp.float32)
        * jnp.tile(adapter_indicator, (1, 2))
    ).astype(jnp.bfloat16)
    mlp_all, gate_adapter_ranks = spread_rows(feed_input, gate_terms)
    gate_activation = jnp.dot(
        mlp_all, gate_up_full[0], preferred_element_type=jnp.float32
    ) + jnp.dot(
        gate_adapter_ranks[:, :adapter_column_count],
        adapter_up_gate_up[0],
        preferred_element_type=jnp.float32,
    )
    up_projected = jnp.dot(mlp_all, gate_up_full[1], preferred_element_type=jnp.float32) + jnp.dot(
        gate_adapter_ranks[:, adapter_column_count:],
        adapter_up_gate_up[1],
        preferred_element_type=jnp.float32,
    )
    hidden_activation = (jax.nn.silu(gate_activation) * up_projected).astype(jnp.bfloat16)

    def down_term(first_row, row_count):
        projected_rows = lax.dot_general(
            hidden_activation,
            down_full,
            (((1,), (1,)), ((), ())),
            preferred_element_type=jnp.float32,
        )
        return jnp.concatenate(
            [
                projected_rows,
                jnp.dot(hidden_activation, adapter_down_feed, preferred_element_type=jnp.float32),
            ],
            axis=1,
        )

    summed = sum_rows(down_term, residual_stream.shape[0])
    down_adapter_ranks = (summed[:, model_width:] * adapter_indicator).astype(jnp.bfloat16)
    return (
        residual_stream.astype(jnp.float32)
        + summed[:, :model_width]
        + jnp.dot(down_adapter_ranks, adapter_up_feed, preferred_element_type=jnp.float32)
    )


def shards(
    states,
    lengths,
    request_adapters,
    attention_norm_gain,
    query_weight,
    key_weight,
    value_weight,
    output_weight,
    adapter_down_attention,
    adapter_up_query,
    adapter_up_key_value,
    adapter_down_output,
    adapter_up_output,
    feed_norm_gain,
    gate_up_weight,
    down_weight,
    adapter_down_gate_up,
    adapter_up_gate_up,
    adapter_down_feed,
    adapter_up_feed,
):
    mp_count = lax.axis_size("mp")
    group_index = lax.axis_index("req")
    mp_index = lax.axis_index("mp")
    slot_dev = states.shape[1]
    model_width = states.shape[3]
    adapter_column_count = adapter_up_output.shape[0]
    total_rows = slot_dev * mp_count
    gate_up_full, down_full = (
        lax.all_gather(gate_up_weight, "req", axis=1, tiled=True),
        lax.all_gather(down_weight, "req", axis=0, tiled=True),
    )
    local_rows = states.reshape(slot_dev, model_width)
    own_lengths = lax.dynamic_index_in_dim(lengths, group_index, 0, keepdims=False)
    own_adapters = lax.dynamic_index_in_dim(request_adapters, group_index, 0, keepdims=False)
    request_count = own_lengths.shape[0]
    local_slots = jnp.arange(slot_dev, dtype=jnp.int32) * mp_count + mp_index
    living, unused_pos, unused_seg, adapter_within = slot_info(
        jnp.broadcast_to(own_lengths[None, :], (slot_dev, request_count)),
        jnp.broadcast_to(own_adapters[None, :], (slot_dev, request_count)),
        local_slots,
    )
    indicator_within = adapter_select_mask(adapter_within, adapter_column_count, ADAPTER_RANK)
    states_all = plane_gather(local_rows, "mp")
    source_device, source_row = plane_rows(mp_index, slot_dev)
    gathered_slots = source_row * mp_count + source_device
    ignored, position_all, segment_all, adapter_all = slot_info(
        jnp.broadcast_to(own_lengths[None, :], (total_rows, request_count)),
        jnp.broadcast_to(own_adapters[None, :], (total_rows, request_count)),
        gathered_slots,
    )
    indicator_all = adapter_select_mask(adapter_all, adapter_column_count, ADAPTER_RANK)
    normed_all = normalize(states_all, attention_norm_gain)
    widths = [
        query_weight.shape[1],
        key_weight.shape[1],
        value_weight.shape[1],
        adapter_down_attention.shape[1],
    ]
    merged = jnp.dot(
        normed_all,
        jnp.concatenate([query_weight, key_weight, value_weight, adapter_down_attention], axis=1),
        preferred_element_type=jnp.float32,
    )
    edges = [sum(widths[:i]) for i in range(len(widths) + 1)]
    query_base, key_base, value_base, adapter_base = (
        merged[:, edges[i] : edges[i + 1]] for i in range(len(widths))
    )
    column_owner = jnp.arange(adapter_base.shape[1], dtype=jnp.int32) % adapter_column_count // ADAPTER_RANK
    adapter_terms_all = jnp.where(
        adapter_all[:, None] == column_owner[None, :], adapter_base, 0.0
    ).astype(jnp.bfloat16)
    query_projected = query_base + jnp.dot(
        adapter_terms_all[:, :adapter_column_count],
        adapter_up_query,
        preferred_element_type=jnp.float32,
    )
    key_projected = key_base + jnp.dot(
        adapter_terms_all[:, adapter_column_count : 2 * adapter_column_count],
        adapter_up_key_value[0],
        preferred_element_type=jnp.float32,
    )
    value_projected = value_base + jnp.dot(
        adapter_terms_all[:, 2 * adapter_column_count :],
        adapter_up_key_value[1],
        preferred_element_type=jnp.float32,
    )
    kv_pair = jnp.stack([key_projected, value_projected])
    partner = align_partner_rows(
        from_partner(kv_pair.astype(jnp.bfloat16), "mp", 0), mp_index % 2, slot_dev
    ).astype(kv_pair.dtype)
    parity = mp_index % 2
    joined = jnp.where(
        parity == 0,
        jnp.concatenate([kv_pair, partner], axis=2),
        jnp.concatenate([partner, kv_pair], axis=2),
    )
    key_projected = joined[0]
    value_projected = joined[1]
    queries = rotate(query_projected.reshape(total_rows, -1, HEAD_SIZE), position_all).astype(
        jnp.bfloat16
    )
    key_rows = rotate(key_projected.reshape(total_rows, -1, HEAD_SIZE), position_all).astype(
        jnp.bfloat16
    )
    value_rows = value_projected.reshape(total_rows, -1, HEAD_SIZE).astype(jnp.bfloat16)
    attention_output = attend(queries, key_rows, value_rows, position_all, segment_all)

    def out_term(first_row, row_count):
        return jnp.concatenate(
            [
                jnp.dot(attention_output, output_weight, preferred_element_type=jnp.float32),
                jnp.dot(attention_output, adapter_down_output, preferred_element_type=jnp.float32),
            ],
            axis=1,
        )

    summed = sum_rows(out_term, slot_dev)
    output_adapter_ranks = (summed[:, model_width:] * indicator_within).astype(jnp.bfloat16)
    residual_stream = (
        local_rows.astype(jnp.float32)
        + summed[:, :model_width]
        + jnp.dot(output_adapter_ranks, adapter_up_output, preferred_element_type=jnp.float32)
    ).astype(jnp.bfloat16)
    layer_result = feed_forward(
        residual_stream,
        indicator_within,
        feed_norm_gain,
        adapter_down_gate_up,
        adapter_up_gate_up,
        gate_up_full,
        down_full,
        adapter_down_feed,
        adapter_up_feed,
    )
    finished = jnp.where(living[:, None], layer_result, jnp.zeros_like(layer_result)).astype(
        jnp.bfloat16
    )
    return finished.reshape(1, slot_dev, 1, model_width)


def solution(mesh):
    placed = (
        P("req", None, "mp", None),
        P(),
        P(),
        P(),
        P(None, "mp"),
        P(None, "mp"),
        P(None, "mp"),
        P("mp", None),
        P(),
        P(None, "mp"),
        P(None, None, "mp"),
        P("mp", None),
        P(),
        P(),
        P(None, "req", "mp"),
        P("req", "mp"),
        P(),
        P(None, None, "mp"),
        P("mp", None),
        P(),
    )
    return jax.shard_map(
        shards, mesh=mesh, in_specs=placed, out_specs=P("req", None, "mp", None), check_vma=False
    )
```

```python
import jax
import jax.numpy as jnp
from jax import lax
from jax.sharding import PartitionSpec as P

HEAD_SIZE = 128
ADAPTER_RANK = 16
WINDOW = 128
SINK = 4


EPSILON = 1e-05
ROPE_THETA = 1000000.0


RING = 4


def _ring_pairs(size, stride, step):
    pairs = []
    for i in range(size):
        low = i % stride
        pos = (i // stride) % RING
        high = i // (stride * RING)
        dst = (high * RING + (pos + step) % RING) * stride + low
        pairs.append((i, dst))
    return pairs


def _shift(x, axis, stride, step):
    return lax.ppermute(x, axis, _ring_pairs(lax.axis_size(axis), stride, step))


def ring_gather(block, axis, stride):
    half = block.shape[0] // 2
    from_minus = _shift(block, axis, stride, 1)
    from_plus = _shift(block, axis, stride, -1)
    first = _shift(from_plus[:half], axis, stride, -1)
    second = _shift(from_minus[half:], axis, stride, 1)
    across = jnp.concatenate([first, second], axis=0)
    return jnp.stack([block, from_plus, across, from_minus])


def ring_scatter(parts, axis, stride):
    half = parts.shape[1] // 2
    wire = jnp.bfloat16
    got_a = _shift(parts[2, :half].astype(wire), axis, stride, 1).astype(jnp.float32)
    got_b = _shift(parts[2, half:].astype(wire), axis, stride, -1).astype(jnp.float32)
    plus = parts[1].at[:half].add(got_a)
    minus = parts[3].at[half:].add(got_b)
    back_a = _shift(minus.astype(wire), axis, stride, -1).astype(jnp.float32)
    back_b = _shift(plus.astype(wire), axis, stride, 1).astype(jnp.float32)
    return parts[0] + back_a + back_b


def ring_gather_direct(block, axis, stride):
    from_minus = _shift(block, axis, stride, 1)
    from_plus = _shift(block, axis, stride, -1)
    across = _shift(block, axis, stride, 2)
    return jnp.stack([block, from_plus, across, from_minus])


def ring_scatter_direct(parts, axis, stride):
    wire = jnp.bfloat16
    got_minus = _shift(parts[1].astype(wire), axis, stride, 1)
    got_plus = _shift(parts[3].astype(wire), axis, stride, -1)
    got_across = _shift(parts[2].astype(wire), axis, stride, 2)
    return (
        parts[0]
        + got_minus.astype(jnp.float32)
        + got_plus.astype(jnp.float32)
        + got_across.astype(jnp.float32)
    )


def plane_gather(block, axis):
    rows, cols = block.shape
    half = rows // 2
    a1 = ring_gather_direct(block[:half], axis, 4)
    b1 = ring_gather_direct(block[half:], axis, 1)
    a2 = ring_gather(a1.reshape(RING * half, cols), axis, 1)
    b2 = ring_gather(b1.reshape(RING * half, cols), axis, 4)
    return jnp.concatenate([a2.reshape(-1, cols), b2.reshape(-1, cols)], axis=0), a2[1]


def plane_rows(mp_index, rows):
    half = rows // 2
    px, py = mp_index // RING, mp_index % RING
    g = jnp.arange(16 * rows, dtype=jnp.int32)
    second = g >= 8 * rows
    h = g % half
    outer = (g % (8 * rows)) // (RING * half)
    inner = (g % (RING * half)) // half
    kx = jnp.where(second, outer, inner)
    ky = jnp.where(second, inner, outer)
    src = ((px + kx) % RING) * RING + (py + ky) % RING
    local = jnp.where(second, h + half, h)
    return src, local


def plane_scatter(parts, axis, rows):
    cols = parts.shape[1]
    half = rows // 2
    a = parts[: 8 * rows].reshape(RING, RING * half, cols)
    b = parts[8 * rows:].reshape(RING, RING * half, cols)
    a1 = ring_scatter(a, axis, 1).reshape(RING, half, cols)
    b1 = ring_scatter(b, axis, 4).reshape(RING, half, cols)
    a2 = ring_scatter_direct(a1, axis, 4)
    b2 = ring_scatter_direct(b1, axis, 1)
    return jnp.concatenate([a2, b2], axis=0)


def align_partner_rows(partner, parity, rows):
    half = rows // 2
    lead = partner.shape[:-2]
    cols = partner.shape[-1]
    first = partner[..., : 8 * rows, :].reshape(*lead, RING, RING * half, cols)
    second = partner[..., 8 * rows :, :].reshape(*lead, RING, RING, half, cols)
    axis_a = len(lead)
    axis_b = len(lead) + 1
    first = jnp.where(parity == 0, jnp.roll(first, 1, axis_a), jnp.roll(first, -1, axis_a))
    second = jnp.where(parity == 0, jnp.roll(second, 1, axis_b), jnp.roll(second, -1, axis_b))
    return jnp.concatenate(
        [first.reshape(*lead, 8 * rows, cols), second.reshape(*lead, 8 * rows, cols)], axis=-2
    )


def from_partner(shard, axis, stride):
    return lax.ppermute(shard, axis, [(i, i ^ 1 << stride) for i in range(lax.axis_size(axis))])


def slot_info(length_rows, adapter_rows, slot_ids):
    request_ends = jnp.cumsum(length_rows, axis=1, dtype=jnp.int32)
    starts = request_ends - length_rows
    count_req = length_rows.shape[1]
    request = jnp.sum(
        (slot_ids[:, None] >= request_ends).astype(jnp.int32), axis=1, dtype=jnp.int32
    )
    living = request < count_req
    matches = request[:, None] == jnp.arange(count_req, dtype=jnp.int32)[None, :]
    opening = jnp.sum(jnp.where(matches, starts, 0), axis=1, dtype=jnp.int32)
    position = jnp.where(living, slot_ids - opening, 0)
    segment = jnp.where(living, request, count_req + slot_ids)
    chosen = jnp.sum(jnp.where(matches, adapter_rows, 0), axis=1, dtype=jnp.int32)
    adapter_slot = jnp.where(living, chosen, -1)
    return (living, position, segment, adapter_slot)


def normalize(input_tokens, gain_vec):
    values = input_tokens.astype(jnp.float32)
    factor = lax.rsqrt(jnp.mean(values * values, axis=-1, keepdims=True) + EPSILON)
    return (values * factor * gain_vec).astype(jnp.bfloat16)


def adapter_select_mask(adapter_slot, adapter_column_count, adapter_rank_size):
    token_owner_request = jnp.arange(adapter_column_count, dtype=jnp.int32) // adapter_rank_size
    return (adapter_slot[:, None] == token_owner_request[None, :]).astype(jnp.float32)


def rotate(vectors, position):
    half_dim = vectors.shape[-1] // 2
    inverse = ROPE_THETA ** (-(jnp.arange(half_dim, dtype=jnp.float32) * (2.0 / vectors.shape[-1])))
    angles = position.astype(jnp.float32)[:, None] * inverse[None, :]
    cosine = jnp.cos(angles)[:, None, :]
    sine_part = jnp.sin(angles)[:, None, :]
    lower_half = vectors[..., :half_dim]
    upper_half = vectors[..., half_dim:]
    return jnp.concatenate(
        [
            lower_half * cosine - upper_half * sine_part,
            upper_half * cosine + lower_half * sine_part,
        ],
        axis=-1,
    )


def attend(queries, key_rows, value_rows, position, segment):
    key_heads = key_rows.shape[1]
    group_size = queries.shape[1] // key_heads
    token_count = queries.shape[0]
    grouped_queries = queries.reshape(token_count, key_heads, group_size, queries.shape[2])
    scores = jnp.einsum(
        "qkgd,skd->kgqs", grouped_queries, key_rows, preferred_element_type=jnp.float32
    ) * queries.shape[2] ** (-0.5)
    allowed = (segment[:, None] == segment[None, :]) & (position[None, :] <= position[:, None])
    allowed = allowed & (
        (position[:, None] - position[None, :] < WINDOW) | (position[None, :] < SINK)
    )
    scores = jnp.where(allowed[None, None], scores, -jnp.inf)
    highest = jnp.max(scores, axis=-1, keepdims=True)
    weights_raw = jnp.exp(scores - highest)
    weights = (weights_raw / jnp.sum(weights_raw, axis=-1, keepdims=True)).astype(jnp.bfloat16)
    blended = jnp.einsum("kgqs,skd->qkgd", weights, value_rows, preferred_element_type=jnp.float32)
    return blended.reshape(token_count, -1).astype(jnp.bfloat16)


def spread_rows(first_part, second_part):
    width = first_part.shape[1]
    joined = plane_gather(jnp.concatenate([first_part, second_part], axis=1), "mp")[0]
    return joined[:, :width], joined[:, width:]


def sum_rows(term_fn, row_count):
    return plane_scatter(term_fn(jnp.int32(0), lax.axis_size("mp") * row_count), "mp", row_count)


def feed_forward(
    residual_stream,
    adapter_indicator,
    feed_norm_gain,
    adapter_down_gate_up,
    adapter_up_gate_up,
    gate_up_full,
    down_full,
    adapter_down_feed,
    adapter_up_feed,
):
    adapter_column_count = adapter_indicator.shape[1]
    model_width = residual_stream.shape[1]
    feed_input = normalize(residual_stream, feed_norm_gain)
    gate_terms = (
        jnp.dot(feed_input, adapter_down_gate_up, preferred_element_type=jnp.float32)
        * jnp.tile(adapter_indicator, (1, 2))
    ).astype(jnp.bfloat16)
    mlp_all, gate_adapter_ranks = spread_rows(feed_input, gate_terms)
    gate_activation = jnp.dot(
        mlp_all, gate_up_full[0], preferred_element_type=jnp.float32
    ) + jnp.dot(
        gate_adapter_ranks[:, :adapter_column_count],
        adapter_up_gate_up[0],
        preferred_element_type=jnp.float32,
    )
    up_projected = jnp.dot(mlp_all, gate_up_full[1], preferred_element_type=jnp.float32) + jnp.dot(
        gate_adapter_ranks[:, adapter_column_count:],
        adapter_up_gate_up[1],
        preferred_element_type=jnp.float32,
    )
    hidden_activation = (jax.nn.silu(gate_activation) * up_projected).astype(jnp.bfloat16)

    def down_term(first_row, row_count):
        projected_rows = lax.dot_general(
            hidden_activation,
            down_full,
            (((1,), (1,)), ((), ())),
            preferred_element_type=jnp.float32,
        )
        return jnp.concatenate(
            [
                projected_rows,
                jnp.dot(hidden_activation, adapter_down_feed, preferred_element_type=jnp.float32),
            ],
            axis=1,
        )

    summed = sum_rows(down_term, residual_stream.shape[0])
    down_adapter_ranks = (summed[:, model_width:] * adapter_indicator).astype(jnp.bfloat16)
    return (
        residual_stream.astype(jnp.float32)
        + summed[:, :model_width]
        + jnp.dot(down_adapter_ranks, adapter_up_feed, preferred_element_type=jnp.float32)
    )


def shards(
    states,
    lengths,
    request_adapters,
    attention_norm_gain,
    query_weight,
    key_weight,
    value_weight,
    output_weight,
    adapter_down_attention,
    adapter_up_query,
    adapter_up_key_value,
    adapter_down_output,
    adapter_up_output,
    feed_norm_gain,
    gate_up_weight,
    down_weight,
    adapter_down_gate_up,
    adapter_up_gate_up,
    adapter_down_feed,
    adapter_up_feed,
):
    mp_count = lax.axis_size("mp")
    group_index = lax.axis_index("req")
    mp_index = lax.axis_index("mp")
    slot_dev = states.shape[1]
    model_width = states.shape[3]
    adapter_column_count = adapter_up_output.shape[0]
    total_rows = slot_dev * mp_count
    gate_up_full, down_full = (
        lax.all_gather(gate_up_weight, "req", axis=1, tiled=True),
        lax.all_gather(down_weight, "req", axis=0, tiled=True),
    )
    local_rows = states.reshape(slot_dev, model_width)
    own_lengths = lax.dynamic_index_in_dim(lengths, group_index, 0, keepdims=False)
    own_adapters = lax.dynamic_index_in_dim(request_adapters, group_index, 0, keepdims=False)
    request_count = own_lengths.shape[0]
    local_slots = jnp.arange(slot_dev, dtype=jnp.int32) * mp_count + mp_index
    living, unused_pos, unused_seg, adapter_within = slot_info(
        jnp.broadcast_to(own_lengths[None, :], (slot_dev, request_count)),
        jnp.broadcast_to(own_adapters[None, :], (slot_dev, request_count)),
        local_slots,
    )
    indicator_within = adapter_select_mask(adapter_within, adapter_column_count, ADAPTER_RANK)
    states_all, arrived = plane_gather(local_rows, "mp")
    key_weight, value_weight, arrived = lax.optimization_barrier((key_weight, value_weight, arrived))
    source_device, source_row = plane_rows(mp_index, slot_dev)
    gathered_slots = source_row * mp_count + source_device
    ignored, position_all, segment_all, adapter_all = slot_info(
        jnp.broadcast_to(own_lengths[None, :], (total_rows, request_count)),
        jnp.broadcast_to(own_adapters[None, :], (total_rows, request_count)),
        gathered_slots,
    )
    indicator_all = adapter_select_mask(adapter_all, adapter_column_count, ADAPTER_RANK)
    normed_all = normalize(states_all, attention_norm_gain)
    widths = [
        query_weight.shape[1],
        key_weight.shape[1],
        value_weight.shape[1],
        adapter_down_attention.shape[1],
    ]
    merged = jnp.dot(
        normed_all,
        jnp.concatenate([query_weight, key_weight, value_weight, adapter_down_attention], axis=1),
        preferred_element_type=jnp.float32,
    )
    edges = [sum(widths[:i]) for i in range(len(widths) + 1)]
    query_base, key_base, value_base, adapter_base = (
        merged[:, edges[i] : edges[i + 1]] for i in range(len(widths))
    )
    adapter_terms_all = (adapter_base * jnp.tile(indicator_all, (1, 3))).astype(jnp.bfloat16)
    query_projected = query_base + jnp.dot(
        adapter_terms_all[:, :adapter_column_count],
        adapter_up_query,
        preferred_element_type=jnp.float32,
    )
    key_projected = key_base + jnp.dot(
        adapter_terms_all[:, adapter_column_count : 2 * adapter_column_count],
        adapter_up_key_value[0],
        preferred_element_type=jnp.float32,
    )
    value_projected = value_base + jnp.dot(
        adapter_terms_all[:, 2 * adapter_column_count :],
        adapter_up_key_value[1],
        preferred_element_type=jnp.float32,
    )
    kv_pair = jnp.stack([key_projected, value_projected])
    partner = align_partner_rows(
        from_partner(kv_pair.astype(jnp.bfloat16), "mp", 0), mp_index % 2, slot_dev
    ).astype(kv_pair.dtype)
    parity = mp_index % 2
    joined = jnp.where(
        parity == 0,
        jnp.concatenate([kv_pair, partner], axis=2),
        jnp.concatenate([partner, kv_pair], axis=2),
    )
    key_projected = joined[0]
    value_projected = joined[1]
    queries = rotate(query_projected.reshape(total_rows, -1, HEAD_SIZE), position_all).astype(
        jnp.bfloat16
    )
    key_rows = rotate(key_projected.reshape(total_rows, -1, HEAD_SIZE), position_all).astype(
        jnp.bfloat16
    )
    value_rows = value_projected.reshape(total_rows, -1, HEAD_SIZE).astype(jnp.bfloat16)
    attention_output = attend(queries, key_rows, value_rows, position_all, segment_all)

    def out_term(first_row, row_count):
        return jnp.concatenate(
            [
                jnp.dot(attention_output, output_weight, preferred_element_type=jnp.float32),
                jnp.dot(attention_output, adapter_down_output, preferred_element_type=jnp.float32),
            ],
            axis=1,
        )

    summed = sum_rows(out_term, slot_dev)
    output_adapter_ranks = (summed[:, model_width:] * indicator_within).astype(jnp.bfloat16)
    residual_stream = (
        local_rows.astype(jnp.float32)
        + summed[:, :model_width]
        + jnp.dot(output_adapter_ranks, adapter_up_output, preferred_element_type=jnp.float32)
    ).astype(jnp.bfloat16)
    layer_result = feed_forward(
        residual_stream,
        indicator_within,
        feed_norm_gain,
        adapter_down_gate_up,
        adapter_up_gate_up,
        gate_up_full,
        down_full,
        adapter_down_feed,
        adapter_up_feed,
    )
    finished = jnp.where(living[:, None], layer_result, jnp.zeros_like(layer_result)).astype(
        jnp.bfloat16
    )
    return finished.reshape(1, slot_dev, 1, model_width)


def solution(mesh):
    placed = (
        P("req", None, "mp", None),
        P(),
        P(),
        P(),
        P(None, "mp"),
        P(None, "mp"),
        P(None, "mp"),
        P("mp", None),
        P(),
        P(None, "mp"),
        P(None, None, "mp"),
        P("mp", None),
        P(),
        P(),
        P(None, "req", "mp"),
        P("req", "mp"),
        P(),
        P(None, None, "mp"),
        P("mp", None),
        P(),
    )
    return jax.shard_map(
        shards, mesh=mesh, in_specs=placed, out_specs=P("req", None, "mp", None), check_vma=False
    )
```

```python
import jax
import jax.numpy as jnp
from jax import lax
from jax.sharding import PartitionSpec as P

HEAD_SIZE = 128
ADAPTER_RANK = 16
WINDOW = 128
SINK = 4


EPSILON = 1e-05
ROPE_THETA = 1000000.0


RING = 4


def _ring_pairs(size, stride, step):
    pairs = []
    for i in range(size):
        low = i % stride
        pos = (i // stride) % RING
        high = i // (stride * RING)
        dst = (high * RING + (pos + step) % RING) * stride + low
        pairs.append((i, dst))
    return pairs


def _shift(x, axis, stride, step):
    return lax.ppermute(x, axis, _ring_pairs(lax.axis_size(axis), stride, step))


def ring_gather(block, axis, stride):
    half = block.shape[0] // 2
    from_minus = _shift(block, axis, stride, 1)
    from_plus = _shift(block, axis, stride, -1)
    first = _shift(from_plus[:half], axis, stride, -1)
    second = _shift(from_minus[half:], axis, stride, 1)
    across = jnp.concatenate([first, second], axis=0)
    return jnp.stack([block, from_plus, across, from_minus])


def ring_scatter(parts, axis, stride):
    half = parts.shape[1] // 2
    wire = jnp.bfloat16
    got_a = _shift(parts[2, :half].astype(wire), axis, stride, 1).astype(jnp.float32)
    got_b = _shift(parts[2, half:].astype(wire), axis, stride, -1).astype(jnp.float32)
    plus = parts[1].astype(jnp.float32).at[:half].add(got_a)
    minus = parts[3].astype(jnp.float32).at[half:].add(got_b)
    back_a = _shift(minus.astype(wire), axis, stride, -1).astype(jnp.float32)
    back_b = _shift(plus.astype(wire), axis, stride, 1).astype(jnp.float32)
    return parts[0].astype(jnp.float32) + back_a + back_b


def ring_gather_direct(block, axis, stride):
    from_minus = _shift(block, axis, stride, 1)
    from_plus = _shift(block, axis, stride, -1)
    across = _shift(block, axis, stride, 2)
    return jnp.stack([block, from_plus, across, from_minus])


def ring_scatter_direct(parts, axis, stride):
    wire = jnp.bfloat16
    got_minus = _shift(parts[1].astype(wire), axis, stride, 1)
    got_plus = _shift(parts[3].astype(wire), axis, stride, -1)
    got_across = _shift(parts[2].astype(wire), axis, stride, 2)
    return (
        parts[0].astype(jnp.float32)
        + got_minus.astype(jnp.float32)
        + got_plus.astype(jnp.float32)
        + got_across.astype(jnp.float32)
    )


def plane_gather(block, axis):
    rows, cols = block.shape
    half = rows // 2
    a1 = ring_gather_direct(block[:half], axis, 4)
    b1 = ring_gather_direct(block[half:], axis, 1)
    a2 = ring_gather(a1.reshape(RING * half, cols), axis, 1)
    b2 = ring_gather(b1.reshape(RING * half, cols), axis, 4)
    return jnp.concatenate([a2.reshape(-1, cols), b2.reshape(-1, cols)], axis=0)


def plane_rows(mp_index, rows):
    half = rows // 2
    px, py = mp_index // RING, mp_index % RING
    g = jnp.arange(16 * rows, dtype=jnp.int32)
    second = g >= 8 * rows
    h = g % half
    outer = (g % (8 * rows)) // (RING * half)
    inner = (g % (RING * half)) // half
    kx = jnp.where(second, outer, inner)
    ky = jnp.where(second, inner, outer)
    src = ((px + kx) % RING) * RING + (py + ky) % RING
    local = jnp.where(second, h + half, h)
    return src, local


def plane_scatter(parts, axis, rows):
    cols = parts.shape[1]
    half = rows // 2
    a = parts[: 8 * rows].reshape(RING, RING * half, cols)
    b = parts[8 * rows:].reshape(RING, RING * half, cols)
    a1 = ring_scatter(a, axis, 1).reshape(RING, half, cols)
    b1 = ring_scatter(b, axis, 4).reshape(RING, half, cols)
    a2 = ring_scatter_direct(a1, axis, 4)
    b2 = ring_scatter_direct(b1, axis, 1)
    return jnp.concatenate([a2, b2], axis=0)


def align_partner_rows(partner, parity, rows):
    half = rows // 2
    lead = partner.shape[:-2]
    cols = partner.shape[-1]
    first = partner[..., : 8 * rows, :].reshape(*lead, RING, RING * half, cols)
    second = partner[..., 8 * rows :, :].reshape(*lead, RING, RING, half, cols)
    axis_a = len(lead)
    axis_b = len(lead) + 1
    first = jnp.where(parity == 0, jnp.roll(first, 1, axis_a), jnp.roll(first, -1, axis_a))
    second = jnp.where(parity == 0, jnp.roll(second, 1, axis_b), jnp.roll(second, -1, axis_b))
    return jnp.concatenate(
        [first.reshape(*lead, 8 * rows, cols), second.reshape(*lead, 8 * rows, cols)], axis=-2
    )


def from_partner(shard, axis, stride):
    return lax.ppermute(shard, axis, [(i, i ^ 1 << stride) for i in range(lax.axis_size(axis))])


def slot_info(length_rows, adapter_rows, slot_ids):
    request_ends = jnp.cumsum(length_rows, axis=1, dtype=jnp.int32)
    starts = request_ends - length_rows
    count_req = length_rows.shape[1]
    request = jnp.sum(
        (slot_ids[:, None] >= request_ends).astype(jnp.int32), axis=1, dtype=jnp.int32
    )
    living = request < count_req
    matches = request[:, None] == jnp.arange(count_req, dtype=jnp.int32)[None, :]
    opening = jnp.sum(jnp.where(matches, starts, 0), axis=1, dtype=jnp.int32)
    position = jnp.where(living, slot_ids - opening, 0)
    segment = jnp.where(living, request, count_req + slot_ids)
    chosen = jnp.sum(jnp.where(matches, adapter_rows, 0), axis=1, dtype=jnp.int32)
    adapter_slot = jnp.where(living, chosen, -1)
    return (living, position, segment, adapter_slot)


def normalize(input_tokens, gain_vec):
    values = input_tokens.astype(jnp.float32)
    factor = lax.rsqrt(jnp.mean(values * values, axis=-1, keepdims=True) + EPSILON)
    return (values * factor * gain_vec).astype(jnp.bfloat16)


def adapter_select_mask(adapter_slot, adapter_column_count, adapter_rank_size):
    token_owner_request = jnp.arange(adapter_column_count, dtype=jnp.int32) // adapter_rank_size
    return (adapter_slot[:, None] == token_owner_request[None, :]).astype(jnp.float32)


def rotate(vectors, position):
    half_dim = vectors.shape[-1] // 2
    inverse = ROPE_THETA ** (-(jnp.arange(half_dim, dtype=jnp.float32) * (2.0 / vectors.shape[-1])))
    angles = position.astype(jnp.float32)[:, None] * inverse[None, :]
    cosine = jnp.cos(angles)[:, None, :]
    sine_part = jnp.sin(angles)[:, None, :]
    lower_half = vectors[..., :half_dim]
    upper_half = vectors[..., half_dim:]
    return jnp.concatenate(
        [
            lower_half * cosine - upper_half * sine_part,
            upper_half * cosine + lower_half * sine_part,
        ],
        axis=-1,
    )


def attend(queries, key_rows, value_rows, position, segment):
    key_heads = key_rows.shape[1]
    group_size = queries.shape[1] // key_heads
    token_count = queries.shape[0]
    grouped_queries = queries.reshape(token_count, key_heads, group_size, queries.shape[2])
    scores = jnp.einsum(
        "qkgd,skd->kgqs", grouped_queries, key_rows, preferred_element_type=jnp.float32
    ) * queries.shape[2] ** (-0.5)
    allowed = (segment[:, None] == segment[None, :]) & (position[None, :] <= position[:, None])
    allowed = allowed & (
        (position[:, None] - position[None, :] < WINDOW) | (position[None, :] < SINK)
    )
    scores = jnp.where(allowed[None, None], scores, -jnp.inf)
    highest = jnp.max(scores, axis=-1, keepdims=True)
    weights_raw = jnp.exp(scores - highest)
    weights = (weights_raw / jnp.sum(weights_raw, axis=-1, keepdims=True)).astype(jnp.bfloat16)
    blended = jnp.einsum("kgqs,skd->qkgd", weights, value_rows, preferred_element_type=jnp.float32)
    return blended.reshape(token_count, -1).astype(jnp.bfloat16)


def spread_rows(first_part, second_part):
    width = first_part.shape[1]
    joined = plane_gather(jnp.concatenate([first_part, second_part], axis=1), "mp")
    return joined[:, :width], joined[:, width:]


def sum_rows(term_fn, row_count):
    partial = term_fn(jnp.int32(0), lax.axis_size("mp") * row_count).astype(jnp.bfloat16)
    return plane_scatter(partial, "mp", row_count)


def feed_forward(
    residual_stream,
    adapter_indicator,
    feed_norm_gain,
    adapter_down_gate_up,
    adapter_up_gate_up,
    gate_up_full,
    down_full,
    adapter_down_feed,
    adapter_up_feed,
):
    adapter_column_count = adapter_indicator.shape[1]
    model_width = residual_stream.shape[1]
    feed_input = normalize(residual_stream, feed_norm_gain)
    gate_terms = (
        jnp.dot(feed_input, adapter_down_gate_up, preferred_element_type=jnp.float32)
        * jnp.tile(adapter_indicator, (1, 2))
    ).astype(jnp.bfloat16)
    mlp_all, gate_adapter_ranks = spread_rows(feed_input, gate_terms)
    gate_activation = jnp.dot(
        mlp_all, gate_up_full[0], preferred_element_type=jnp.float32
    ) + jnp.dot(
        gate_adapter_ranks[:, :adapter_column_count],
        adapter_up_gate_up[0],
        preferred_element_type=jnp.float32,
    )
    up_projected = jnp.dot(mlp_all, gate_up_full[1], preferred_element_type=jnp.float32) + jnp.dot(
        gate_adapter_ranks[:, adapter_column_count:],
        adapter_up_gate_up[1],
        preferred_element_type=jnp.float32,
    )
    hidden_activation = (jax.nn.silu(gate_activation) * up_projected).astype(jnp.bfloat16)

    def down_term(first_row, row_count):
        projected_rows = lax.dot_general(
            hidden_activation,
            down_full,
            (((1,), (1,)), ((), ())),
            preferred_element_type=jnp.float32,
        )
        return jnp.concatenate(
            [
                projected_rows,
                jnp.dot(hidden_activation, adapter_down_feed, preferred_element_type=jnp.float32),
            ],
            axis=1,
        )

    summed = sum_rows(down_term, residual_stream.shape[0])
    down_adapter_ranks = (summed[:, model_width:] * adapter_indicator).astype(jnp.bfloat16)
    return (
        residual_stream.astype(jnp.float32)
        + summed[:, :model_width]
        + jnp.dot(down_adapter_ranks, adapter_up_feed, preferred_element_type=jnp.float32)
    )


def shards(
    states,
    lengths,
    request_adapters,
    attention_norm_gain,
    query_weight,
    key_weight,
    value_weight,
    output_weight,
    adapter_down_attention,
    adapter_up_query,
    adapter_up_key_value,
    adapter_down_output,
    adapter_up_output,
    feed_norm_gain,
    gate_up_weight,
    down_weight,
    adapter_down_gate_up,
    adapter_up_gate_up,
    adapter_down_feed,
    adapter_up_feed,
):
    mp_count = lax.axis_size("mp")
    group_index = lax.axis_index("req")
    mp_index = lax.axis_index("mp")
    slot_dev = states.shape[1]
    model_width = states.shape[3]
    adapter_column_count = adapter_up_output.shape[0]
    total_rows = slot_dev * mp_count
    gate_up_full, down_full = (
        lax.all_gather(gate_up_weight, "req", axis=1, tiled=True),
        lax.all_gather(down_weight, "req", axis=0, tiled=True),
    )
    local_rows = states.reshape(slot_dev, model_width)
    own_lengths = lax.dynamic_index_in_dim(lengths, group_index, 0, keepdims=False)
    own_adapters = lax.dynamic_index_in_dim(request_adapters, group_index, 0, keepdims=False)
    request_count = own_lengths.shape[0]
    local_slots = jnp.arange(slot_dev, dtype=jnp.int32) * mp_count + mp_index
    living, unused_pos, unused_seg, adapter_within = slot_info(
        jnp.broadcast_to(own_lengths[None, :], (slot_dev, request_count)),
        jnp.broadcast_to(own_adapters[None, :], (slot_dev, request_count)),
        local_slots,
    )
    indicator_within = adapter_select_mask(adapter_within, adapter_column_count, ADAPTER_RANK)
    states_all = plane_gather(local_rows, "mp")
    source_device, source_row = plane_rows(mp_index, slot_dev)
    gathered_slots = source_row * mp_count + source_device
    ignored, position_all, segment_all, adapter_all = slot_info(
        jnp.broadcast_to(own_lengths[None, :], (total_rows, request_count)),
        jnp.broadcast_to(own_adapters[None, :], (total_rows, request_count)),
        gathered_slots,
    )
    indicator_all = adapter_select_mask(adapter_all, adapter_column_count, ADAPTER_RANK)
    normed_all = normalize(states_all, attention_norm_gain)
    widths = [
        query_weight.shape[1],
        key_weight.shape[1],
        value_weight.shape[1],
        adapter_down_attention.shape[1],
    ]
    merged = jnp.dot(
        normed_all,
        jnp.concatenate([query_weight, key_weight, value_weight, adapter_down_attention], axis=1),
        preferred_element_type=jnp.float32,
    )
    edges = [sum(widths[:i]) for i in range(len(widths) + 1)]
    query_base, key_base, value_base, adapter_base = (
        merged[:, edges[i] : edges[i + 1]] for i in range(len(widths))
    )
    adapter_terms_all = (adapter_base * jnp.tile(indicator_all, (1, 3))).astype(jnp.bfloat16)
    query_projected = query_base + jnp.dot(
        adapter_terms_all[:, :adapter_column_count],
        adapter_up_query,
        preferred_element_type=jnp.float32,
    )
    key_projected = key_base + jnp.dot(
        adapter_terms_all[:, adapter_column_count : 2 * adapter_column_count],
        adapter_up_key_value[0],
        preferred_element_type=jnp.float32,
    )
    value_projected = value_base + jnp.dot(
        adapter_terms_all[:, 2 * adapter_column_count :],
        adapter_up_key_value[1],
        preferred_element_type=jnp.float32,
    )
    kv_pair = jnp.stack([key_projected, value_projected])
    partner = align_partner_rows(
        from_partner(kv_pair.astype(jnp.bfloat16), "mp", 0), mp_index % 2, slot_dev
    ).astype(kv_pair.dtype)
    parity = mp_index % 2
    joined = jnp.where(
        parity == 0,
        jnp.concatenate([kv_pair, partner], axis=2),
        jnp.concatenate([partner, kv_pair], axis=2),
    )
    key_projected = joined[0]
    value_projected = joined[1]
    queries = rotate(query_projected.reshape(total_rows, -1, HEAD_SIZE), position_all).astype(
        jnp.bfloat16
    )
    key_rows = rotate(key_projected.reshape(total_rows, -1, HEAD_SIZE), position_all).astype(
        jnp.bfloat16
    )
    value_rows = value_projected.reshape(total_rows, -1, HEAD_SIZE).astype(jnp.bfloat16)
    attention_output = attend(queries, key_rows, value_rows, position_all, segment_all)

    def out_term(first_row, row_count):
        return jnp.concatenate(
            [
                jnp.dot(attention_output, output_weight, preferred_element_type=jnp.float32),
                jnp.dot(attention_output, adapter_down_output, preferred_element_type=jnp.float32),
            ],
            axis=1,
        )

    summed = sum_rows(out_term, slot_dev)
    output_adapter_ranks = (summed[:, model_width:] * indicator_within).astype(jnp.bfloat16)
    residual_stream = (
        local_rows.astype(jnp.float32)
        + summed[:, :model_width]
        + jnp.dot(output_adapter_ranks, adapter_up_output, preferred_element_type=jnp.float32)
    ).astype(jnp.bfloat16)
    layer_result = feed_forward(
        residual_stream,
        indicator_within,
        feed_norm_gain,
        adapter_down_gate_up,
        adapter_up_gate_up,
        gate_up_full,
        down_full,
        adapter_down_feed,
        adapter_up_feed,
    )
    finished = jnp.where(living[:, None], layer_result, jnp.zeros_like(layer_result)).astype(
        jnp.bfloat16
    )
    return finished.reshape(1, slot_dev, 1, model_width)


def solution(mesh):
    placed = (
        P("req", None, "mp", None),
        P(),
        P(),
        P(),
        P(None, "mp"),
        P(None, "mp"),
        P(None, "mp"),
        P("mp", None),
        P(),
        P(None, "mp"),
        P(None, None, "mp"),
        P("mp", None),
        P(),
        P(),
        P(None, "req", "mp"),
        P("req", "mp"),
        P(),
        P(None, None, "mp"),
        P("mp", None),
        P(),
    )
    return jax.shard_map(
        shards, mesh=mesh, in_specs=placed, out_specs=P("req", None, "mp", None), check_vma=False
    )
```
